32 devices in a mesh: req: 16 (over z, y, x), tp: 2 (over core).
Axes of the slice: x: 2, y: 2, z: 4, core: 2. Of those that a mesh axis runs over, the one named last changes fastest.
Arguments:
- new_queries: bfloat16 [4096, 2048], P('req', 'tp'), may hold values from -9 to 9
- new_keys: bfloat16 [4096, 2048], P('req', 'tp'), may hold values from -9 to 9
- new_values: bfloat16 [4096, 2048], P('req', 'tp'), may hold values from -5 to 5
- kv_pages: bfloat16 [256, 2, 128, 2048], P('req', None, None, 'tp'), may hold values from -5.5 to 5.5
- page_table: int32 [16, 16], replicated, may hold values from -1 to 255, as said below
- cache_len: int32 [16], replicated, may hold values from 1 to 2048, as said below
- w_out: bfloat16 [2048, 4096], P('tp'), may hold values from -0.25 to 0.25
- out_bias: bfloat16 [4096], P('tp'), may hold values from -3 to 3
Outputs:
- projected: bfloat16 [4096, 4096], P('req', 'tp')
The draws below stay inside these ranges and needn't reach their ends.
Inputs may be any that keep to these rules, and one draw needn't show every extreme that they name: page_table[r, s] is the page holding cached positions s * 128 to (s + 1) * 128 - 1 of request r, for s below ceil(cache_len[r] / 128), and -1 after; page p is held by index p // 16 of req; the pages of one request lie on distinct indices of req; every page belongs to exactly one request. `cache_len`: some request has exactly 2048 cached positions.
All inputs are finite; a program needn't handle non-finite values.
Results may differ from the reference program's by a relative error of at most 0.0053.
Values may be sent and summed in bfloat16 or wider, within the bound.
No kernel may reach another device: no remote copies, remote signals or barrier semaphores. Data moves between devices by JAX's collectives and lax.ppermute only.
A program may use at most 192 MiB of HBM per device.

```python
import math
import jax
import jax.numpy as jnp
from jax import lax

D = 4096
HEADS = 16
HEAD_DIM = 128
ROT = 32
PAGE_LEN = 128
PAGES_DEV = 16
MOST = 16
TOKENS = 4096
POOL = 256
N_REQ = 16


def draw_new_queries(key, part):
    normal_part = jnp.clip(1.4 * jax.random.normal(jax.random.fold_in(key, 11), (TOKENS, HEADS, HEAD_DIM), jnp.float32), -5.5, 5.5)
    return normal_part.reshape(TOKENS, HEADS * HEAD_DIM).astype(jnp.bfloat16)


def draw_new_keys(key, part):
    normal_part = jnp.clip(1.4 * jax.random.normal(jax.random.fold_in(key, 13), (TOKENS, HEADS, HEAD_DIM), jnp.float32), -5.5, 5.5)
    return normal_part.reshape(TOKENS, HEADS * HEAD_DIM).astype(jnp.bfloat16)


def draw_kv_pages(key, part):
    shape_full = (POOL, 2, PAGE_LEN, HEADS * HEAD_DIM)
    kind_scale = jnp.array([1.4, 1.0], jnp.float32).reshape(1, 2, 1, 1)
    raw_part = jnp.clip(jax.random.normal(jax.random.fold_in(key, 23), shape_full, jnp.float32) * kind_scale, -5.5, 5.5)
    return raw_part.astype(jnp.bfloat16)


def build_table(key):
    request_order = jax.random.permutation(jax.random.fold_in(key, 101), N_REQ)
    rank_of = jnp.argsort(request_order).astype(jnp.int32)
    gift_size = (MOST - PAGES_DEV) // 4
    spread_max = max(0, min(PAGES_DEV - 1, MOST - PAGES_DEV))
    pair_steps = jax.random.randint(jax.random.fold_in(key, 102), (N_REQ,), 0, spread_max + 1)
    pair_index = jnp.clip((rank_of - 5) // 2, 0, N_REQ - 1)
    pair_delta = pair_steps[pair_index]
    pair_first = (rank_of >= 5) & ((rank_of - 5) % 2 == 0) & (rank_of + 1 < N_REQ)
    pair_second = (rank_of >= 6) & ((rank_of - 5) % 2 == 1)
    page_counts = PAGES_DEV + jnp.where(rank_of == 0, MOST - PAGES_DEV, 0) - jnp.where((rank_of >= 1) & (rank_of <= 4), gift_size, 0)
    page_counts = page_counts + jnp.where(pair_first, pair_delta, 0) - jnp.where(pair_second, pair_delta, 0)
    page_counts = page_counts.astype(jnp.int32)
    page_starts = jnp.cumsum(page_counts) - page_counts
    slot_index = jnp.arange(MOST, dtype=jnp.int32)
    sequence_pos = page_starts[:, None] + slot_index[None, :]
    in_use = slot_index[None, :] < page_counts[:, None]
    column_pos = sequence_pos % N_REQ
    depth_pos = jnp.clip(sequence_pos // N_REQ, 0, PAGES_DEV - 1)
    owner_map = jax.random.permutation(jax.random.fold_in(key, 103), N_REQ)
    local_keys = jax.random.split(jax.random.fold_in(key, 104), N_REQ)
    local_maps = jax.vmap(lambda single: jax.random.permutation(single, PAGES_DEV))(local_keys)
    local_ids = local_maps[column_pos, depth_pos]
    page_ids = jnp.where(in_use, owner_map[column_pos] * PAGES_DEV + local_ids, -1).astype(jnp.int32)
    tails = jax.random.randint(jax.random.fold_in(key, 105), (N_REQ,), 1, PAGE_LEN + 1)
    tails = jnp.where(rank_of == 0, PAGE_LEN, tails)
    lengths_out = ((page_counts - 1) * PAGE_LEN + tails).astype(jnp.int32)
    return (page_ids, lengths_out)


def draw_page_table(key, part):
    return build_table(jax.random.fold_in(key, 5))[0]


def draw_cache_len(key, part):
    return build_table(jax.random.fold_in(key, 5))[1]


def shard_levels(key, shape, pieces, least, top_value):
    level, own = 1.0, jax.random.fold_in(key, 6)
    for position, blocks in pieces:
        draws = jnp.exp(jax.random.uniform(jax.random.fold_in(own, position), (blocks,), jnp.float32, least / len(pieces), top_value / len(pieces)))
        level = level * jnp.repeat(draws, shape[position] // blocks).reshape([-1 if axis == position else 1 for axis in range(len(shape))])
    return level


def gaussian(key, extent, scale, most, cuts=(), kind=jnp.bfloat16):
    drawn = jax.random.normal(key, extent, jnp.float32) * scale
    if len(cuts) > 0:
        drawn = shard_levels(key, extent, cuts, -0.22, 0.18) * drawn
    return jnp.clip(drawn, min=-most, max=most).astype(kind)


def setup_inputs(seed: int = 0) -> dict:
    key_list = jax.random.split(jax.random.key(seed), 9)
    return {
        "new_queries": draw_new_queries(jax.random.fold_in(key_list[8], 71), 0),
        "new_keys": draw_new_keys(jax.random.fold_in(key_list[8], 71), 0),
        "new_values": gaussian(key_list[2], (TOKENS, HEADS * HEAD_DIM), 1.0, 5.0, ((0, 16), (1, 2))),
        "kv_pages": draw_kv_pages(jax.random.fold_in(key_list[8], 71), 0),
        "page_table": draw_page_table(jax.random.fold_in(key_list[8], 71), 0),
        "cache_len": draw_cache_len(jax.random.fold_in(key_list[8], 71), 0),
        "w_out": gaussian(key_list[6], (HEADS * HEAD_DIM, D), (HEADS * HEAD_DIM // 4) ** -0.5, 0.25, ((0, 2),)),
        "out_bias": gaussian(key_list[7], (D,), 0.5, 3.0, ((0, 2),)),
    }


NEG_FILL = -1e+30

def as_float(value):
    return lax.optimization_barrier(value).astype(jnp.float32)

def rotate_rows(block, positions):
    row_count = block.shape[0]
    shaped = block.astype(jnp.float32).reshape(row_count, -1, HEAD_DIM)
    half_rot = ROT // 2
    frequency = 10000.0 ** (-2.0 * jnp.arange(half_rot, dtype=jnp.float32) / ROT)
    angles = positions.astype(jnp.float32)[:, None] * frequency[None, :]
    cosine = jnp.cos(angles)[:, None, :]
    sines = jnp.sin(angles)[:, None, :]
    first_half = shaped[:, :, :half_rot]
    second_half = shaped[:, :, half_rot:ROT]
    turned = jnp.concatenate([first_half * cosine - second_half * sines, second_half * cosine + first_half * sines, shaped[:, :, ROT:]], axis=2)
    return turned.reshape(row_count, -1).astype(jnp.bfloat16)

def block_partials(query_heads, key_blocks, value_blocks, usable):
    head_count = key_blocks.shape[2]
    score_scale = 1.0 / math.sqrt(HEAD_DIM)
    query_f = as_float(query_heads)
    keys_f = as_float(key_blocks)
    values_f = as_float(value_blocks)

    def one_head(head_index):
        keys_h = lax.dynamic_index_in_dim(keys_f, head_index, 2, keepdims=False)
        values_h = lax.dynamic_index_in_dim(values_f, head_index, 2, keepdims=False)
        query_h = lax.dynamic_index_in_dim(query_f, head_index, 1, keepdims=False)
        scores = jnp.einsum('ce,bke->bck', query_h, keys_h, precision=lax.Precision.HIGHEST)
        scores = jnp.where(usable, scores * score_scale, NEG_FILL)
        maxima = lax.optimization_barrier(jnp.max(scores, axis=2))
        weights = jnp.where(usable, jnp.exp(scores - maxima[:, :, None]), 0.0)
        totals = lax.optimization_barrier(jnp.sum(weights, axis=2))
        rounded = as_float(weights.astype(jnp.bfloat16))
        weighted = jnp.einsum('bck,bke->bce', rounded, values_h, precision=lax.Precision.HIGHEST)
        return (maxima, totals, weighted)
    return lax.map(one_head, jnp.arange(head_count, dtype=jnp.int32))

def combine(maxima, totals, weighted):
    peak_score = lax.optimization_barrier(jnp.max(maxima, axis=1, keepdims=True))
    factor = jnp.exp(maxima - peak_score)
    numerator = lax.optimization_barrier(jnp.sum(factor[..., None] * weighted, axis=1))
    denominator = lax.optimization_barrier(jnp.sum(factor * totals, axis=1))
    return numerator / denominator[..., None]

def reference(new_queries, new_keys, new_values, kv_pages, page_table, cache_len, w_out, out_bias):
    request_count = page_table.shape[0]
    span_len = new_queries.shape[0] // request_count
    head_count = new_queries.shape[1] // HEAD_DIM
    page_size = kv_pages.shape[2]
    slot_count = page_table.shape[1]

    def one_request(request):
        start = (request * span_len).astype(jnp.int32)
        own_length = cache_len[request]
        positions = own_length + jnp.arange(span_len, dtype=jnp.int32)
        query_rot = rotate_rows(lax.dynamic_slice_in_dim(new_queries, start, span_len, 0), positions)
        key_rot = rotate_rows(lax.dynamic_slice_in_dim(new_keys, start, span_len, 0), positions)
        own_values = lax.dynamic_slice_in_dim(new_values, start, span_len, 0)
        query_heads = query_rot.reshape(span_len, head_count, HEAD_DIM)
        causal = (jnp.arange(span_len, dtype=jnp.int32)[:, None] >= jnp.arange(span_len, dtype=jnp.int32)[None, :])[None]
        local_parts = block_partials(query_heads, key_rot.reshape(1, span_len, head_count, HEAD_DIM), own_values.reshape(1, span_len, head_count, HEAD_DIM), causal)
        own_row = page_table[request]
        safe_ids = jnp.maximum(own_row, 0).astype(jnp.int32)
        fetched = jnp.take(kv_pages, safe_ids, axis=0)
        key_place = jnp.arange(slot_count, dtype=jnp.int32)[:, None] * page_size + jnp.arange(page_size, dtype=jnp.int32)[None, :]
        usable = ((own_row[:, None] >= 0) & (key_place < own_length))[:, None, :]
        cache_parts = block_partials(query_heads, fetched[:, 0].reshape(slot_count, page_size, head_count, HEAD_DIM), fetched[:, 1].reshape(slot_count, page_size, head_count, HEAD_DIM), usable)
        maxima = jnp.concatenate([local_parts[0], cache_parts[0]], axis=1)
        totals = jnp.concatenate([local_parts[1], cache_parts[1]], axis=1)
        weighted = jnp.concatenate([local_parts[2], cache_parts[2]], axis=1)
        merged = combine(maxima, totals, weighted)
        return jnp.transpose(merged, (1, 0, 2)).reshape(span_len, head_count * HEAD_DIM).astype(jnp.bfloat16)
    attended = lax.map(one_request, jnp.arange(request_count, dtype=jnp.int32))
    attended = attended.reshape(request_count * span_len, head_count * HEAD_DIM)
    summed = jnp.dot(attended, w_out, preferred_element_type=jnp.float32)
    return (summed + out_bias.astype(jnp.float32)).astype(jnp.bfloat16)
```

```python
import math
from functools import partial

import jax
import jax.numpy as jnp
from jax import lax
from jax.experimental import pallas as pl
from jax.experimental.pallas import tpu as pltpu
from jax.sharding import PartitionSpec as P

HEAD_DIM = 128
ROT = 32


NEG_FILL = -1e30


def rotate_rows(block, positions):
    row_count = block.shape[0]
    shaped = block.astype(jnp.float32).reshape(row_count, -1, HEAD_DIM)
    half_rot = ROT // 2
    frequency = 10000.0 ** (-2.0 * jnp.arange(half_rot, dtype=jnp.float32) / ROT)
    angles = positions.astype(jnp.float32)[:, None] * frequency[None, :]
    cosine = jnp.cos(angles)[:, None, :]
    sines = jnp.sin(angles)[:, None, :]
    first_half = shaped[:, :, :half_rot]
    second_half = shaped[:, :, half_rot:ROT]
    turned = jnp.concatenate(
        [
            first_half * cosine - second_half * sines,
            second_half * cosine + first_half * sines,
            shaped[:, :, ROT:],
        ],
        axis=2,
    )
    return turned.reshape(row_count, -1).astype(jnp.bfloat16)


def attention_kernel(nvalid_ref, q_ref, kl_ref, vl_ref, kp_ref, vp_ref, o_ref):
    score_scale = 1.0 / math.sqrt(HEAD_DIM)
    dims = (((1,), (1,)), ((), ()))
    q = q_ref[...]
    span = q.shape[0]
    page_size = kp_ref.shape[1]
    block_count = kp_ref.shape[0]

    s = lax.dot_general(q, kl_ref[...], dims, preferred_element_type=jnp.float32) * score_scale
    row = lax.broadcasted_iota(jnp.int32, (span, span), 0)
    col = lax.broadcasted_iota(jnp.int32, (span, span), 1)
    causal = row >= col
    s = jnp.where(causal, s, NEG_FILL)
    m = jnp.max(s, axis=1, keepdims=True)
    p = jnp.where(causal, jnp.exp(s - m), 0.0)
    l = jnp.sum(p, axis=1, keepdims=True)
    acc = jnp.dot(p.astype(jnp.bfloat16), vl_ref[...], preferred_element_type=jnp.float32)

    page_col = lax.broadcasted_iota(jnp.int32, (span, page_size), 1)

    def body(j, carry):
        m, l, acc = carry
        n = nvalid_ref[j]
        usable = page_col < n
        s = lax.dot_general(q, kp_ref[j], dims, preferred_element_type=jnp.float32) * score_scale
        s = jnp.where(usable, s, NEG_FILL)
        m_b = jnp.max(s, axis=1, keepdims=True)
        p = jnp.where(usable, jnp.exp(s - m_b), 0.0)
        l_b = jnp.sum(p, axis=1, keepdims=True)
        o_b = jnp.dot(p.astype(jnp.bfloat16), vp_ref[j], preferred_element_type=jnp.float32)
        m_new = jnp.maximum(m, m_b)
        a = jnp.exp(m - m_new)
        b = jnp.exp(m_b - m_new)
        return (m_new, l * a + l_b * b, acc * a + o_b * b)

    m, l, acc = lax.fori_loop(0, block_count, body, (m, l, acc))
    o_ref[...] = (acc / l).astype(o_ref.dtype)


def attend(nvalid, query_rot, key_rot, values, incoming):
    span, width = query_rot.shape
    head_count = width // HEAD_DIM
    block_count, _, page_size, _ = incoming.shape
    grid_spec = pltpu.PrefetchScalarGridSpec(
        num_scalar_prefetch=1,
        grid=(head_count,),
        in_specs=[
            pl.BlockSpec((span, HEAD_DIM), lambda h, nv: (0, h)),
            pl.BlockSpec((span, HEAD_DIM), lambda h, nv: (0, h)),
            pl.BlockSpec((span, HEAD_DIM), lambda h, nv: (0, h)),
            pl.BlockSpec((block_count, None, page_size, HEAD_DIM), lambda h, nv: (0, 0, 0, h)),
            pl.BlockSpec((block_count, None, page_size, HEAD_DIM), lambda h, nv: (0, 1, 0, h)),
        ],
        out_specs=pl.BlockSpec((span, HEAD_DIM), lambda h, nv: (0, h)),
    )
    return pl.pallas_call(
        attention_kernel,
        grid_spec=grid_spec,
        out_shape=jax.ShapeDtypeStruct((span, width), jnp.bfloat16),
    )(nvalid, query_rot, key_rot, values, incoming, incoming)


def on_device(new_queries, new_keys, new_values, kv_pages, page_table, cache_len, w_out, out_bias):
    own_index = lax.axis_index("req")
    tp_index = lax.axis_index("tp")
    tp_count = lax.axis_size("tp")
    span_len = new_queries.shape[0]
    page_count = kv_pages.shape[0]
    page_size = kv_pages.shape[2]
    request_count = page_table.shape[0]
    slot_count = page_table.shape[1]
    out_cols = w_out.shape[1] // tp_count

    w_recv = []
    for shift in range(1, tp_count):
        target = (tp_index + shift) % tp_count
        piece = lax.dynamic_slice_in_dim(w_out, target * out_cols, out_cols, axis=1)
        perm = [(i, (i + shift) % tp_count) for i in range(tp_count)]
        w_recv.append(lax.ppermute(piece, "tp", perm))
    w_mine = lax.dynamic_slice_in_dim(w_out, tp_index * out_cols, out_cols, axis=1)

    slot_ids = jnp.arange(slot_count, dtype=jnp.int32)
    request_ids = jnp.arange(request_count, dtype=jnp.int32)
    owners = jnp.where(page_table >= 0, page_table // page_count, -1)
    held_here = owners == own_index
    local_page = jnp.sum(jnp.where(held_here, page_table - own_index * page_count, 0), axis=1)
    outgoing = jnp.take(kv_pages, local_page, axis=0)
    incoming = lax.all_to_all(outgoing, "req", split_axis=0, concat_axis=0, tiled=True)

    own_length = lax.dynamic_index_in_dim(cache_len, own_index, 0, keepdims=False)
    positions = own_length + jnp.arange(span_len, dtype=jnp.int32)
    query_rot = rotate_rows(new_queries, positions)
    key_rot = rotate_rows(new_keys, positions)

    own_row = lax.dynamic_index_in_dim(page_table, own_index, 0, keepdims=False)
    row_owner = jnp.where(own_row >= 0, own_row // page_count, -1)
    matches = row_owner[None, :] == request_ids[:, None]
    present = jnp.any(matches, axis=1)
    slot_of = jnp.sum(jnp.where(matches, slot_ids[None, :], 0), axis=1)
    nvalid = jnp.where(present, jnp.clip(own_length - slot_of * page_size, 0, page_size), 0)
    nvalid = nvalid.astype(jnp.int32)

    attended = attend(nvalid, query_rot, key_rot, new_values, incoming)

    summed = jnp.dot(attended, w_mine, preferred_element_type=jnp.float32)
    for shift in range(1, tp_count):
        perm = [(i, (i + shift) % tp_count) for i in range(tp_count)]
        other = lax.ppermute(attended, "tp", perm)
        summed = summed + jnp.dot(other, w_recv[shift - 1], preferred_element_type=jnp.float32)
    return (summed + out_bias.astype(jnp.float32)).astype(jnp.bfloat16)


def solution(mesh):
    return jax.shard_map(
        on_device,
        mesh=mesh,
        in_specs=(
            P("req", "tp"),
            P("req", "tp"),
            P("req", "tp"),
            P("req", None, None, "tp"),
            P(),
            P(),
            P("tp", None),
            P("tp"),
        ),
        out_specs=P("req", "tp"),
        check_vma=False,
    )
```

```python
import math
from functools import partial

import jax
import jax.numpy as jnp
from jax import lax
from jax.experimental import pallas as pl
from jax.experimental.pallas import tpu as pltpu
from jax.sharding import PartitionSpec as P

HEAD_DIM = 128
ROT = 32


NEG_FILL = -1e30


def rotate_rows(block, positions):
    row_count = block.shape[0]
    shaped = block.astype(jnp.float32).reshape(row_count, -1, HEAD_DIM)
    half_rot = ROT // 2
    frequency = 10000.0 ** (-2.0 * jnp.arange(half_rot, dtype=jnp.float32) / ROT)
    angles = positions.astype(jnp.float32)[:, None] * frequency[None, :]
    cosine = jnp.cos(angles)[:, None, :]
    sines = jnp.sin(angles)[:, None, :]
    first_half = shaped[:, :, :half_rot]
    second_half = shaped[:, :, half_rot:ROT]
    turned = jnp.concatenate(
        [
            first_half * cosine - second_half * sines,
            second_half * cosine + first_half * sines,
            shaped[:, :, ROT:],
        ],
        axis=2,
    )
    return turned.reshape(row_count, -1).astype(jnp.bfloat16)


def attention_kernel(q_ref, kl_ref, vl_ref, kp_ref, vp_ref, ok_ref, o_ref):
    score_scale = 1.0 / math.sqrt(HEAD_DIM)
    dims = (((1,), (1,)), ((), ()))
    q = q_ref[...]
    span = q.shape[0]
    block_count, page_size, _ = kp_ref.shape
    keys_p = kp_ref[...].reshape(block_count * page_size, HEAD_DIM)
    values_p = vp_ref[...].reshape(block_count * page_size, HEAD_DIM)

    s_loc = lax.dot_general(q, kl_ref[...], dims, preferred_element_type=jnp.float32) * score_scale
    row = lax.broadcasted_iota(jnp.int32, (span, span), 0)
    col = lax.broadcasted_iota(jnp.int32, (span, span), 1)
    s_loc = jnp.where(row >= col, s_loc, NEG_FILL)
    s_pg = lax.dot_general(q, keys_p, dims, preferred_element_type=jnp.float32) * score_scale
    s_pg = jnp.where(ok_ref[...] > 0, s_pg, NEG_FILL)
    m = jnp.maximum(jnp.max(s_loc, axis=1, keepdims=True), jnp.max(s_pg, axis=1, keepdims=True))
    p_loc = jnp.exp(s_loc - m)
    p_pg = jnp.exp(s_pg - m)
    l = jnp.sum(p_loc, axis=1, keepdims=True) + jnp.sum(p_pg, axis=1, keepdims=True)
    acc = jnp.dot(p_loc.astype(jnp.bfloat16), vl_ref[...], preferred_element_type=jnp.float32)
    acc = acc + jnp.dot(p_pg.astype(jnp.bfloat16), values_p, preferred_element_type=jnp.float32)
    o_ref[...] = (acc / l).astype(o_ref.dtype)


def attend(key_ok, query_rot, key_rot, values, incoming):
    span, width = query_rot.shape
    head_count = width // HEAD_DIM
    block_count, _, page_size, _ = incoming.shape
    return pl.pallas_call(
        attention_kernel,
        grid=(head_count,),
        in_specs=[
            pl.BlockSpec((span, HEAD_DIM), lambda h: (0, h)),
            pl.BlockSpec((span, HEAD_DIM), lambda h: (0, h)),
            pl.BlockSpec((span, HEAD_DIM), lambda h: (0, h)),
            pl.BlockSpec((block_count, None, page_size, HEAD_DIM), lambda h: (0, 0, 0, h)),
            pl.BlockSpec((block_count, None, page_size, HEAD_DIM), lambda h: (0, 1, 0, h)),
            pl.BlockSpec((1, block_count * page_size), lambda h: (0, 0)),
        ],
        out_specs=pl.BlockSpec((span, HEAD_DIM), lambda h: (0, h)),
        out_shape=jax.ShapeDtypeStruct((span, width), jnp.bfloat16),
    )(query_rot, key_rot, values, incoming, incoming, key_ok)


def on_device(new_queries, new_keys, new_values, kv_pages, page_table, cache_len, w_out, out_bias):
    own_index = lax.axis_index("req")
    tp_index = lax.axis_index("tp")
    tp_count = lax.axis_size("tp")
    span_len = new_queries.shape[0]
    page_count = kv_pages.shape[0]
    page_size = kv_pages.shape[2]
    request_count = page_table.shape[0]
    slot_count = page_table.shape[1]
    out_cols = w_out.shape[1] // tp_count

    w_recv = []
    for shift in range(1, tp_count):
        target = (tp_index + shift) % tp_count
        piece = lax.dynamic_slice_in_dim(w_out, target * out_cols, out_cols, axis=1)
        perm = [(i, (i + shift) % tp_count) for i in range(tp_count)]
        w_recv.append(lax.ppermute(piece, "tp", perm))
    w_mine = lax.dynamic_slice_in_dim(w_out, tp_index * out_cols, out_cols, axis=1)

    slot_ids = jnp.arange(slot_count, dtype=jnp.int32)
    request_ids = jnp.arange(request_count, dtype=jnp.int32)
    owners = jnp.where(page_table >= 0, page_table // page_count, -1)
    held_here = owners == own_index
    local_page = jnp.sum(jnp.where(held_here, page_table - own_index * page_count, 0), axis=1)
    outgoing = jnp.take(kv_pages, local_page, axis=0, mode="clip")
    incoming = lax.all_to_all(outgoing, "req", split_axis=0, concat_axis=0, tiled=True)

    own_length = lax.dynamic_index_in_dim(cache_len, own_index, 0, keepdims=False)
    positions = own_length + jnp.arange(span_len, dtype=jnp.int32)
    query_rot = rotate_rows(new_queries, positions)
    key_rot = rotate_rows(new_keys, positions)

    own_row = lax.dynamic_index_in_dim(page_table, own_index, 0, keepdims=False)
    row_owner = jnp.where(own_row >= 0, own_row // page_count, -1)
    matches = row_owner[None, :] == request_ids[:, None]
    present = jnp.any(matches, axis=1)
    slot_of = jnp.sum(jnp.where(matches, slot_ids[None, :], 0), axis=1)
    nvalid = jnp.where(present, jnp.clip(own_length - slot_of * page_size, 0, page_size), 0)
    within = jnp.arange(page_size, dtype=jnp.int32)
    key_ok = (within[None, :] < nvalid[:, None]).astype(jnp.int32).reshape(1, request_count * page_size)

    attended = attend(key_ok, query_rot, key_rot, new_values, incoming)

    summed = jnp.dot(attended, w_mine, preferred_element_type=jnp.float32)
    for shift in range(1, tp_count):
        perm = [(i, (i + shift) % tp_count) for i in range(tp_count)]
        other = lax.ppermute(attended, "tp", perm)
        summed = summed + jnp.dot(other, w_recv[shift - 1], preferred_element_type=jnp.float32)
    return (summed + out_bias.astype(jnp.float32)).astype(jnp.bfloat16)


def solution(mesh):
    return jax.shard_map(
        on_device,
        mesh=mesh,
        in_specs=(
            P("req", "tp"),
            P("req", "tp"),
            P("req", "tp"),
            P("req", None, None, "tp"),
            P(),
            P(),
            P("tp", None),
            P("tp"),
        ),
        out_specs=P("req", "tp"),
        check_vma=False,
    )
```

```python
import math
from functools import partial

import jax
import jax.numpy as jnp
from jax import lax
from jax.experimental import pallas as pl
from jax.experimental.pallas import tpu as pltpu
from jax.sharding import PartitionSpec as P

HEAD_DIM = 128
ROT = 32


NEG_FILL = -1e30


def rotate_rows(block, positions):
    row_count = block.shape[0]
    shaped = block.astype(jnp.float32).reshape(row_count, -1, HEAD_DIM)
    half_rot = ROT // 2
    frequency = 10000.0 ** (-2.0 * jnp.arange(half_rot, dtype=jnp.float32) / ROT)
    angles = positions.astype(jnp.float32)[:, None] * frequency[None, :]
    cosine = jnp.cos(angles)[:, None, :]
    sines = jnp.sin(angles)[:, None, :]
    first_half = shaped[:, :, :half_rot]
    second_half = shaped[:, :, half_rot:ROT]
    turned = jnp.concatenate(
        [
            first_half * cosine - second_half * sines,
            second_half * cosine + first_half * sines,
            shaped[:, :, ROT:],
        ],
        axis=2,
    )
    return turned.reshape(row_count, -1).astype(jnp.bfloat16)


def attention_kernel(*refs, with_local):
    if with_local:
        q_ref, kl_ref, vl_ref, kp_ref, vp_ref, ok_ref, o_ref, m_ref, l_ref = refs
    else:
        q_ref, kp_ref, vp_ref, ok_ref, o_ref, m_ref, l_ref = refs
    score_scale = 1.0 / math.sqrt(HEAD_DIM)
    dims = (((1,), (1,)), ((), ()))
    q = q_ref[...]
    span = q.shape[0]
    block_count, page_size, _ = kp_ref.shape
    keys_p = kp_ref[...].reshape(block_count * page_size, HEAD_DIM)
    values_p = vp_ref[...].reshape(block_count * page_size, HEAD_DIM)

    s_pg = lax.dot_general(q, keys_p, dims, preferred_element_type=jnp.float32) * score_scale
    s_pg = jnp.where(ok_ref[...] > 0, s_pg, NEG_FILL)
    m = jnp.max(s_pg, axis=1, keepdims=True)
    if with_local:
        s_loc = lax.dot_general(q, kl_ref[...], dims, preferred_element_type=jnp.float32) * score_scale
        row = lax.broadcasted_iota(jnp.int32, (span, span), 0)
        col = lax.broadcasted_iota(jnp.int32, (span, span), 1)
        s_loc = jnp.where(row >= col, s_loc, NEG_FILL)
        m = jnp.maximum(m, jnp.max(s_loc, axis=1, keepdims=True))
    p_pg = jnp.exp(s_pg - m)
    l = jnp.sum(p_pg, axis=1, keepdims=True)
    acc = jnp.dot(p_pg.astype(jnp.bfloat16), values_p, preferred_element_type=jnp.float32)
    if with_local:
        p_loc = jnp.exp(s_loc - m)
        l = l + jnp.sum(p_loc, axis=1, keepdims=True)
        acc = acc + jnp.dot(p_loc.astype(jnp.bfloat16), vl_ref[...], preferred_element_type=jnp.float32)
    o_ref[...] = (acc / l).astype(o_ref.dtype)
    m_ref[...] = m
    l_ref[...] = l


def attend(key_ok, query_rot, incoming, which, out_dtype, local=None):
    span, width = query_rot.shape
    head_count = width // HEAD_DIM
    block_count = incoming.shape[0]
    page_size = incoming.shape[3]
    col_spec = pl.BlockSpec((span, HEAD_DIM), lambda h: (0, h))
    page_specs = [
        pl.BlockSpec((block_count, None, None, page_size, HEAD_DIM), lambda h: (0, which, 0, 0, h)),
        pl.BlockSpec((block_count, None, None, page_size, HEAD_DIM), lambda h: (0, which, 1, 0, h)),
        pl.BlockSpec((1, block_count * page_size), lambda h: (0, 0)),
    ]
    stat_spec = pl.BlockSpec((None, span, 1), lambda h: (h, 0, 0))
    if local is None:
        in_specs = [col_spec] + page_specs
        operands = (query_rot, incoming, incoming, key_ok)
    else:
        in_specs = [col_spec, col_spec, col_spec] + page_specs
        operands = (query_rot, local[0], local[1], incoming, incoming, key_ok)
    return pl.pallas_call(
        partial(attention_kernel, with_local=local is not None),
        grid=(head_count,),
        in_specs=in_specs,
        out_specs=[col_spec, stat_spec, stat_spec],
        out_shape=[
            jax.ShapeDtypeStruct((span, width), out_dtype),
            jax.ShapeDtypeStruct((head_count, span, 1), jnp.float32),
            jax.ShapeDtypeStruct((head_count, span, 1), jnp.float32),
        ],
    )(*operands)


def usable_keys(page_table, request, length, source_base, source_count, page_count, page_size):
    row = lax.dynamic_index_in_dim(page_table, request, 0, keepdims=False)
    row_owner = jnp.where(row >= 0, row // page_count, -1)
    sources = source_base + jnp.arange(source_count, dtype=jnp.int32)
    slot_ids = jnp.arange(row.shape[0], dtype=jnp.int32)
    matches = row_owner[None, :] == sources[:, None]
    present = jnp.any(matches, axis=1)
    slot_of = jnp.sum(jnp.where(matches, slot_ids[None, :], 0), axis=1)
    nvalid = jnp.where(present, jnp.clip(length - slot_of * page_size, 0, page_size), 0)
    within = jnp.arange(page_size, dtype=jnp.int32)
    return (within[None, :] < nvalid[:, None]).astype(jnp.int32).reshape(1, source_count * page_size)


def by_rows(stat):
    return jnp.transpose(stat, (1, 0, 2))


def on_device(new_queries, new_keys, new_values, kv_pages, page_table, cache_len, w_out, out_bias):
    half = lax.axis_index("half")
    sub = lax.axis_index("sub")
    sub_count = lax.axis_size("sub")
    tp_index = lax.axis_index("tp")
    tp_count = lax.axis_size("tp")
    own_index = half * sub_count + sub
    partner = (1 - half) * sub_count + sub
    span_len = new_queries.shape[0]
    width = new_queries.shape[1]
    head_count = width // HEAD_DIM
    page_count = kv_pages.shape[0]
    page_size = kv_pages.shape[2]
    out_cols = w_out.shape[1] // tp_count
    swap = [(0, 1), (1, 0)]

    w_recv = []
    for shift in range(1, tp_count):
        target = (tp_index + shift) % tp_count
        piece = lax.dynamic_slice_in_dim(w_out, target * out_cols, out_cols, axis=1)
        perm = [(i, (i + shift) % tp_count) for i in range(tp_count)]
        w_recv.append(lax.ppermute(piece, "tp", perm))
    w_mine = lax.dynamic_slice_in_dim(w_out, tp_index * out_cols, out_cols, axis=1)

    owners = jnp.where(page_table >= 0, page_table // page_count, -1)
    held_here = owners == own_index
    local_page = jnp.sum(jnp.where(held_here, page_table - own_index * page_count, 0), axis=1)
    dest = jnp.arange(sub_count, dtype=jnp.int32)
    wanted = jnp.stack([half * sub_count + dest, (1 - half) * sub_count + dest], axis=1).reshape(-1)
    outgoing = jnp.take(kv_pages, jnp.take(local_page, wanted), axis=0, mode="clip")
    outgoing = outgoing.reshape((sub_count, 2) + kv_pages.shape[1:])
    incoming = lax.all_to_all(outgoing, "sub", split_axis=0, concat_axis=0, tiled=True)

    own_length = lax.dynamic_index_in_dim(cache_len, own_index, 0, keepdims=False)
    partner_length = lax.dynamic_index_in_dim(cache_len, partner, 0, keepdims=False)
    positions = own_length + jnp.arange(span_len, dtype=jnp.int32)
    query_rot = rotate_rows(new_queries, positions)
    key_rot = rotate_rows(new_keys, positions)
    partner_query = lax.ppermute(query_rot, "half", swap)

    source_base = half * sub_count
    ok_own = usable_keys(page_table, own_index, own_length, source_base, sub_count, page_count, page_size)
    ok_partner = usable_keys(page_table, partner, partner_length, source_base, sub_count, page_count, page_size)

    far_out, far_max, far_sum = attend(ok_partner, partner_query, incoming, 1, jnp.bfloat16)
    far_stats = jnp.concatenate([far_max, far_sum], axis=2)
    back_out = lax.ppermute(far_out, "half", swap)
    back_stats = lax.ppermute(far_stats, "half", swap)
    near_out, near_max, near_sum = attend(
        ok_own, query_rot, incoming, 0, jnp.float32, local=(key_rot, new_values)
    )

    near_max = by_rows(near_max)
    near_sum = by_rows(near_sum)
    back_stats = by_rows(back_stats)
    back_max = back_stats[:, :, 0:1]
    back_sum = back_stats[:, :, 1:2]
    peak = jnp.maximum(near_max, back_max)
    near_w = jnp.exp(near_max - peak) * near_sum
    back_w = jnp.exp(back_max - peak) * back_sum
    near3 = near_out.reshape(span_len, head_count, HEAD_DIM)
    back3 = back_out.astype(jnp.float32).reshape(span_len, head_count, HEAD_DIM)
    merged = (near3 * near_w + back3 * back_w) / (near_w + back_w)
    attended = merged.reshape(span_len, width).astype(jnp.bfloat16)

    summed = jnp.dot(attended, w_mine, preferred_element_type=jnp.float32)
    for shift in range(1, tp_count):
        perm = [(i, (i + shift) % tp_count) for i in range(tp_count)]
        other = lax.ppermute(attended, "tp", perm)
        summed = summed + jnp.dot(other, w_recv[shift - 1], preferred_element_type=jnp.float32)
    return (summed + out_bias.astype(jnp.float32)).astype(jnp.bfloat16)


def solution(mesh):
    req_count = mesh.shape["req"]
    tp_count = mesh.shape["tp"]
    assert tuple(mesh.axis_names) == ("req", "tp")
    devices = mesh.devices.reshape(2, req_count // 2, tp_count)
    split_mesh = jax.sharding.Mesh(devices, ("half", "sub", "tp"))
    rows = ("half", "sub")
    return jax.shard_map(
        on_device,
        mesh=split_mesh,
        in_specs=(
            P(rows, "tp"),
            P(rows, "tp"),
            P(rows, "tp"),
            P(rows, None, None, "tp"),
            P(),
            P(),
            P("tp", None),
            P("tp"),
        ),
        out_specs=P(rows, "tp"),
        check_vma=False,
    )
```

```python
import math
from functools import partial

import jax
import jax.numpy as jnp
from jax import lax
from jax.experimental import pallas as pl
from jax.experimental.pallas import tpu as pltpu
from jax.sharding import PartitionSpec as P

HEAD_DIM = 128
ROT = 32


NEG_FILL = -1e30


def rotate_rows(block, positions):
    row_count = block.shape[0]
    shaped = block.astype(jnp.float32).reshape(row_count, -1, HEAD_DIM)
    half_rot = ROT // 2
    frequency = 10000.0 ** (-2.0 * jnp.arange(half_rot, dtype=jnp.float32) / ROT)
    angles = positions.astype(jnp.float32)[:, None] * frequency[None, :]
    cosine = jnp.cos(angles)[:, None, :]
    sines = jnp.sin(angles)[:, None, :]
    first_half = shaped[:, :, :half_rot]
    second_half = shaped[:, :, half_rot:ROT]
    turned = jnp.concatenate(
        [
            first_half * cosine - second_half * sines,
            second_half * cosine + first_half * sines,
            shaped[:, :, ROT:],
        ],
        axis=2,
    )
    return turned.reshape(row_count, -1).astype(jnp.bfloat16)


def attention_kernel(*refs, with_local):
    if with_local:
        q_ref, kl_ref, vl_ref, kp_ref, vp_ref, ok_ref, o_ref, m_ref, l_ref = refs
    else:
        q_ref, kp_ref, vp_ref, ok_ref, o_ref, m_ref, l_ref = refs
    score_scale = 1.0 / math.sqrt(HEAD_DIM)
    dims = (((1,), (1,)), ((), ()))
    q = q_ref[...]
    span = q.shape[0]
    block_count, page_size, _ = kp_ref.shape
    keys_p = kp_ref[...].reshape(block_count * page_size, HEAD_DIM)
    values_p = vp_ref[...].reshape(block_count * page_size, HEAD_DIM)

    s_pg = lax.dot_general(q, keys_p, dims, preferred_element_type=jnp.float32) * score_scale
    s_pg = jnp.where(ok_ref[...] > 0, s_pg, NEG_FILL)
    m = jnp.max(s_pg, axis=1, keepdims=True)
    if with_local:
        s_loc = lax.dot_general(q, kl_ref[...], dims, preferred_element_type=jnp.float32) * score_scale
        row = lax.broadcasted_iota(jnp.int32, (span, span), 0)
        col = lax.broadcasted_iota(jnp.int32, (span, span), 1)
        s_loc = jnp.where(row >= col, s_loc, NEG_FILL)
        m = jnp.maximum(m, jnp.max(s_loc, axis=1, keepdims=True))
    p_pg = jnp.exp(s_pg - m)
    l = jnp.sum(p_pg, axis=1, keepdims=True)
    acc = jnp.dot(p_pg.astype(jnp.bfloat16), values_p, preferred_element_type=jnp.float32)
    if with_local:
        p_loc = jnp.exp(s_loc - m)
        l = l + jnp.sum(p_loc, axis=1, keepdims=True)
        acc = acc + jnp.dot(p_loc.astype(jnp.bfloat16), vl_ref[...], preferred_element_type=jnp.float32)
    o_ref[...] = (acc / l).astype(o_ref.dtype)
    m_ref[...] = m
    l_ref[...] = l


def attend(key_ok, query_rot, incoming, out_dtype, local=None):
    span, width = query_rot.shape
    head_count = width // HEAD_DIM
    block_count = incoming.shape[0]
    page_size = incoming.shape[2]
    col_spec = pl.BlockSpec((span, HEAD_DIM), lambda h: (0, h))
    page_specs = [
        pl.BlockSpec((block_count, None, page_size, HEAD_DIM), lambda h: (0, 0, 0, h)),
        pl.BlockSpec((block_count, None, page_size, HEAD_DIM), lambda h: (0, 1, 0, h)),
        pl.BlockSpec((1, block_count * page_size), lambda h: (0, 0)),
    ]
    stat_spec = pl.BlockSpec((None, span, 1), lambda h: (h, 0, 0))
    if local is None:
        in_specs = [col_spec] + page_specs
        operands = (query_rot, incoming, incoming, key_ok)
    else:
        in_specs = [col_spec, col_spec, col_spec] + page_specs
        operands = (query_rot, local[0], local[1], incoming, incoming, key_ok)
    return pl.pallas_call(
        partial(attention_kernel, with_local=local is not None),
        grid=(head_count,),
        in_specs=in_specs,
        out_specs=[col_spec, stat_spec, stat_spec],
        out_shape=[
            jax.ShapeDtypeStruct((span, width), out_dtype),
            jax.ShapeDtypeStruct((head_count, span, 1), jnp.float32),
            jax.ShapeDtypeStruct((head_count, span, 1), jnp.float32),
        ],
    )(*operands)


def usable_keys(page_table, request, length, source_base, source_count, page_count, page_size):
    row = lax.dynamic_index_in_dim(page_table, request, 0, keepdims=False)
    row_owner = jnp.where(row >= 0, row // page_count, -1)
    sources = source_base + jnp.arange(source_count, dtype=jnp.int32)
    slot_ids = jnp.arange(row.shape[0], dtype=jnp.int32)
    matches = row_owner[None, :] == sources[:, None]
    present = jnp.any(matches, axis=1)
    slot_of = jnp.sum(jnp.where(matches, slot_ids[None, :], 0), axis=1)
    nvalid = jnp.where(present, jnp.clip(length - slot_of * page_size, 0, page_size), 0)
    within = jnp.arange(page_size, dtype=jnp.int32)
    return (within[None, :] < nvalid[:, None]).astype(jnp.int32).reshape(1, source_count * page_size)


def by_rows(stat):
    return jnp.transpose(stat, (1, 0, 2))


def on_device(new_queries, new_keys, new_values, kv_pages, page_table, cache_len, w_out, out_bias):
    half = lax.axis_index("half")
    sub = lax.axis_index("sub")
    sub_count = lax.axis_size("sub")
    tp_index = lax.axis_index("tp")
    tp_count = lax.axis_size("tp")
    own_index = half * sub_count + sub
    partner = (1 - half) * sub_count + sub
    span_len = new_queries.shape[0]
    width = new_queries.shape[1]
    head_count = width // HEAD_DIM
    page_count = kv_pages.shape[0]
    page_size = kv_pages.shape[2]
    out_cols = w_out.shape[1] // tp_count
    swap = [(0, 1), (1, 0)]

    w_recv = []
    for shift in range(1, tp_count):
        target = (tp_index + shift) % tp_count
        piece = lax.dynamic_slice_in_dim(w_out, target * out_cols, out_cols, axis=1)
        perm = [(i, (i + shift) % tp_count) for i in range(tp_count)]
        w_recv.append(lax.ppermute(piece, "tp", perm))
    w_mine = lax.dynamic_slice_in_dim(w_out, tp_index * out_cols, out_cols, axis=1)

    owners = jnp.where(page_table >= 0, page_table // page_count, -1)
    held_here = owners == own_index
    local_page = jnp.sum(jnp.where(held_here, page_table - own_index * page_count, 0), axis=1)
    dest = jnp.arange(sub_count, dtype=jnp.int32)
    far_pages = jnp.take(kv_pages, jnp.take(local_page, (1 - half) * sub_count + dest), axis=0, mode="clip")
    far_incoming = lax.all_to_all(far_pages, "sub", split_axis=0, concat_axis=0, tiled=True)
    near_pages = jnp.take(kv_pages, jnp.take(local_page, half * sub_count + dest), axis=0, mode="clip")
    near_incoming = lax.all_to_all(near_pages, "sub", split_axis=0, concat_axis=0, tiled=True)

    own_length = lax.dynamic_index_in_dim(cache_len, own_index, 0, keepdims=False)
    partner_length = lax.dynamic_index_in_dim(cache_len, partner, 0, keepdims=False)
    positions = own_length + jnp.arange(span_len, dtype=jnp.int32)
    query_rot = rotate_rows(new_queries, positions)
    key_rot = rotate_rows(new_keys, positions)
    partner_query = lax.ppermute(query_rot, "half", swap)

    source_base = half * sub_count
    ok_own = usable_keys(page_table, own_index, own_length, source_base, sub_count, page_count, page_size)
    ok_partner = usable_keys(page_table, partner, partner_length, source_base, sub_count, page_count, page_size)

    far_out, far_max, far_sum = attend(ok_partner, partner_query, far_incoming, jnp.bfloat16)
    far_stats = jnp.concatenate([far_max, far_sum], axis=2)
    back_out = lax.ppermute(far_out, "half", swap)
    back_stats = lax.ppermute(far_stats, "half", swap)
    near_out, near_max, near_sum = attend(
        ok_own, query_rot, near_incoming, jnp.float32, local=(key_rot, new_values)
    )

    near_max = by_rows(near_max)
    near_sum = by_rows(near_sum)
    back_stats = by_rows(back_stats)
    back_max = back_stats[:, :, 0:1]
    back_sum = back_stats[:, :, 1:2]
    peak = jnp.maximum(near_max, back_max)
    near_w = jnp.exp(near_max - peak) * near_sum
    back_w = jnp.exp(back_max - peak) * back_sum
    near3 = near_out.reshape(span_len, head_count, HEAD_DIM)
    back3 = back_out.astype(jnp.float32).reshape(span_len, head_count, HEAD_DIM)
    merged = (near3 * near_w + back3 * back_w) / (near_w + back_w)
    attended = merged.reshape(span_len, width).astype(jnp.bfloat16)

    summed = jnp.dot(attended, w_mine, preferred_element_type=jnp.float32)
    for shift in range(1, tp_count):
        perm = [(i, (i + shift) % tp_count) for i in range(tp_count)]
        other = lax.ppermute(attended, "tp", perm)
        summed = summed + jnp.dot(other, w_recv[shift - 1], preferred_element_type=jnp.float32)
    return (summed + out_bias.astype(jnp.float32)).astype(jnp.bfloat16)


def solution(mesh):
    req_count = mesh.shape["req"]
    tp_count = mesh.shape["tp"]
    assert tuple(mesh.axis_names) == ("req", "tp")
    devices = mesh.devices.reshape(2, req_count // 2, tp_count)
    split_mesh = jax.sharding.Mesh(devices, ("half", "sub", "tp"))
    rows = ("half", "sub")
    return jax.shard_map(
        on_device,
        mesh=split_mesh,
        in_specs=(
            P(rows, "tp"),
            P(rows, "tp"),
            P(rows, "tp"),
            P(rows, None, None, "tp"),
            P(),
            P(),
            P("tp", None),
            P("tp"),
        ),
        out_specs=P(rows, "tp"),
        check_vma=False,
    )
```

```python
import math
from functools import partial

import jax
import jax.numpy as jnp
from jax import lax
from jax.experimental import pallas as pl
from jax.experimental.pallas import tpu as pltpu
from jax.sharding import PartitionSpec as P

HEAD_DIM = 128
ROT = 32


NEG_FILL = -1e30


def rotate_rows(block, positions):
    row_count = block.shape[0]
    shaped = block.astype(jnp.float32).reshape(row_count, -1, HEAD_DIM)
    half_rot = ROT // 2
    frequency = 10000.0 ** (-2.0 * jnp.arange(half_rot, dtype=jnp.float32) / ROT)
    angles = positions.astype(jnp.float32)[:, None] * frequency[None, :]
    cosine = jnp.cos(angles)[:, None, :]
    sines = jnp.sin(angles)[:, None, :]
    first_half = shaped[:, :, :half_rot]
    second_half = shaped[:, :, half_rot:ROT]
    turned = jnp.concatenate(
        [
            first_half * cosine - second_half * sines,
            second_half * cosine + first_half * sines,
            shaped[:, :, ROT:],
        ],
        axis=2,
    )
    return turned.reshape(row_count, -1).astype(jnp.bfloat16)


def attention_kernel(*refs, with_local):
    if with_local:
        q_ref, kl_ref, vl_ref, kp_ref, vp_ref, ok_ref, o_ref, m_ref, l_ref = refs
    else:
        q_ref, kp_ref, vp_ref, ok_ref, o_ref, m_ref, l_ref = refs
    score_scale = 1.0 / math.sqrt(HEAD_DIM)
    dims = (((1,), (1,)), ((), ()))
    q = q_ref[...]
    span = q.shape[0]
    block_count, page_size, _ = kp_ref.shape
    keys_p = kp_ref[...].reshape(block_count * page_size, HEAD_DIM)
    values_p = vp_ref[...].reshape(block_count * page_size, HEAD_DIM)

    s_pg = lax.dot_general(q, keys_p, dims, preferred_element_type=jnp.float32) * score_scale
    s_pg = jnp.where(ok_ref[...] > 0, s_pg, NEG_FILL)
    m = jnp.max(s_pg, axis=1, keepdims=True)
    if with_local:
        s_loc = lax.dot_general(q, kl_ref[...], dims, preferred_element_type=jnp.float32) * score_scale
        row = lax.broadcasted_iota(jnp.int32, (span, span), 0)
        col = lax.broadcasted_iota(jnp.int32, (span, span), 1)
        s_loc = jnp.where(row >= col, s_loc, NEG_FILL)
        m = jnp.maximum(m, jnp.max(s_loc, axis=1, keepdims=True))
    p_pg = jnp.exp(s_pg - m)
    l = jnp.sum(p_pg, axis=1, keepdims=True)
    acc = jnp.dot(p_pg.astype(jnp.bfloat16), values_p, preferred_element_type=jnp.float32)
    if with_local:
        p_loc = jnp.exp(s_loc - m)
        l = l + jnp.sum(p_loc, axis=1, keepdims=True)
        acc = acc + jnp.dot(p_loc.astype(jnp.bfloat16), vl_ref[...], preferred_element_type=jnp.float32)
    o_ref[...] = (acc / l).astype(o_ref.dtype)
    m_ref[...] = m
    l_ref[...] = l


def attend(key_ok, query_rot, incoming, out_dtype, local=None):
    span, width = query_rot.shape
    head_count = width // HEAD_DIM
    block_count = incoming.shape[0]
    page_size = incoming.shape[2]
    col_spec = pl.BlockSpec((span, HEAD_DIM), lambda h: (0, h))
    page_specs = [
        pl.BlockSpec((block_count, None, page_size, HEAD_DIM), lambda h: (0, 0, 0, h)),
        pl.BlockSpec((block_count, None, page_size, HEAD_DIM), lambda h: (0, 1, 0, h)),
        pl.BlockSpec((1, block_count * page_size), lambda h: (0, 0)),
    ]
    stat_spec = pl.BlockSpec((None, span, 1), lambda h: (h, 0, 0))
    if local is None:
        in_specs = [col_spec] + page_specs
        operands = (query_rot, incoming, incoming, key_ok)
    else:
        in_specs = [col_spec, col_spec, col_spec] + page_specs
        operands = (query_rot, local[0], local[1], incoming, incoming, key_ok)
    return pl.pallas_call(
        partial(attention_kernel, with_local=local is not None),
        grid=(head_count,),
        in_specs=in_specs,
        out_specs=[col_spec, stat_spec, stat_spec],
        out_shape=[
            jax.ShapeDtypeStruct((span, width), out_dtype),
            jax.ShapeDtypeStruct((head_count, span, 1), jnp.float32),
            jax.ShapeDtypeStruct((head_count, span, 1), jnp.float32),
        ],
    )(*operands)


def usable_keys(page_table, request, length, source_base, source_count, page_count, page_size):
    row = lax.dynamic_index_in_dim(page_table, request, 0, keepdims=False)
    row_owner = jnp.where(row >= 0, row // page_count, -1)
    sources = source_base + jnp.arange(source_count, dtype=jnp.int32)
    slot_ids = jnp.arange(row.shape[0], dtype=jnp.int32)
    matches = row_owner[None, :] == sources[:, None]
    present = jnp.any(matches, axis=1)
    slot_of = jnp.sum(jnp.where(matches, slot_ids[None, :], 0), axis=1)
    nvalid = jnp.where(present, jnp.clip(length - slot_of * page_size, 0, page_size), 0)
    within = jnp.arange(page_size, dtype=jnp.int32)
    return (within[None, :] < nvalid[:, None]).astype(jnp.int32).reshape(1, source_count * page_size)


def by_rows(stat):
    return jnp.transpose(stat, (1, 0, 2))


def on_device(new_queries, new_keys, new_values, kv_pages, page_table, cache_len, w_out, out_bias):
    half = lax.axis_index("half")
    sub = lax.axis_index("sub")
    sub_count = lax.axis_size("sub")
    tp_index = lax.axis_index("tp")
    tp_count = lax.axis_size("tp")
    own_index = half * sub_count + sub
    partner = (1 - half) * sub_count + sub
    span_len = new_queries.shape[0]
    width = new_queries.shape[1]
    head_count = width // HEAD_DIM
    page_count = kv_pages.shape[0]
    page_size = kv_pages.shape[2]
    out_cols = w_out.shape[1] // tp_count
    swap = [(0, 1), (1, 0)]

    w_recv = []
    for shift in range(1, tp_count):
        target = (tp_index + shift) % tp_count
        piece = lax.dynamic_slice_in_dim(w_out, target * out_cols, out_cols, axis=1)
        perm = [(i, (i + shift) % tp_count) for i in range(tp_count)]
        w_recv.append(lax.ppermute(piece, "tp", perm))
    w_mine = lax.dynamic_slice_in_dim(w_out, tp_index * out_cols, out_cols, axis=1)

    owners = jnp.where(page_table >= 0, page_table // page_count, -1)
    held_here = owners == own_index
    local_page = jnp.sum(jnp.where(held_here, page_table - own_index * page_count, 0), axis=1)
    dest = jnp.arange(sub_count, dtype=jnp.int32)
    own_length = lax.dynamic_index_in_dim(cache_len, own_index, 0, keepdims=False)
    partner_length = lax.dynamic_index_in_dim(cache_len, partner, 0, keepdims=False)
    positions = own_length + jnp.arange(span_len, dtype=jnp.int32)
    query_rot = rotate_rows(new_queries, positions)
    partner_query = lax.ppermute(query_rot, "half", swap)

    far_pages = jnp.take(kv_pages, jnp.take(local_page, (1 - half) * sub_count + dest), axis=0, mode="clip")
    partner_query, far_pages = lax.optimization_barrier((partner_query, far_pages))
    far_incoming = lax.all_to_all(far_pages, "sub", split_axis=0, concat_axis=0, tiled=True)
    near_pages = jnp.take(kv_pages, jnp.take(local_page, half * sub_count + dest), axis=0, mode="clip")
    near_incoming = lax.all_to_all(near_pages, "sub", split_axis=0, concat_axis=0, tiled=True)
    key_rot = rotate_rows(new_keys, positions)

    source_base = half * sub_count
    ok_own = usable_keys(page_table, own_index, own_length, source_base, sub_count, page_count, page_size)
    ok_partner = usable_keys(page_table, partner, partner_length, source_base, sub_count, page_count, page_size)

    far_out, far_max, far_sum = attend(ok_partner, partner_query, far_incoming, jnp.bfloat16)
    far_stats = jnp.concatenate([far_max, far_sum], axis=2)
    back_out = lax.ppermute(far_out, "half", swap)
    back_stats = lax.ppermute(far_stats, "half", swap)
    near_out, near_max, near_sum = attend(
        ok_own, query_rot, near_incoming, jnp.float32, local=(key_rot, new_values)
    )

    near_max = by_rows(near_max)
    near_sum = by_rows(near_sum)
    back_stats = by_rows(back_stats)
    back_max = back_stats[:, :, 0:1]
    back_sum = back_stats[:, :, 1:2]
    peak = jnp.maximum(near_max, back_max)
    near_w = jnp.exp(near_max - peak) * near_sum
    back_w = jnp.exp(back_max - peak) * back_sum
    near3 = near_out.reshape(span_len, head_count, HEAD_DIM)
    back3 = back_out.astype(jnp.float32).reshape(span_len, head_count, HEAD_DIM)
    merged = (near3 * near_w + back3 * back_w) / (near_w + back_w)
    attended = merged.reshape(span_len, width).astype(jnp.bfloat16)

    summed = jnp.dot(attended, w_mine, preferred_element_type=jnp.float32)
    for shift in range(1, tp_count):
        perm = [(i, (i + shift) % tp_count) for i in range(tp_count)]
        other = lax.ppermute(attended, "tp", perm)
        summed = summed + jnp.dot(other, w_recv[shift - 1], preferred_element_type=jnp.float32)
    return (summed + out_bias.astype(jnp.float32)).astype(jnp.bfloat16)


def solution(mesh):
    req_count = mesh.shape["req"]
    tp_count = mesh.shape["tp"]
    assert tuple(mesh.axis_names) == ("req", "tp")
    devices = mesh.devices.reshape(2, req_count // 2, tp_count)
    split_mesh = jax.sharding.Mesh(devices, ("half", "sub", "tp"))
    rows = ("half", "sub")
    return jax.shard_map(
        on_device,
        mesh=split_mesh,
        in_specs=(
            P(rows, "tp"),
            P(rows, "tp"),
            P(rows, "tp"),
            P(rows, None, None, "tp"),
            P(),
            P(),
            P("tp", None),
            P("tp"),
        ),
        out_specs=P(rows, "tp"),
        check_vma=False,
    )
```

```python
import math
from functools import partial

import jax
import jax.numpy as jnp
from jax import lax
from jax.experimental import pallas as pl
from jax.experimental.pallas import tpu as pltpu
from jax.sharding import PartitionSpec as P

HEAD_DIM = 128
ROT = 32


NEG_FILL = -1e30


def rotate_rows(block, positions):
    row_count = block.shape[0]
    shaped = block.astype(jnp.float32).reshape(row_count, -1, HEAD_DIM)
    half_rot = ROT // 2
    frequency = 10000.0 ** (-2.0 * jnp.arange(half_rot, dtype=jnp.float32) / ROT)
    angles = positions.astype(jnp.float32)[:, None] * frequency[None, :]
    cosine = jnp.cos(angles)[:, None, :]
    sines = jnp.sin(angles)[:, None, :]
    first_half = shaped[:, :, :half_rot]
    second_half = shaped[:, :, half_rot:ROT]
    turned = jnp.concatenate(
        [
            first_half * cosine - second_half * sines,
            second_half * cosine + first_half * sines,
            shaped[:, :, ROT:],
        ],
        axis=2,
    )
    return turned.reshape(row_count, -1).astype(jnp.bfloat16)


def attention_kernel(*refs, with_local):
    if with_local:
        q_ref, kl_ref, vl_ref, kp_ref, vp_ref, ok_ref, bo_ref, bst_ref, o_ref = refs
    else:
        q_ref, kp_ref, vp_ref, ok_ref, o_ref, st_ref = refs
    score_scale = 1.0 / math.sqrt(HEAD_DIM)
    dims = (((1,), (1,)), ((), ()))
    q = q_ref[...]
    span = q.shape[0]
    block_count, page_size, _ = kp_ref.shape
    keys_p = kp_ref[...].reshape(block_count * page_size, HEAD_DIM)
    values_p = vp_ref[...].reshape(block_count * page_size, HEAD_DIM)

    s_pg = lax.dot_general(q, keys_p, dims, preferred_element_type=jnp.float32) * score_scale
    s_pg = jnp.where(ok_ref[...] > 0, s_pg, NEG_FILL)
    m = jnp.max(s_pg, axis=1, keepdims=True)
    if with_local:
        s_loc = lax.dot_general(q, kl_ref[...], dims, preferred_element_type=jnp.float32) * score_scale
        row = lax.broadcasted_iota(jnp.int32, (span, span), 0)
        col = lax.broadcasted_iota(jnp.int32, (span, span), 1)
        s_loc = jnp.where(row >= col, s_loc, NEG_FILL)
        m = jnp.maximum(m, jnp.max(s_loc, axis=1, keepdims=True))
    p_pg = jnp.exp(s_pg - m)
    l = jnp.sum(p_pg, axis=1, keepdims=True)
    acc = jnp.dot(p_pg.astype(jnp.bfloat16), values_p, preferred_element_type=jnp.float32)
    if with_local:
        p_loc = jnp.exp(s_loc - m)
        l = l + jnp.sum(p_loc, axis=1, keepdims=True)
        acc = acc + jnp.dot(p_loc.astype(jnp.bfloat16), vl_ref[...], preferred_element_type=jnp.float32)
        stats = bst_ref[...]
        back_max = stats[:, 0:1]
        back_sum = stats[:, 1:2]
        peak = jnp.maximum(m, back_max)
        near_w = jnp.exp(m - peak)
        back_w = jnp.exp(back_max - peak) * back_sum
        merged = acc * near_w + bo_ref[...].astype(jnp.float32) * back_w
        o_ref[...] = (merged / (l * near_w + back_w)).astype(o_ref.dtype)
    else:
        o_ref[...] = (acc / l).astype(o_ref.dtype)
        st_ref[:, 0:1] = m
        st_ref[:, 1:2] = l


def attend(key_ok, query_rot, incoming, which, local=None, back=None):
    span, width = query_rot.shape
    head_count = width // HEAD_DIM
    block_count = incoming.shape[0]
    page_size = incoming.shape[3]
    col_spec = pl.BlockSpec((span, HEAD_DIM), lambda h: (0, h))
    page_specs = [
        pl.BlockSpec((block_count, None, None, page_size, HEAD_DIM), lambda h: (0, which, 0, 0, h)),
        pl.BlockSpec((block_count, None, None, page_size, HEAD_DIM), lambda h: (0, which, 1, 0, h)),
        pl.BlockSpec((1, block_count * page_size), lambda h: (0, 0)),
    ]
    stat_spec = pl.BlockSpec((None, span, 2), lambda h: (h, 0, 0))
    out_shape = jax.ShapeDtypeStruct((span, width), jnp.bfloat16)
    if local is None:
        in_specs = [col_spec] + page_specs
        operands = (query_rot, incoming, incoming, key_ok)
        out_specs = [col_spec, stat_spec]
        out_shape = [out_shape, jax.ShapeDtypeStruct((head_count, span, 2), jnp.float32)]
    else:
        in_specs = [col_spec, col_spec, col_spec] + page_specs + [col_spec, stat_spec]
        operands = (query_rot, local[0], local[1], incoming, incoming, key_ok, back[0], back[1])
        out_specs = col_spec
    return pl.pallas_call(
        partial(attention_kernel, with_local=local is not None),
        grid=(head_count,),
        in_specs=in_specs,
        out_specs=out_specs,
        out_shape=out_shape,
    )(*operands)


def usable_keys(page_table, request, length, source_base, source_count, page_count, page_size):
    row = lax.dynamic_index_in_dim(page_table, request, 0, keepdims=False)
    row_owner = jnp.where(row >= 0, row // page_count, -1)
    sources = source_base + jnp.arange(source_count, dtype=jnp.int32)
    slot_ids = jnp.arange(row.shape[0], dtype=jnp.int32)
    matches = row_owner[None, :] == sources[:, None]
    present = jnp.any(matches, axis=1)
    slot_of = jnp.sum(jnp.where(matches, slot_ids[None, :], 0), axis=1)
    nvalid = jnp.where(present, jnp.clip(length - slot_of * page_size, 0, page_size), 0)
    within = jnp.arange(page_size, dtype=jnp.int32)
    return (within[None, :] < nvalid[:, None]).astype(jnp.int32).reshape(1, source_count * page_size)


def on_device(new_queries, new_keys, new_values, kv_pages, page_table, cache_len, w_out, out_bias):
    half = lax.axis_index("half")
    sub = lax.axis_index("sub")
    sub_count = lax.axis_size("sub")
    tp_index = lax.axis_index("tp")
    tp_count = lax.axis_size("tp")
    own_index = half * sub_count + sub
    partner = (1 - half) * sub_count + sub
    span_len = new_queries.shape[0]
    width = new_queries.shape[1]
    head_count = width // HEAD_DIM
    page_count = kv_pages.shape[0]
    page_size = kv_pages.shape[2]
    out_cols = w_out.shape[1] // tp_count
    swap = [(0, 1), (1, 0)]

    w_recv = []
    for shift in range(1, tp_count):
        target = (tp_index + shift) % tp_count
        piece = lax.dynamic_slice_in_dim(w_out, target * out_cols, out_cols, axis=1)
        perm = [(i, (i + shift) % tp_count) for i in range(tp_count)]
        w_recv.append(lax.ppermute(piece, "tp", perm))
    w_mine = lax.dynamic_slice_in_dim(w_out, tp_index * out_cols, out_cols, axis=1)

    owners = jnp.where(page_table >= 0, page_table // page_count, -1)
    held_here = owners == own_index
    local_page = jnp.sum(jnp.where(held_here, page_table - own_index * page_count, 0), axis=1)
    dest = jnp.arange(sub_count, dtype=jnp.int32)
    wanted = jnp.stack([half * sub_count + dest, (1 - half) * sub_count + dest], axis=1).reshape(-1)
    outgoing = jnp.take(kv_pages, jnp.take(local_page, wanted), axis=0, mode="clip")
    outgoing = outgoing.reshape((sub_count, 2) + kv_pages.shape[1:])
    incoming = lax.all_to_all(outgoing, "sub", split_axis=0, concat_axis=0, tiled=True)

    own_length = lax.dynamic_index_in_dim(cache_len, own_index, 0, keepdims=False)
    partner_length = lax.dynamic_index_in_dim(cache_len, partner, 0, keepdims=False)
    positions = own_length + jnp.arange(span_len, dtype=jnp.int32)
    query_rot = rotate_rows(new_queries, positions)
    key_rot = rotate_rows(new_keys, positions)
    partner_query = lax.ppermute(query_rot, "half", swap)

    source_base = half * sub_count
    ok_own = usable_keys(page_table, own_index, own_length, source_base, sub_count, page_count, page_size)
    ok_partner = usable_keys(page_table, partner, partner_length, source_base, sub_count, page_count, page_size)

    far_out, far_stats = attend(ok_partner, partner_query, incoming, 1)
    back_out = lax.ppermute(far_out, "half", swap)
    back_stats = lax.ppermute(far_stats, "half", swap)
    attended = attend(
        ok_own, query_rot, incoming, 0, local=(key_rot, new_values), back=(back_out, back_stats)
    )

    summed = jnp.dot(attended, w_mine, preferred_element_type=jnp.float32)
    for shift in range(1, tp_count):
        perm = [(i, (i + shift) % tp_count) for i in range(tp_count)]
        other = lax.ppermute(attended, "tp", perm)
        summed = summed + jnp.dot(other, w_recv[shift - 1], preferred_element_type=jnp.float32)
    return (summed + out_bias.astype(jnp.float32)).astype(jnp.bfloat16)


def solution(mesh):
    req_count = mesh.shape["req"]
    tp_count = mesh.shape["tp"]
    assert tuple(mesh.axis_names) == ("req", "tp")
    devices = mesh.devices.reshape(2, req_count // 2, tp_count)
    split_mesh = jax.sharding.Mesh(devices, ("half", "sub", "tp"))
    rows = ("half", "sub")
    return jax.shard_map(
        on_device,
        mesh=split_mesh,
        in_specs=(
            P(rows, "tp"),
            P(rows, "tp"),
            P(rows, "tp"),
            P(rows, None, None, "tp"),
            P(),
            P(),
            P("tp", None),
            P("tp"),
        ),
        out_specs=P(rows, "tp"),
        check_vma=False,
    )
```

```python
import math
from functools import partial

import jax
import jax.numpy as jnp
from jax import lax
from jax.experimental import pallas as pl
from jax.experimental.pallas import tpu as pltpu
from jax.sharding import PartitionSpec as P

HEAD_DIM = 128
ROT = 32


NEG_FILL = -1e30


def rotate_rows(block, positions):
    row_count = block.shape[0]
    shaped = block.astype(jnp.float32).reshape(row_count, -1, HEAD_DIM)
    half_rot = ROT // 2
    frequency = 10000.0 ** (-2.0 * jnp.arange(half_rot, dtype=jnp.float32) / ROT)
    angles = positions.astype(jnp.float32)[:, None] * frequency[None, :]
    cosine = jnp.cos(angles)[:, None, :]
    sines = jnp.sin(angles)[:, None, :]
    first_half = shaped[:, :, :half_rot]
    second_half = shaped[:, :, half_rot:ROT]
    turned = jnp.concatenate(
        [
            first_half * cosine - second_half * sines,
            second_half * cosine + first_half * sines,
            shaped[:, :, ROT:],
        ],
        axis=2,
    )
    return turned.reshape(row_count, -1).astype(jnp.bfloat16)


def attention_kernel(*refs, with_local):
    if with_local:
        q_ref, kl_ref, vl_ref, kp_ref, vp_ref, ok_ref, o_ref, st_ref = refs
    else:
        q_ref, kp_ref, vp_ref, ok_ref, o_ref, st_ref = refs
    score_scale = 1.0 / math.sqrt(HEAD_DIM)
    dims = (((1,), (1,)), ((), ()))
    q = q_ref[...]
    span = q.shape[0]
    block_count, page_size, _ = kp_ref.shape
    keys_p = kp_ref[...].reshape(block_count * page_size, HEAD_DIM)
    values_p = vp_ref[...].reshape(block_count * page_size, HEAD_DIM)

    s_pg = lax.dot_general(q, keys_p, dims, preferred_element_type=jnp.float32) * score_scale
    s_pg = jnp.where(ok_ref[...] > 0, s_pg, NEG_FILL)
    m = jnp.max(s_pg, axis=1, keepdims=True)
    if with_local:
        s_loc = lax.dot_general(q, kl_ref[...], dims, preferred_element_type=jnp.float32) * score_scale
        row = lax.broadcasted_iota(jnp.int32, (span, span), 0)
        col = lax.broadcasted_iota(jnp.int32, (span, span), 1)
        s_loc = jnp.where(row >= col, s_loc, NEG_FILL)
        m = jnp.maximum(m, jnp.max(s_loc, axis=1, keepdims=True))
    p_pg = jnp.exp(s_pg - m)
    l = jnp.sum(p_pg, axis=1, keepdims=True)
    acc = jnp.dot(p_pg.astype(jnp.bfloat16), values_p, preferred_element_type=jnp.float32)
    if with_local:
        p_loc = jnp.exp(s_loc - m)
        l = l + jnp.sum(p_loc, axis=1, keepdims=True)
        acc = acc + jnp.dot(p_loc.astype(jnp.bfloat16), vl_ref[...], preferred_element_type=jnp.float32)
        o_ref[...] = acc
        st_ref[:, 0:1] = m
        st_ref[:, 1:2] = l
    else:
        o_ref[...] = (acc / l).astype(o_ref.dtype)
        st_ref[:, 0:1] = m
        st_ref[:, 1:2] = l


def attend(key_ok, query_rot, incoming, which, local=None):
    span, width = query_rot.shape
    head_count = width // HEAD_DIM
    block_count = incoming.shape[0]
    page_size = incoming.shape[3]
    col_spec = pl.BlockSpec((span, HEAD_DIM), lambda h: (0, h))
    page_specs = [
        pl.BlockSpec((block_count, None, None, page_size, HEAD_DIM), lambda h: (0, which, 0, 0, h)),
        pl.BlockSpec((block_count, None, None, page_size, HEAD_DIM), lambda h: (0, which, 1, 0, h)),
        pl.BlockSpec((1, block_count * page_size), lambda h: (0, 0)),
    ]
    stat_spec = pl.BlockSpec((None, span, 2), lambda h: (h, 0, 0))
    stat_shape = jax.ShapeDtypeStruct((head_count, span, 2), jnp.float32)
    out_specs = [col_spec, stat_spec]
    if local is None:
        in_specs = [col_spec] + page_specs
        operands = (query_rot, incoming, incoming, key_ok)
        out_shape = [jax.ShapeDtypeStruct((span, width), jnp.bfloat16), stat_shape]
    else:
        in_specs = [col_spec, col_spec, col_spec] + page_specs
        operands = (query_rot, local[0], local[1], incoming, incoming, key_ok)
        out_shape = [jax.ShapeDtypeStruct((span, width), jnp.float32), stat_shape]
    return pl.pallas_call(
        partial(attention_kernel, with_local=local is not None),
        grid=(head_count,),
        in_specs=in_specs,
        out_specs=out_specs,
        out_shape=out_shape,
    )(*operands)


def merge_kernel(na_ref, nst_ref, bo_ref, bst_ref, o_ref):
    near = nst_ref[...]
    back = bst_ref[...]
    near_max = near[:, 0:1]
    near_sum = near[:, 1:2]
    back_max = back[:, 0:1]
    back_sum = back[:, 1:2]
    peak = jnp.maximum(near_max, back_max)
    near_w = jnp.exp(near_max - peak)
    back_w = jnp.exp(back_max - peak) * back_sum
    merged = na_ref[...] * near_w + bo_ref[...].astype(jnp.float32) * back_w
    o_ref[...] = (merged / (near_sum * near_w + back_w)).astype(o_ref.dtype)


def merge(near_acc, near_stats, back_out, back_stats):
    span, width = near_acc.shape
    col_spec = pl.BlockSpec((span, HEAD_DIM), lambda h: (0, h))
    stat_spec = pl.BlockSpec((None, span, 2), lambda h: (h, 0, 0))
    return pl.pallas_call(
        merge_kernel,
        grid=(width // HEAD_DIM,),
        in_specs=[col_spec, stat_spec, col_spec, stat_spec],
        out_specs=col_spec,
        out_shape=jax.ShapeDtypeStruct((span, width), jnp.bfloat16),
    )(near_acc, near_stats, back_out, back_stats)


def usable_keys(page_table, request, length, source_base, source_count, page_count, page_size):
    row = lax.dynamic_index_in_dim(page_table, request, 0, keepdims=False)
    row_owner = jnp.where(row >= 0, row // page_count, -1)
    sources = source_base + jnp.arange(source_count, dtype=jnp.int32)
    slot_ids = jnp.arange(row.shape[0], dtype=jnp.int32)
    matches = row_owner[None, :] == sources[:, None]
    present = jnp.any(matches, axis=1)
    slot_of = jnp.sum(jnp.where(matches, slot_ids[None, :], 0), axis=1)
    nvalid = jnp.where(present, jnp.clip(length - slot_of * page_size, 0, page_size), 0)
    within = jnp.arange(page_size, dtype=jnp.int32)
    return (within[None, :] < nvalid[:, None]).astype(jnp.int32).reshape(1, source_count * page_size)


def on_device(new_queries, new_keys, new_values, kv_pages, page_table, cache_len, w_out, out_bias):
    half = lax.axis_index("half")
    sub = lax.axis_index("sub")
    sub_count = lax.axis_size("sub")
    tp_index = lax.axis_index("tp")
    tp_count = lax.axis_size("tp")
    own_index = half * sub_count + sub
    partner = (1 - half) * sub_count + sub
    span_len = new_queries.shape[0]
    width = new_queries.shape[1]
    head_count = width // HEAD_DIM
    page_count = kv_pages.shape[0]
    page_size = kv_pages.shape[2]
    out_cols = w_out.shape[1] // tp_count
    swap = [(0, 1), (1, 0)]

    w_recv = []
    for shift in range(1, tp_count):
        target = (tp_index + shift) % tp_count
        piece = lax.dynamic_slice_in_dim(w_out, target * out_cols, out_cols, axis=1)
        perm = [(i, (i + shift) % tp_count) for i in range(tp_count)]
        w_recv.append(lax.ppermute(piece, "tp", perm))
    w_mine = lax.dynamic_slice_in_dim(w_out, tp_index * out_cols, out_cols, axis=1)

    owners = jnp.where(page_table >= 0, page_table // page_count, -1)
    held_here = owners == own_index
    local_page = jnp.sum(jnp.where(held_here, page_table - own_index * page_count, 0), axis=1)
    dest = jnp.arange(sub_count, dtype=jnp.int32)
    wanted = jnp.stack([half * sub_count + dest, (1 - half) * sub_count + dest], axis=1).reshape(-1)
    outgoing = jnp.take(kv_pages, jnp.take(local_page, wanted), axis=0, mode="clip")
    outgoing = outgoing.reshape((sub_count, 2) + kv_pages.shape[1:])
    incoming = lax.all_to_all(outgoing, "sub", split_axis=0, concat_axis=0, tiled=True)

    own_length = lax.dynamic_index_in_dim(cache_len, own_index, 0, keepdims=False)
    partner_length = lax.dynamic_index_in_dim(cache_len, partner, 0, keepdims=False)
    positions = own_length + jnp.arange(span_len, dtype=jnp.int32)
    query_rot = rotate_rows(new_queries, positions)
    key_rot = rotate_rows(new_keys, positions)
    partner_query = lax.ppermute(query_rot, "half", swap)

    source_base = half * sub_count
    ok_own = usable_keys(page_table, own_index, own_length, source_base, sub_count, page_count, page_size)
    ok_partner = usable_keys(page_table, partner, partner_length, source_base, sub_count, page_count, page_size)

    far_out, far_stats = attend(ok_partner, partner_query, incoming, 1)
    back_out = lax.ppermute(far_out, "half", swap)
    back_stats = lax.ppermute(far_stats, "half", swap)
    near_acc, near_stats = attend(ok_own, query_rot, incoming, 0, local=(key_rot, new_values))
    attended = merge(near_acc, near_stats, back_out, back_stats)

    summed = jnp.dot(attended, w_mine, preferred_element_type=jnp.float32)
    for shift in range(1, tp_count):
        perm = [(i, (i + shift) % tp_count) for i in range(tp_count)]
        other = lax.ppermute(attended, "tp", perm)
        summed = summed + jnp.dot(other, w_recv[shift - 1], preferred_element_type=jnp.float32)
    return (summed + out_bias.astype(jnp.float32)).astype(jnp.bfloat16)


def solution(mesh):
    req_count = mesh.shape["req"]
    tp_count = mesh.shape["tp"]
    assert tuple(mesh.axis_names) == ("req", "tp")
    devices = mesh.devices.reshape(2, req_count // 2, tp_count)
    split_mesh = jax.sharding.Mesh(devices, ("half", "sub", "tp"))
    rows = ("half", "sub")
    return jax.shard_map(
        on_device,
        mesh=split_mesh,
        in_specs=(
            P(rows, "tp"),
            P(rows, "tp"),
            P(rows, "tp"),
            P(rows, None, None, "tp"),
            P(),
            P(),
            P("tp", None),
            P("tp"),
        ),
        out_specs=P(rows, "tp"),
        check_vma=False,
    )
```

```python
import math
from functools import partial

import jax
import jax.numpy as jnp
from jax import lax
from jax.experimental import pallas as pl
from jax.experimental.pallas import tpu as pltpu
from jax.sharding import PartitionSpec as P

HEAD_DIM = 128
ROT = 32


NEG_FILL = -1e30


def rotate_rows(block, positions):
    row_count = block.shape[0]
    shaped = block.astype(jnp.float32).reshape(row_count, -1, HEAD_DIM)
    half_rot = ROT // 2
    frequency = 10000.0 ** (-2.0 * jnp.arange(half_rot, dtype=jnp.float32) / ROT)
    angles = positions.astype(jnp.float32)[:, None] * frequency[None, :]
    cosine = jnp.cos(angles)[:, None, :]
    sines = jnp.sin(angles)[:, None, :]
    first_half = shaped[:, :, :half_rot]
    second_half = shaped[:, :, half_rot:ROT]
    turned = jnp.concatenate(
        [
            first_half * cosine - second_half * sines,
            second_half * cosine + first_half * sines,
            shaped[:, :, ROT:],
        ],
        axis=2,
    )
    return turned.reshape(row_count, -1).astype(jnp.bfloat16)


def attention_kernel(*refs, with_local):
    if with_local:
        q_ref, kl_ref, vl_ref, kp_ref, vp_ref, ok_ref, o_ref, m_ref, l_ref = refs
    else:
        q_ref, kp_ref, vp_ref, ok_ref, o_ref, m_ref, l_ref = refs
    score_scale = 1.0 / math.sqrt(HEAD_DIM)
    dims = (((1,), (1,)), ((), ()))
    q = q_ref[...]
    span = q.shape[0]
    block_count, page_size, _ = kp_ref.shape
    keys_p = kp_ref[...].reshape(block_count * page_size, HEAD_DIM)
    values_p = vp_ref[...].reshape(block_count * page_size, HEAD_DIM)

    s_pg = lax.dot_general(q, keys_p, dims, preferred_element_type=jnp.float32) * score_scale
    s_pg = jnp.where(ok_ref[...] > 0, s_pg, NEG_FILL)
    m = jnp.max(s_pg, axis=1, keepdims=True)
    if with_local:
        s_loc = lax.dot_general(q, kl_ref[...], dims, preferred_element_type=jnp.float32) * score_scale
        row = lax.broadcasted_iota(jnp.int32, (span, span), 0)
        col = lax.broadcasted_iota(jnp.int32, (span, span), 1)
        s_loc = jnp.where(row >= col, s_loc, NEG_FILL)
        m = jnp.maximum(m, jnp.max(s_loc, axis=1, keepdims=True))
    p_pg = jnp.exp(s_pg - m)
    l = jnp.sum(p_pg, axis=1, keepdims=True)
    acc = jnp.dot(p_pg.astype(jnp.bfloat16), values_p, preferred_element_type=jnp.float32)
    if with_local:
        p_loc = jnp.exp(s_loc - m)
        l = l + jnp.sum(p_loc, axis=1, keepdims=True)
        acc = acc + jnp.dot(p_loc.astype(jnp.bfloat16), vl_ref[...], preferred_element_type=jnp.float32)
    o_ref[...] = (acc / l).astype(o_ref.dtype)
    m_ref[...] = m
    l_ref[...] = l


def attend(key_ok, query_rot, incoming, out_dtype, local=None):
    span, width = query_rot.shape
    head_count = width // HEAD_DIM
    block_count = incoming.shape[0]
    page_size = incoming.shape[2]
    col_spec = pl.BlockSpec((span, HEAD_DIM), lambda h: (0, h))
    page_specs = [
        pl.BlockSpec((block_count, None, page_size, HEAD_DIM), lambda h: (0, 0, 0, h)),
        pl.BlockSpec((block_count, None, page_size, HEAD_DIM), lambda h: (0, 1, 0, h)),
        pl.BlockSpec((1, block_count * page_size), lambda h: (0, 0)),
    ]
    stat_spec = pl.BlockSpec((None, span, 1), lambda h: (h, 0, 0))
    if local is None:
        in_specs = [col_spec] + page_specs
        operands = (query_rot, incoming, incoming, key_ok)
    else:
        in_specs = [col_spec, col_spec, col_spec] + page_specs
        operands = (query_rot, local[0], local[1], incoming, incoming, key_ok)
    return pl.pallas_call(
        partial(attention_kernel, with_local=local is not None),
        grid=(head_count,),
        in_specs=in_specs,
        out_specs=[col_spec, stat_spec, stat_spec],
        out_shape=[
            jax.ShapeDtypeStruct((span, width), out_dtype),
            jax.ShapeDtypeStruct((head_count, span, 1), jnp.float32),
            jax.ShapeDtypeStruct((head_count, span, 1), jnp.float32),
        ],
    )(*operands)


def usable_keys(page_table, request, length, source_base, source_count, page_count, page_size):
    row = lax.dynamic_index_in_dim(page_table, request, 0, keepdims=False)
    row_owner = jnp.where(row >= 0, row // page_count, -1)
    sources = source_base + jnp.arange(source_count, dtype=jnp.int32)
    slot_ids = jnp.arange(row.shape[0], dtype=jnp.int32)
    matches = row_owner[None, :] == sources[:, None]
    present = jnp.any(matches, axis=1)
    slot_of = jnp.sum(jnp.where(matches, slot_ids[None, :], 0), axis=1)
    nvalid = jnp.where(present, jnp.clip(length - slot_of * page_size, 0, page_size), 0)
    within = jnp.arange(page_size, dtype=jnp.int32)
    return (within[None, :] < nvalid[:, None]).astype(jnp.int32).reshape(1, source_count * page_size)


def by_rows(stat):
    return jnp.transpose(stat, (1, 0, 2))


def on_device(new_queries, new_keys, new_values, kv_pages, page_table, cache_len, w_out, out_bias):
    half = lax.axis_index("half")
    sub = lax.axis_index("sub")
    sub_count = lax.axis_size("sub")
    tp_index = lax.axis_index("tp")
    tp_count = lax.axis_size("tp")
    own_index = half * sub_count + sub
    partner = (1 - half) * sub_count + sub
    span_len = new_queries.shape[0]
    width = new_queries.shape[1]
    head_count = width // HEAD_DIM
    page_count = kv_pages.shape[0]
    page_size = kv_pages.shape[2]
    out_cols = w_out.shape[1] // tp_count
    swap = [(0, 1), (1, 0)]

    w_recv = []
    for shift in range(1, tp_count):
        target = (tp_index + shift) % tp_count
        piece = lax.dynamic_slice_in_dim(w_out, target * out_cols, out_cols, axis=1)
        perm = [(i, (i + shift) % tp_count) for i in range(tp_count)]
        w_recv.append(lax.ppermute(piece, "tp", perm))
    w_mine = lax.dynamic_slice_in_dim(w_out, tp_index * out_cols, out_cols, axis=1)

    owners = jnp.where(page_table >= 0, page_table // page_count, -1)
    held_here = owners == own_index
    local_page = jnp.sum(jnp.where(held_here, page_table - own_index * page_count, 0), axis=1)
    dest = jnp.arange(sub_count, dtype=jnp.int32)
    own_length = lax.dynamic_index_in_dim(cache_len, own_index, 0, keepdims=False)
    partner_length = lax.dynamic_index_in_dim(cache_len, partner, 0, keepdims=False)
    positions = own_length + jnp.arange(span_len, dtype=jnp.int32)
    query_rot = rotate_rows(new_queries, positions)
    partner_query = lax.ppermute(query_rot, "half", swap)

    far_pages = jnp.take(kv_pages, jnp.take(local_page, (1 - half) * sub_count + dest), axis=0, mode="clip")
    far_incoming = lax.all_to_all(far_pages, "sub", split_axis=0, concat_axis=0, tiled=True)
    near_pages = jnp.take(kv_pages, jnp.take(local_page, half * sub_count + dest), axis=0, mode="clip")
    partner_query, near_pages = lax.optimization_barrier((partner_query, near_pages))
    near_incoming = lax.all_to_all(near_pages, "sub", split_axis=0, concat_axis=0, tiled=True)
    key_rot = rotate_rows(new_keys, positions)

    source_base = half * sub_count
    ok_own = usable_keys(page_table, own_index, own_length, source_base, sub_count, page_count, page_size)
    ok_partner = usable_keys(page_table, partner, partner_length, source_base, sub_count, page_count, page_size)

    far_out, far_max, far_sum = attend(ok_partner, partner_query, far_incoming, jnp.bfloat16)
    far_stats = jnp.concatenate([far_max, far_sum], axis=2)
    back_out = lax.ppermute(far_out, "half", swap)
    back_stats = lax.ppermute(far_stats, "half", swap)
    near_out, near_max, near_sum = attend(
        ok_own, query_rot, near_incoming, jnp.float32, local=(key_rot, new_values)
    )

    near_max = by_rows(near_max)
    near_sum = by_rows(near_sum)
    back_stats = by_rows(back_stats)
    back_max = back_stats[:, :, 0:1]
    back_sum = back_stats[:, :, 1:2]
    peak = jnp.maximum(near_max, back_max)
    near_w = jnp.exp(near_max - peak) * near_sum
    back_w = jnp.exp(back_max - peak) * back_sum
    near3 = near_out.reshape(span_len, head_count, HEAD_DIM)
    back3 = back_out.astype(jnp.float32).reshape(span_len, head_count, HEAD_DIM)
    merged = (near3 * near_w + back3 * back_w) / (near_w + back_w)
    attended = merged.reshape(span_len, width).astype(jnp.bfloat16)

    summed = jnp.dot(attended, w_mine, preferred_element_type=jnp.float32)
    for shift in range(1, tp_count):
        perm = [(i, (i + shift) % tp_count) for i in range(tp_count)]
        other = lax.ppermute(attended, "tp", perm)
        summed = summed + jnp.dot(other, w_recv[shift - 1], preferred_element_type=jnp.float32)
    return (summed + out_bias.astype(jnp.float32)).astype(jnp.bfloat16)


def solution(mesh):
    req_count = mesh.shape["req"]
    tp_count = mesh.shape["tp"]
    assert tuple(mesh.axis_names) == ("req", "tp")
    devices = mesh.devices.reshape(2, req_count // 2, tp_count)
    split_mesh = jax.sharding.Mesh(devices, ("half", "sub", "tp"))
    rows = ("half", "sub")
    return jax.shard_map(
        on_device,
        mesh=split_mesh,
        in_specs=(
            P(rows, "tp"),
            P(rows, "tp"),
            P(rows, "tp"),
            P(rows, None, None, "tp"),
            P(),
            P(),
            P("tp", None),
            P("tp"),
        ),
        out_specs=P(rows, "tp"),
        check_vma=False,
    )
```

```python
import math
from functools import partial

import jax
import jax.numpy as jnp
from jax import lax
from jax.experimental import pallas as pl
from jax.experimental.pallas import tpu as pltpu
from jax.sharding import PartitionSpec as P

HEAD_DIM = 128
ROT = 32


NEG_FILL = -1e30


def rotate_rows(block, positions):
    row_count = block.shape[0]
    shaped = block.astype(jnp.float32).reshape(row_count, -1, HEAD_DIM)
    half_rot = ROT // 2
    frequency = 10000.0 ** (-2.0 * jnp.arange(half_rot, dtype=jnp.float32) / ROT)
    angles = positions.astype(jnp.float32)[:, None] * frequency[None, :]
    cosine = jnp.cos(angles)[:, None, :]
    sines = jnp.sin(angles)[:, None, :]
    first_half = shaped[:, :, :half_rot]
    second_half = shaped[:, :, half_rot:ROT]
    turned = jnp.concatenate(
        [
            first_half * cosine - second_half * sines,
            second_half * cosine + first_half * sines,
            shaped[:, :, ROT:],
        ],
        axis=2,
    )
    return turned.reshape(row_count, -1).astype(jnp.bfloat16)


def attention_kernel(*refs, with_local):
    if with_local:
        q_ref, kl_ref, vl_ref, kp_ref, vp_ref, ok_ref, bo_ref, bst_ref, o_ref = refs
    else:
        q_ref, kp_ref, vp_ref, ok_ref, o_ref, st_ref = refs
    score_scale = 1.0 / math.sqrt(HEAD_DIM)
    dims = (((1,), (1,)), ((), ()))
    q = q_ref[...]
    span = q.shape[0]
    block_count, page_size, _ = kp_ref.shape
    keys_p = kp_ref[...].reshape(block_count * page_size, HEAD_DIM)
    values_p = vp_ref[...].reshape(block_count * page_size, HEAD_DIM)

    s_pg = lax.dot_general(q, keys_p, dims, preferred_element_type=jnp.float32) * score_scale
    s_pg = jnp.where(ok_ref[...] > 0, s_pg, NEG_FILL)
    m = jnp.max(s_pg, axis=1, keepdims=True)
    if with_local:
        s_loc = lax.dot_general(q, kl_ref[...], dims, preferred_element_type=jnp.float32) * score_scale
        row = lax.broadcasted_iota(jnp.int32, (span, span), 0)
        col = lax.broadcasted_iota(jnp.int32, (span, span), 1)
        s_loc = jnp.where(row >= col, s_loc, NEG_FILL)
        m = jnp.maximum(m, jnp.max(s_loc, axis=1, keepdims=True))
    p_pg = jnp.exp(s_pg - m)
    l = jnp.sum(p_pg, axis=1, keepdims=True)
    acc = jnp.dot(p_pg.astype(jnp.bfloat16), values_p, preferred_element_type=jnp.float32)
    if with_local:
        p_loc = jnp.exp(s_loc - m)
        l = l + jnp.sum(p_loc, axis=1, keepdims=True)
        acc = acc + jnp.dot(p_loc.astype(jnp.bfloat16), vl_ref[...], preferred_element_type=jnp.float32)
        stats = bst_ref[...]
        back_max = stats[:, 0:1]
        back_sum = stats[:, 1:2]
        peak = jnp.maximum(m, back_max)
        near_w = jnp.exp(m - peak)
        back_w = jnp.exp(back_max - peak) * back_sum
        merged = acc * near_w + bo_ref[...].astype(jnp.float32) * back_w
        o_ref[...] = (merged / (l * near_w + back_w)).astype(o_ref.dtype)
    else:
        o_ref[...] = (acc / l).astype(o_ref.dtype)
        st_ref[:, 0:1] = m
        st_ref[:, 1:2] = l


def attend(key_ok, query_rot, incoming, local=None, back=None):
    span, width = query_rot.shape
    head_count = width // HEAD_DIM
    block_count = incoming.shape[0]
    page_size = incoming.shape[2]
    col_spec = pl.BlockSpec((span, HEAD_DIM), lambda h: (0, h))
    page_specs = [
        pl.BlockSpec((block_count, None, page_size, HEAD_DIM), lambda h: (0, 0, 0, h)),
        pl.BlockSpec((block_count, None, page_size, HEAD_DIM), lambda h: (0, 1, 0, h)),
        pl.BlockSpec((1, block_count * page_size), lambda h: (0, 0)),
    ]
    stat_spec = pl.BlockSpec((None, span, 2), lambda h: (h, 0, 0))
    out_shape = jax.ShapeDtypeStruct((span, width), jnp.bfloat16)
    if local is None:
        in_specs = [col_spec] + page_specs
        operands = (query_rot, incoming, incoming, key_ok)
        out_specs = [col_spec, stat_spec]
        out_shape = [out_shape, jax.ShapeDtypeStruct((head_count, span, 2), jnp.float32)]
    else:
        in_specs = [col_spec, col_spec, col_spec] + page_specs + [col_spec, stat_spec]
        operands = (query_rot, local[0], local[1], incoming, incoming, key_ok, back[0], back[1])
        out_specs = col_spec
    return pl.pallas_call(
        partial(attention_kernel, with_local=local is not None),
        grid=(head_count,),
        in_specs=in_specs,
        out_specs=out_specs,
        out_shape=out_shape,
    )(*operands)


def usable_keys(page_table, request, length, source_base, source_count, page_count, page_size):
    row = lax.dynamic_index_in_dim(page_table, request, 0, keepdims=False)
    row_owner = jnp.where(row >= 0, row // page_count, -1)
    sources = source_base + jnp.arange(source_count, dtype=jnp.int32)
    slot_ids = jnp.arange(row.shape[0], dtype=jnp.int32)
    matches = row_owner[None, :] == sources[:, None]
    present = jnp.any(matches, axis=1)
    slot_of = jnp.sum(jnp.where(matches, slot_ids[None, :], 0), axis=1)
    nvalid = jnp.where(present, jnp.clip(length - slot_of * page_size, 0, page_size), 0)
    within = jnp.arange(page_size, dtype=jnp.int32)
    return (within[None, :] < nvalid[:, None]).astype(jnp.int32).reshape(1, source_count * page_size)


def on_device(new_queries, new_keys, new_values, kv_pages, page_table, cache_len, w_out, out_bias):
    half = lax.axis_index("half")
    sub = lax.axis_index("sub")
    sub_count = lax.axis_size("sub")
    tp_index = lax.axis_index("tp")
    tp_count = lax.axis_size("tp")
    own_index = half * sub_count + sub
    partner = (1 - half) * sub_count + sub
    span_len = new_queries.shape[0]
    width = new_queries.shape[1]
    head_count = width // HEAD_DIM
    page_count = kv_pages.shape[0]
    page_size = kv_pages.shape[2]
    out_cols = w_out.shape[1] // tp_count
    swap = [(0, 1), (1, 0)]

    w_recv = []
    for shift in range(1, tp_count):
        target = (tp_index + shift) % tp_count
        piece = lax.dynamic_slice_in_dim(w_out, target * out_cols, out_cols, axis=1)
        perm = [(i, (i + shift) % tp_count) for i in range(tp_count)]
        w_recv.append(lax.ppermute(piece, "tp", perm))
    w_mine = lax.dynamic_slice_in_dim(w_out, tp_index * out_cols, out_cols, axis=1)

    owners = jnp.where(page_table >= 0, page_table // page_count, -1)
    held_here = owners == own_index
    local_page = jnp.sum(jnp.where(held_here, page_table - own_index * page_count, 0), axis=1)
    dest = jnp.arange(sub_count, dtype=jnp.int32)
    own_length = lax.dynamic_index_in_dim(cache_len, own_index, 0, keepdims=False)
    partner_length = lax.dynamic_index_in_dim(cache_len, partner, 0, keepdims=False)
    positions = own_length + jnp.arange(span_len, dtype=jnp.int32)
    query_rot = rotate_rows(new_queries, positions)
    partner_query = lax.ppermute(query_rot, "half", swap)

    far_pages = jnp.take(kv_pages, jnp.take(local_page, (1 - half) * sub_count + dest), axis=0, mode="clip")
    far_incoming = lax.all_to_all(far_pages, "sub", split_axis=0, concat_axis=0, tiled=True)
    near_pages = jnp.take(kv_pages, jnp.take(local_page, half * sub_count + dest), axis=0, mode="clip")
    partner_query, near_pages = lax.optimization_barrier((partner_query, near_pages))
    near_incoming = lax.all_to_all(near_pages, "sub", split_axis=0, concat_axis=0, tiled=True)
    key_rot = rotate_rows(new_keys, positions)

    source_base = half * sub_count
    ok_own = usable_keys(page_table, own_index, own_length, source_base, sub_count, page_count, page_size)
    ok_partner = usable_keys(page_table, partner, partner_length, source_base, sub_count, page_count, page_size)

    far_out, far_stats = attend(ok_partner, partner_query, far_incoming)
    back_out = lax.ppermute(far_out, "half", swap)
    back_stats = lax.ppermute(far_stats, "half", swap)
    attended = attend(
        ok_own, query_rot, near_incoming, local=(key_rot, new_values), back=(back_out, back_stats)
    )

    summed = jnp.dot(attended, w_mine, preferred_element_type=jnp.float32)
    for shift in range(1, tp_count):
        perm = [(i, (i + shift) % tp_count) for i in range(tp_count)]
        other = lax.ppermute(attended, "tp", perm)
        summed = summed + jnp.dot(other, w_recv[shift - 1], preferred_element_type=jnp.float32)
    return (summed + out_bias.astype(jnp.float32)).astype(jnp.bfloat16)


def solution(mesh):
    req_count = mesh.shape["req"]
    tp_count = mesh.shape["tp"]
    assert tuple(mesh.axis_names) == ("req", "tp")
    devices = mesh.devices.reshape(2, req_count // 2, tp_count)
    split_mesh = jax.sharding.Mesh(devices, ("half", "sub", "tp"))
    rows = ("half", "sub")
    return jax.shard_map(
        on_device,
        mesh=split_mesh,
        in_specs=(
            P(rows, "tp"),
            P(rows, "tp"),
            P(rows, "tp"),
            P(rows, None, None, "tp"),
            P(),
            P(),
            P("tp", None),
            P("tp"),
        ),
        out_specs=P(rows, "tp"),
        check_vma=False,
    )
```

```python
import math
from functools import partial

import jax
import jax.numpy as jnp
from jax import lax
from jax.experimental import pallas as pl
from jax.experimental.pallas import tpu as pltpu
from jax.sharding import PartitionSpec as P

HEAD_DIM = 128
ROT = 32


NEG_FILL = -1e30


def rotate_rows(block, positions):
    row_count = block.shape[0]
    shaped = block.astype(jnp.float32).reshape(row_count, -1, HEAD_DIM)
    half_rot = ROT // 2
    frequency = 10000.0 ** (-2.0 * jnp.arange(half_rot, dtype=jnp.float32) / ROT)
    angles = positions.astype(jnp.float32)[:, None] * frequency[None, :]
    cosine = jnp.cos(angles)[:, None, :]
    sines = jnp.sin(angles)[:, None, :]
    first_half = shaped[:, :, :half_rot]
    second_half = shaped[:, :, half_rot:ROT]
    turned = jnp.concatenate(
        [
            first_half * cosine - second_half * sines,
            second_half * cosine + first_half * sines,
            shaped[:, :, ROT:],
        ],
        axis=2,
    )
    return turned.reshape(row_count, -1).astype(jnp.bfloat16)


SCORE_DIMS = (((1,), (1,)), ((), ()))


def page_partial(q, kp_ref, vp_ref, ok_ref):
    score_scale = 1.0 / math.sqrt(HEAD_DIM)
    block_count, page_size, _ = kp_ref.shape
    keys_p = kp_ref[...].reshape(block_count * page_size, HEAD_DIM)
    values_p = vp_ref[...].reshape(block_count * page_size, HEAD_DIM)
    s = lax.dot_general(q, keys_p, SCORE_DIMS, preferred_element_type=jnp.float32) * score_scale
    s = jnp.where(ok_ref[...] > 0, s, NEG_FILL)
    m = jnp.max(s, axis=1, keepdims=True)
    p = jnp.exp(s - m)
    l = jnp.sum(p, axis=1, keepdims=True)
    acc = jnp.dot(p.astype(jnp.bfloat16), values_p, preferred_element_type=jnp.float32)
    return m, l, acc


def local_kernel(q_ref, kl_ref, vl_ref, acc_ref, st_ref):
    score_scale = 1.0 / math.sqrt(HEAD_DIM)
    q = q_ref[...]
    span = q.shape[0]
    s = lax.dot_general(q, kl_ref[...], SCORE_DIMS, preferred_element_type=jnp.float32) * score_scale
    row = lax.broadcasted_iota(jnp.int32, (span, span), 0)
    col = lax.broadcasted_iota(jnp.int32, (span, span), 1)
    s = jnp.where(row >= col, s, NEG_FILL)
    m = jnp.max(s, axis=1, keepdims=True)
    p = jnp.exp(s - m)
    acc_ref[...] = jnp.dot(p.astype(jnp.bfloat16), vl_ref[...], preferred_element_type=jnp.float32)
    st_ref[:, 0:1] = m
    st_ref[:, 1:2] = jnp.sum(p, axis=1, keepdims=True)


def far_kernel(q_ref, kp_ref, vp_ref, ok_ref, o_ref, st_ref):
    m, l, acc = page_partial(q_ref[...], kp_ref, vp_ref, ok_ref)
    o_ref[...] = (acc / l).astype(o_ref.dtype)
    st_ref[:, 0:1] = m
    st_ref[:, 1:2] = l


def near_kernel(q_ref, kp_ref, vp_ref, ok_ref, la_ref, lst_ref, bo_ref, bst_ref, o_ref):
    m, l, acc = page_partial(q_ref[...], kp_ref, vp_ref, ok_ref)
    local = lst_ref[...]
    local_max = local[:, 0:1]
    local_sum = local[:, 1:2]
    back = bst_ref[...]
    back_max = back[:, 0:1]
    back_sum = back[:, 1:2]
    peak = jnp.maximum(jnp.maximum(m, local_max), back_max)
    page_w = jnp.exp(m - peak)
    local_w = jnp.exp(local_max - peak)
    back_w = jnp.exp(back_max - peak) * back_sum
    merged = acc * page_w + la_ref[...] * local_w + bo_ref[...].astype(jnp.float32) * back_w
    total = l * page_w + local_sum * local_w + back_w
    o_ref[...] = (merged / total).astype(o_ref.dtype)


def head_specs(span, block_count, page_size):
    col_spec = pl.BlockSpec((span, HEAD_DIM), lambda h: (0, h))
    stat_spec = pl.BlockSpec((None, span, 2), lambda h: (h, 0, 0))
    page_specs = [
        pl.BlockSpec((block_count, None, page_size, HEAD_DIM), lambda h: (0, 0, 0, h)),
        pl.BlockSpec((block_count, None, page_size, HEAD_DIM), lambda h: (0, 1, 0, h)),
        pl.BlockSpec((1, block_count * page_size), lambda h: (0, 0)),
    ]
    return col_spec, stat_spec, page_specs


def local_attend(query_rot, key_rot, values):
    span, width = query_rot.shape
    head_count = width // HEAD_DIM
    col_spec, stat_spec, _ = head_specs(span, 1, 1)
    return pl.pallas_call(
        local_kernel,
        grid=(head_count,),
        in_specs=[col_spec, col_spec, col_spec],
        out_specs=[col_spec, stat_spec],
        out_shape=[
            jax.ShapeDtypeStruct((span, width), jnp.float32),
            jax.ShapeDtypeStruct((head_count, span, 2), jnp.float32),
        ],
    )(query_rot, key_rot, values)


def far_attend(key_ok, query_rot, incoming):
    span, width = query_rot.shape
    head_count = width // HEAD_DIM
    col_spec, stat_spec, page_specs = head_specs(span, incoming.shape[0], incoming.shape[2])
    return pl.pallas_call(
        far_kernel,
        grid=(head_count,),
        in_specs=[col_spec] + page_specs,
        out_specs=[col_spec, stat_spec],
        out_shape=[
            jax.ShapeDtypeStruct((span, width), jnp.bfloat16),
            jax.ShapeDtypeStruct((head_count, span, 2), jnp.float32),
        ],
    )(query_rot, incoming, incoming, key_ok)


def near_attend(key_ok, query_rot, incoming, local_acc, local_stats, back_out, back_stats):
    span, width = query_rot.shape
    head_count = width // HEAD_DIM
    col_spec, stat_spec, page_specs = head_specs(span, incoming.shape[0], incoming.shape[2])
    return pl.pallas_call(
        near_kernel,
        grid=(head_count,),
        in_specs=[col_spec] + page_specs + [col_spec, stat_spec, col_spec, stat_spec],
        out_specs=col_spec,
        out_shape=jax.ShapeDtypeStruct((span, width), jnp.bfloat16),
    )(query_rot, incoming, incoming, key_ok, local_acc, local_stats, back_out, back_stats)


def usable_keys(page_table, request, length, source_base, source_count, page_count, page_size):
    row = lax.dynamic_index_in_dim(page_table, request, 0, keepdims=False)
    row_owner = jnp.where(row >= 0, row // page_count, -1)
    sources = source_base + jnp.arange(source_count, dtype=jnp.int32)
    slot_ids = jnp.arange(row.shape[0], dtype=jnp.int32)
    matches = row_owner[None, :] == sources[:, None]
    present = jnp.any(matches, axis=1)
    slot_of = jnp.sum(jnp.where(matches, slot_ids[None, :], 0), axis=1)
    nvalid = jnp.where(present, jnp.clip(length - slot_of * page_size, 0, page_size), 0)
    within = jnp.arange(page_size, dtype=jnp.int32)
    return (within[None, :] < nvalid[:, None]).astype(jnp.int32).reshape(1, source_count * page_size)


def on_device(new_queries, new_keys, new_values, kv_pages, page_table, cache_len, w_out, out_bias):
    half = lax.axis_index("half")
    sub = lax.axis_index("sub")
    sub_count = lax.axis_size("sub")
    tp_index = lax.axis_index("tp")
    tp_count = lax.axis_size("tp")
    own_index = half * sub_count + sub
    partner = (1 - half) * sub_count + sub
    span_len = new_queries.shape[0]
    width = new_queries.shape[1]
    head_count = width // HEAD_DIM
    page_count = kv_pages.shape[0]
    page_size = kv_pages.shape[2]
    out_cols = w_out.shape[1] // tp_count
    swap = [(0, 1), (1, 0)]

    w_recv = []
    for shift in range(1, tp_count):
        target = (tp_index + shift) % tp_count
        piece = lax.dynamic_slice_in_dim(w_out, target * out_cols, out_cols, axis=1)
        perm = [(i, (i + shift) % tp_count) for i in range(tp_count)]
        w_recv.append(lax.ppermute(piece, "tp", perm))
    w_mine = lax.dynamic_slice_in_dim(w_out, tp_index * out_cols, out_cols, axis=1)

    owners = jnp.where(page_table >= 0, page_table // page_count, -1)
    held_here = owners == own_index
    local_page = jnp.sum(jnp.where(held_here, page_table - own_index * page_count, 0), axis=1)
    dest = jnp.arange(sub_count, dtype=jnp.int32)
    own_length = lax.dynamic_index_in_dim(cache_len, own_index, 0, keepdims=False)
    partner_length = lax.dynamic_index_in_dim(cache_len, partner, 0, keepdims=False)
    positions = own_length + jnp.arange(span_len, dtype=jnp.int32)
    query_rot = rotate_rows(new_queries, positions)
    partner_query = lax.ppermute(query_rot, "half", swap)

    far_pages = jnp.take(kv_pages, jnp.take(local_page, (1 - half) * sub_count + dest), axis=0, mode="clip")
    far_incoming = lax.all_to_all(far_pages, "sub", split_axis=0, concat_axis=0, tiled=True)
    near_pages = jnp.take(kv_pages, jnp.take(local_page, half * sub_count + dest), axis=0, mode="clip")
    partner_query, near_pages = lax.optimization_barrier((partner_query, near_pages))
    near_incoming = lax.all_to_all(near_pages, "sub", split_axis=0, concat_axis=0, tiled=True)
    key_rot = rotate_rows(new_keys, positions)

    source_base = half * sub_count
    ok_own = usable_keys(page_table, own_index, own_length, source_base, sub_count, page_count, page_size)
    ok_partner = usable_keys(page_table, partner, partner_length, source_base, sub_count, page_count, page_size)

    local_acc, local_stats = local_attend(query_rot, key_rot, new_values)
    far_out, far_stats = far_attend(ok_partner, partner_query, far_incoming)
    back_out = lax.ppermute(far_out, "half", swap)
    back_stats = lax.ppermute(far_stats, "half", swap)
    attended = near_attend(
        ok_own, query_rot, near_incoming, local_acc, local_stats, back_out, back_stats
    )

    summed = jnp.dot(attended, w_mine, preferred_element_type=jnp.float32)
    for shift in range(1, tp_count):
        perm = [(i, (i + shift) % tp_count) for i in range(tp_count)]
        other = lax.ppermute(attended, "tp", perm)
        summed = summed + jnp.dot(other, w_recv[shift - 1], preferred_element_type=jnp.float32)
    return (summed + out_bias.astype(jnp.float32)).astype(jnp.bfloat16)


def solution(mesh):
    req_count = mesh.shape["req"]
    tp_count = mesh.shape["tp"]
    assert tuple(mesh.axis_names) == ("req", "tp")
    devices = mesh.devices.reshape(2, req_count // 2, tp_count)
    split_mesh = jax.sharding.Mesh(devices, ("half", "sub", "tp"))
    rows = ("half", "sub")
    return jax.shard_map(
        on_device,
        mesh=split_mesh,
        in_specs=(
            P(rows, "tp"),
            P(rows, "tp"),
            P(rows, "tp"),
            P(rows, None, None, "tp"),
            P(),
            P(),
            P("tp", None),
            P("tp"),
        ),
        out_specs=P(rows, "tp"),
        check_vma=False,
    )
```

```python
import math
from functools import partial

import jax
import jax.numpy as jnp
from jax import lax
from jax.experimental import pallas as pl
from jax.experimental.pallas import tpu as pltpu
from jax.sharding import PartitionSpec as P

HEAD_DIM = 128
ROT = 32


NEG_FILL = -1e30


def rotate_rows(block, positions):
    row_count = block.shape[0]
    shaped = block.astype(jnp.float32).reshape(row_count, -1, HEAD_DIM)
    half_rot = ROT // 2
    frequency = 10000.0 ** (-2.0 * jnp.arange(half_rot, dtype=jnp.float32) / ROT)
    angles = positions.astype(jnp.float32)[:, None] * frequency[None, :]
    cosine = jnp.cos(angles)[:, None, :]
    sines = jnp.sin(angles)[:, None, :]
    first_half = shaped[:, :, :half_rot]
    second_half = shaped[:, :, half_rot:ROT]
    turned = jnp.concatenate(
        [
            first_half * cosine - second_half * sines,
            second_half * cosine + first_half * sines,
            shaped[:, :, ROT:],
        ],
        axis=2,
    )
    return turned.reshape(row_count, -1).astype(jnp.bfloat16)


SCORE_DIMS = (((1,), (1,)), ((), ()))


def page_partial(q, kp_ref, vp_ref, ok_ref):
    score_scale = 1.0 / math.sqrt(HEAD_DIM)
    block_count, page_size, _ = kp_ref.shape
    keys_p = kp_ref[...].reshape(block_count * page_size, HEAD_DIM)
    values_p = vp_ref[...].reshape(block_count * page_size, HEAD_DIM)
    s = lax.dot_general(q, keys_p, SCORE_DIMS, preferred_element_type=jnp.float32) * score_scale
    s = jnp.where(ok_ref[...] > 0, s, NEG_FILL)
    m = jnp.max(s, axis=1, keepdims=True)
    p = jnp.exp(s - m)
    l = jnp.sum(p, axis=1, keepdims=True)
    acc = jnp.dot(p.astype(jnp.bfloat16), values_p, preferred_element_type=jnp.float32)
    return m, l, acc


def local_kernel(q_ref, kl_ref, vl_ref, acc_ref, st_ref):
    score_scale = 1.0 / math.sqrt(HEAD_DIM)
    q = q_ref[...]
    span = q.shape[0]
    s = lax.dot_general(q, kl_ref[...], SCORE_DIMS, preferred_element_type=jnp.float32) * score_scale
    row = lax.broadcasted_iota(jnp.int32, (span, span), 0)
    col = lax.broadcasted_iota(jnp.int32, (span, span), 1)
    s = jnp.where(row >= col, s, NEG_FILL)
    m = jnp.max(s, axis=1, keepdims=True)
    p = jnp.exp(s - m)
    acc_ref[...] = jnp.dot(p.astype(jnp.bfloat16), vl_ref[...], preferred_element_type=jnp.float32)
    st_ref[:, 0:1] = m
    st_ref[:, 1:2] = jnp.sum(p, axis=1, keepdims=True)


def far_kernel(q_ref, kp_ref, vp_ref, ok_ref, o_ref, st_ref):
    m, l, acc = page_partial(q_ref[...], kp_ref, vp_ref, ok_ref)
    o_ref[...] = (acc / l).astype(o_ref.dtype)
    st_ref[:, 0:1] = m
    st_ref[:, 1:2] = l


def near_kernel(q_ref, kp_ref, vp_ref, ok_ref, la_ref, lst_ref, bo_ref, bst_ref, w_ref, o_ref, proj_ref):
    m, l, acc = page_partial(q_ref[...], kp_ref, vp_ref, ok_ref)
    local = lst_ref[...]
    local_max = local[:, 0:1]
    local_sum = local[:, 1:2]
    back = bst_ref[...]
    back_max = back[:, 0:1]
    back_sum = back[:, 1:2]
    peak = jnp.maximum(jnp.maximum(m, local_max), back_max)
    page_w = jnp.exp(m - peak)
    local_w = jnp.exp(local_max - peak)
    back_w = jnp.exp(back_max - peak) * back_sum
    merged = acc * page_w + la_ref[...] * local_w + bo_ref[...].astype(jnp.float32) * back_w
    total = l * page_w + local_sum * local_w + back_w
    attended = (merged / total).astype(o_ref.dtype)
    o_ref[...] = attended

    @pl.when(pl.program_id(0) == 0)
    def _():
        proj_ref[...] = jnp.zeros_like(proj_ref)

    proj_ref[...] += jnp.dot(attended, w_ref[...], preferred_element_type=jnp.float32)


def head_specs(span, block_count, page_size):
    col_spec = pl.BlockSpec((span, HEAD_DIM), lambda h: (0, h))
    stat_spec = pl.BlockSpec((None, span, 2), lambda h: (h, 0, 0))
    page_specs = [
        pl.BlockSpec((block_count, None, page_size, HEAD_DIM), lambda h: (0, 0, 0, h)),
        pl.BlockSpec((block_count, None, page_size, HEAD_DIM), lambda h: (0, 1, 0, h)),
        pl.BlockSpec((1, block_count * page_size), lambda h: (0, 0)),
    ]
    return col_spec, stat_spec, page_specs


def local_attend(query_rot, key_rot, values):
    span, width = query_rot.shape
    head_count = width // HEAD_DIM
    col_spec, stat_spec, _ = head_specs(span, 1, 1)
    return pl.pallas_call(
        local_kernel,
        grid=(head_count,),
        in_specs=[col_spec, col_spec, col_spec],
        out_specs=[col_spec, stat_spec],
        out_shape=[
            jax.ShapeDtypeStruct((span, width), jnp.float32),
            jax.ShapeDtypeStruct((head_count, span, 2), jnp.float32),
        ],
    )(query_rot, key_rot, values)


def far_attend(key_ok, query_rot, incoming):
    span, width = query_rot.shape
    head_count = width // HEAD_DIM
    col_spec, stat_spec, page_specs = head_specs(span, incoming.shape[0], incoming.shape[2])
    return pl.pallas_call(
        far_kernel,
        grid=(head_count,),
        in_specs=[col_spec] + page_specs,
        out_specs=[col_spec, stat_spec],
        out_shape=[
            jax.ShapeDtypeStruct((span, width), jnp.bfloat16),
            jax.ShapeDtypeStruct((head_count, span, 2), jnp.float32),
        ],
    )(query_rot, incoming, incoming, key_ok)


def near_attend(key_ok, query_rot, incoming, local_acc, local_stats, back_out, back_stats, w_rows):
    span, width = query_rot.shape
    head_count = width // HEAD_DIM
    out_cols = w_rows.shape[1]
    col_spec, stat_spec, page_specs = head_specs(span, incoming.shape[0], incoming.shape[2])
    w_spec = pl.BlockSpec((HEAD_DIM, out_cols), lambda h: (h, 0))
    proj_spec = pl.BlockSpec((span, out_cols), lambda h: (0, 0))
    return pl.pallas_call(
        near_kernel,
        grid=(head_count,),
        in_specs=[col_spec] + page_specs + [col_spec, stat_spec, col_spec, stat_spec, w_spec],
        out_specs=[col_spec, proj_spec],
        out_shape=[
            jax.ShapeDtypeStruct((span, width), jnp.bfloat16),
            jax.ShapeDtypeStruct((span, out_cols), jnp.float32),
        ],
    )(query_rot, incoming, incoming, key_ok, local_acc, local_stats, back_out, back_stats, w_rows)


def usable_keys(page_table, request, length, source_base, source_count, page_count, page_size):
    row = lax.dynamic_index_in_dim(page_table, request, 0, keepdims=False)
    row_owner = jnp.where(row >= 0, row // page_count, -1)
    sources = source_base + jnp.arange(source_count, dtype=jnp.int32)
    slot_ids = jnp.arange(row.shape[0], dtype=jnp.int32)
    matches = row_owner[None, :] == sources[:, None]
    present = jnp.any(matches, axis=1)
    slot_of = jnp.sum(jnp.where(matches, slot_ids[None, :], 0), axis=1)
    nvalid = jnp.where(present, jnp.clip(length - slot_of * page_size, 0, page_size), 0)
    within = jnp.arange(page_size, dtype=jnp.int32)
    return (within[None, :] < nvalid[:, None]).astype(jnp.int32).reshape(1, source_count * page_size)


def on_device(new_queries, new_keys, new_values, kv_pages, page_table, cache_len, w_out, out_bias):
    half = lax.axis_index("half")
    sub = lax.axis_index("sub")
    sub_count = lax.axis_size("sub")
    tp_index = lax.axis_index("tp")
    tp_count = lax.axis_size("tp")
    own_index = half * sub_count + sub
    partner = (1 - half) * sub_count + sub
    span_len = new_queries.shape[0]
    width = new_queries.shape[1]
    head_count = width // HEAD_DIM
    page_count = kv_pages.shape[0]
    page_size = kv_pages.shape[2]
    out_cols = w_out.shape[1] // tp_count
    swap = [(0, 1), (1, 0)]

    w_recv = []
    for shift in range(1, tp_count):
        target = (tp_index + shift) % tp_count
        piece = lax.dynamic_slice_in_dim(w_out, target * out_cols, out_cols, axis=1)
        perm = [(i, (i + shift) % tp_count) for i in range(tp_count)]
        w_recv.append(lax.ppermute(piece, "tp", perm))
    w_mine = lax.dynamic_slice_in_dim(w_out, tp_index * out_cols, out_cols, axis=1)

    owners = jnp.where(page_table >= 0, page_table // page_count, -1)
    held_here = owners == own_index
    local_page = jnp.sum(jnp.where(held_here, page_table - own_index * page_count, 0), axis=1)
    dest = jnp.arange(sub_count, dtype=jnp.int32)
    own_length = lax.dynamic_index_in_dim(cache_len, own_index, 0, keepdims=False)
    partner_length = lax.dynamic_index_in_dim(cache_len, partner, 0, keepdims=False)
    positions = own_length + jnp.arange(span_len, dtype=jnp.int32)
    query_rot = rotate_rows(new_queries, positions)
    partner_query = lax.ppermute(query_rot, "half", swap)

    far_pages = jnp.take(kv_pages, jnp.take(local_page, (1 - half) * sub_count + dest), axis=0, mode="clip")
    far_incoming = lax.all_to_all(far_pages, "sub", split_axis=0, concat_axis=0, tiled=True)
    near_pages = jnp.take(kv_pages, jnp.take(local_page, half * sub_count + dest), axis=0, mode="clip")
    partner_query, near_pages = lax.optimization_barrier((partner_query, near_pages))
    near_incoming = lax.all_to_all(near_pages, "sub", split_axis=0, concat_axis=0, tiled=True)
    key_rot = rotate_rows(new_keys, positions)

    source_base = half * sub_count
    ok_own = usable_keys(page_table, own_index, own_length, source_base, sub_count, page_count, page_size)
    ok_partner = usable_keys(page_table, partner, partner_length, source_base, sub_count, page_count, page_size)

    local_acc, local_stats = local_attend(query_rot, key_rot, new_values)
    far_out, far_stats = far_attend(ok_partner, partner_query, far_incoming)
    back_out = lax.ppermute(far_out, "half", swap)
    back_stats = lax.ppermute(far_stats, "half", swap)
    attended, summed = near_attend(
        ok_own, query_rot, near_incoming, local_acc, local_stats, back_out, back_stats, w_mine
    )

    for shift in range(1, tp_count):
        perm = [(i, (i + shift) % tp_count) for i in range(tp_count)]
        other = lax.ppermute(attended, "tp", perm)
        summed = summed + jnp.dot(other, w_recv[shift - 1], preferred_element_type=jnp.float32)
    return (summed + out_bias.astype(jnp.float32)).astype(jnp.bfloat16)


def solution(mesh):
    req_count = mesh.shape["req"]
    tp_count = mesh.shape["tp"]
    assert tuple(mesh.axis_names) == ("req", "tp")
    devices = mesh.devices.reshape(2, req_count // 2, tp_count)
    split_mesh = jax.sharding.Mesh(devices, ("half", "sub", "tp"))
    rows = ("half", "sub")
    return jax.shard_map(
        on_device,
        mesh=split_mesh,
        in_specs=(
            P(rows, "tp"),
            P(rows, "tp"),
            P(rows, "tp"),
            P(rows, None, None, "tp"),
            P(),
            P(),
            P("tp", None),
            P("tp"),
        ),
        out_specs=P(rows, "tp"),
        check_vma=False,
    )
```

```python
import math
from functools import partial

import jax
import jax.numpy as jnp
from jax import lax
from jax.experimental import pallas as pl
from jax.experimental.pallas import tpu as pltpu
from jax.sharding import PartitionSpec as P

HEAD_DIM = 128
ROT = 32


NEG_FILL = -1e30


def rotate_rows(block, positions):
    row_count = block.shape[0]
    shaped = block.astype(jnp.float32).reshape(row_count, -1, HEAD_DIM)
    half_rot = ROT // 2
    frequency = 10000.0 ** (-2.0 * jnp.arange(half_rot, dtype=jnp.float32) / ROT)
    angles = positions.astype(jnp.float32)[:, None] * frequency[None, :]
    cosine = jnp.cos(angles)[:, None, :]
    sines = jnp.sin(angles)[:, None, :]
    first_half = shaped[:, :, :half_rot]
    second_half = shaped[:, :, half_rot:ROT]
    turned = jnp.concatenate(
        [
            first_half * cosine - second_half * sines,
            second_half * cosine + first_half * sines,
            shaped[:, :, ROT:],
        ],
        axis=2,
    )
    return turned.reshape(row_count, -1).astype(jnp.bfloat16)


SCORE_DIMS = (((1,), (1,)), ((), ()))


def page_partial(q, kp_ref, vp_ref, ok_ref):
    score_scale = 1.0 / math.sqrt(HEAD_DIM)
    block_count, page_size, _ = kp_ref.shape
    keys_p = kp_ref[...].reshape(block_count * page_size, HEAD_DIM)
    values_p = vp_ref[...].reshape(block_count * page_size, HEAD_DIM)
    s = lax.dot_general(q, keys_p, SCORE_DIMS, preferred_element_type=jnp.float32) * score_scale
    s = jnp.where(ok_ref[...] > 0, s, NEG_FILL)
    m = jnp.max(s, axis=1, keepdims=True)
    p = jnp.exp(s - m)
    l = jnp.sum(p, axis=1, keepdims=True)
    acc = jnp.dot(p.astype(jnp.bfloat16), values_p, preferred_element_type=jnp.float32)
    return m, l, acc


def local_kernel(q_ref, kl_ref, vl_ref, acc_ref, st_ref):
    score_scale = 1.0 / math.sqrt(HEAD_DIM)
    q = q_ref[...]
    span = q.shape[0]
    s = lax.dot_general(q, kl_ref[...], SCORE_DIMS, preferred_element_type=jnp.float32) * score_scale
    row = lax.broadcasted_iota(jnp.int32, (span, span), 0)
    col = lax.broadcasted_iota(jnp.int32, (span, span), 1)
    s = jnp.where(row >= col, s, NEG_FILL)
    m = jnp.max(s, axis=1, keepdims=True)
    p = jnp.exp(s - m)
    acc_ref[...] = jnp.dot(p.astype(jnp.bfloat16), vl_ref[...], preferred_element_type=jnp.float32)
    st_ref[:, 0:1] = m
    st_ref[:, 1:2] = jnp.sum(p, axis=1, keepdims=True)


def far_kernel(q_ref, kp_ref, vp_ref, ok_ref, o_ref, st_ref):
    m, l, acc = page_partial(q_ref[...], kp_ref, vp_ref, ok_ref)
    o_ref[...] = (acc / l).astype(o_ref.dtype)
    st_ref[:, 0:1] = m
    st_ref[:, 1:2] = l


def near_kernel(q_ref, kp_ref, vp_ref, ok_ref, la_ref, lst_ref, bo_ref, bst_ref, o_ref):
    m, l, acc = page_partial(q_ref[...], kp_ref, vp_ref, ok_ref)
    local = lst_ref[...]
    local_max = local[:, 0:1]
    local_sum = local[:, 1:2]
    back = bst_ref[...]
    back_max = back[:, 0:1]
    back_sum = back[:, 1:2]
    peak = jnp.maximum(jnp.maximum(m, local_max), back_max)
    page_w = jnp.exp(m - peak)
    local_w = jnp.exp(local_max - peak)
    back_w = jnp.exp(back_max - peak) * back_sum
    merged = acc * page_w + la_ref[...] * local_w + bo_ref[...].astype(jnp.float32) * back_w
    total = l * page_w + local_sum * local_w + back_w
    o_ref[...] = (merged / total).astype(o_ref.dtype)


def head_specs(span, block_count, page_size):
    col_spec = pl.BlockSpec((span, HEAD_DIM), lambda h: (0, h))
    stat_spec = pl.BlockSpec((None, span, 2), lambda h: (h, 0, 0))
    page_specs = [
        pl.BlockSpec((block_count, None, page_size, HEAD_DIM), lambda h: (0, 0, 0, h)),
        pl.BlockSpec((block_count, None, page_size, HEAD_DIM), lambda h: (0, 1, 0, h)),
        pl.BlockSpec((1, block_count * page_size), lambda h: (0, 0)),
    ]
    return col_spec, stat_spec, page_specs


def local_attend(query_rot, key_rot, values):
    span, width = query_rot.shape
    head_count = width // HEAD_DIM
    col_spec, stat_spec, _ = head_specs(span, 1, 1)
    return pl.pallas_call(
        local_kernel,
        grid=(head_count,),
        in_specs=[col_spec, col_spec, col_spec],
        out_specs=[col_spec, stat_spec],
        out_shape=[
            jax.ShapeDtypeStruct((span, width), jnp.float32),
            jax.ShapeDtypeStruct((head_count, span, 2), jnp.float32),
        ],
    )(query_rot, key_rot, values)


def far_attend(key_ok, query_rot, incoming):
    span, width = query_rot.shape
    head_count = width // HEAD_DIM
    col_spec, stat_spec, page_specs = head_specs(span, incoming.shape[0], incoming.shape[2])
    return pl.pallas_call(
        far_kernel,
        grid=(head_count,),
        in_specs=[col_spec] + page_specs,
        out_specs=[col_spec, stat_spec],
        out_shape=[
            jax.ShapeDtypeStruct((span, width), jnp.bfloat16),
            jax.ShapeDtypeStruct((head_count, span, 2), jnp.float32),
        ],
    )(query_rot, incoming, incoming, key_ok)


def near_attend(key_ok, query_rot, incoming, local_acc, local_stats, back_out, back_stats):
    span, width = query_rot.shape
    head_count = width // HEAD_DIM
    col_spec, stat_spec, page_specs = head_specs(span, incoming.shape[0], incoming.shape[2])
    return pl.pallas_call(
        near_kernel,
        grid=(head_count,),
        in_specs=[col_spec] + page_specs + [col_spec, stat_spec, col_spec, stat_spec],
        out_specs=col_spec,
        out_shape=jax.ShapeDtypeStruct((span, width), jnp.bfloat16),
    )(query_rot, incoming, incoming, key_ok, local_acc, local_stats, back_out, back_stats)


def projection_kernel(*refs):
    count = (len(refs) - 2) // 2
    total = refs[2 * count][...].astype(jnp.float32)
    for j in range(count):
        total = total + jnp.dot(refs[j][...], refs[count + j][...], preferred_element_type=jnp.float32)
    refs[-1][...] = total.astype(refs[-1].dtype)


def project(parts, weights, bias):
    span, rows = parts[0].shape
    out_cols = weights[0].shape[1]
    block = 512 if out_cols % 512 == 0 else out_cols
    a_spec = pl.BlockSpec((span, rows), lambda c: (0, 0))
    w_spec = pl.BlockSpec((rows, block), lambda c: (0, c))
    b_spec = pl.BlockSpec((1, block), lambda c: (0, c))
    return pl.pallas_call(
        projection_kernel,
        grid=(out_cols // block,),
        in_specs=[a_spec] * len(parts) + [w_spec] * len(weights) + [b_spec],
        out_specs=pl.BlockSpec((span, block), lambda c: (0, c)),
        out_shape=jax.ShapeDtypeStruct((span, out_cols), jnp.bfloat16),
    )(*parts, *weights, bias.reshape(1, out_cols))


def usable_keys(page_table, request, length, source_base, source_count, page_count, page_size):
    row = lax.dynamic_index_in_dim(page_table, request, 0, keepdims=False)
    row_owner = jnp.where(row >= 0, row // page_count, -1)
    sources = source_base + jnp.arange(source_count, dtype=jnp.int32)
    slot_ids = jnp.arange(row.shape[0], dtype=jnp.int32)
    matches = row_owner[None, :] == sources[:, None]
    present = jnp.any(matches, axis=1)
    slot_of = jnp.sum(jnp.where(matches, slot_ids[None, :], 0), axis=1)
    nvalid = jnp.where(present, jnp.clip(length - slot_of * page_size, 0, page_size), 0)
    within = jnp.arange(page_size, dtype=jnp.int32)
    return (within[None, :] < nvalid[:, None]).astype(jnp.int32).reshape(1, source_count * page_size)


def on_device(new_queries, new_keys, new_values, kv_pages, page_table, cache_len, w_out, out_bias):
    half = lax.axis_index("half")
    sub = lax.axis_index("sub")
    sub_count = lax.axis_size("sub")
    tp_index = lax.axis_index("tp")
    tp_count = lax.axis_size("tp")
    own_index = half * sub_count + sub
    partner = (1 - half) * sub_count + sub
    span_len = new_queries.shape[0]
    width = new_queries.shape[1]
    head_count = width // HEAD_DIM
    page_count = kv_pages.shape[0]
    page_size = kv_pages.shape[2]
    out_cols = w_out.shape[1] // tp_count
    swap = [(0, 1), (1, 0)]

    w_recv = []
    for shift in range(1, tp_count):
        target = (tp_index + shift) % tp_count
        piece = lax.dynamic_slice_in_dim(w_out, target * out_cols, out_cols, axis=1)
        perm = [(i, (i + shift) % tp_count) for i in range(tp_count)]
        w_recv.append(lax.ppermute(piece, "tp", perm))
    w_mine = lax.dynamic_slice_in_dim(w_out, tp_index * out_cols, out_cols, axis=1)

    owners = jnp.where(page_table >= 0, page_table // page_count, -1)
    held_here = owners == own_index
    local_page = jnp.sum(jnp.where(held_here, page_table - own_index * page_count, 0), axis=1)
    dest = jnp.arange(sub_count, dtype=jnp.int32)
    own_length = lax.dynamic_index_in_dim(cache_len, own_index, 0, keepdims=False)
    partner_length = lax.dynamic_index_in_dim(cache_len, partner, 0, keepdims=False)
    positions = own_length + jnp.arange(span_len, dtype=jnp.int32)
    query_rot = rotate_rows(new_queries, positions)
    partner_query = lax.ppermute(query_rot, "half", swap)

    far_pages = jnp.take(kv_pages, jnp.take(local_page, (1 - half) * sub_count + dest), axis=0, mode="clip")
    far_incoming = lax.all_to_all(far_pages, "sub", split_axis=0, concat_axis=0, tiled=True)
    near_pages = jnp.take(kv_pages, jnp.take(local_page, half * sub_count + dest), axis=0, mode="clip")
    partner_query, near_pages = lax.optimization_barrier((partner_query, near_pages))
    near_incoming = lax.all_to_all(near_pages, "sub", split_axis=0, concat_axis=0, tiled=True)
    key_rot = rotate_rows(new_keys, positions)

    source_base = half * sub_count
    ok_own = usable_keys(page_table, own_index, own_length, source_base, sub_count, page_count, page_size)
    ok_partner = usable_keys(page_table, partner, partner_length, source_base, sub_count, page_count, page_size)

    local_acc, local_stats = local_attend(query_rot, key_rot, new_values)
    far_out, far_stats = far_attend(ok_partner, partner_query, far_incoming)
    back_out = lax.ppermute(far_out, "half", swap)
    back_stats = lax.ppermute(far_stats, "half", swap)
    attended = near_attend(
        ok_own, query_rot, near_incoming, local_acc, local_stats, back_out, back_stats
    )

    parts = [attended]
    for shift in range(1, tp_count):
        perm = [(i, (i + shift) % tp_count) for i in range(tp_count)]
        parts.append(lax.ppermute(attended, "tp", perm))
    return project(parts, [w_mine] + w_recv, out_bias)


def solution(mesh):
    req_count = mesh.shape["req"]
    tp_count = mesh.shape["tp"]
    assert tuple(mesh.axis_names) == ("req", "tp")
    devices = mesh.devices.reshape(2, req_count // 2, tp_count)
    split_mesh = jax.sharding.Mesh(devices, ("half", "sub", "tp"))
    rows = ("half", "sub")
    return jax.shard_map(
        on_device,
        mesh=split_mesh,
        in_specs=(
            P(rows, "tp"),
            P(rows, "tp"),
            P(rows, "tp"),
            P(rows, None, None, "tp"),
            P(),
            P(),
            P("tp", None),
            P("tp"),
        ),
        out_specs=P(rows, "tp"),
        check_vma=False,
    )
```

```python
import math
from functools import partial

import jax
import jax.numpy as jnp
from jax import lax
from jax.experimental import pallas as pl
from jax.experimental.pallas import tpu as pltpu
from jax.sharding import PartitionSpec as P

HEAD_DIM = 128
ROT = 32


NEG_FILL = -1e30


def rotate_rows(block, positions):
    row_count = block.shape[0]
    shaped = block.astype(jnp.float32).reshape(row_count, -1, HEAD_DIM)
    half_rot = ROT // 2
    frequency = 10000.0 ** (-2.0 * jnp.arange(half_rot, dtype=jnp.float32) / ROT)
    angles = positions.astype(jnp.float32)[:, None] * frequency[None, :]
    cosine = jnp.cos(angles)[:, None, :]
    sines = jnp.sin(angles)[:, None, :]
    first_half = shaped[:, :, :half_rot]
    second_half = shaped[:, :, half_rot:ROT]
    turned = jnp.concatenate(
        [
            first_half * cosine - second_half * sines,
            second_half * cosine + first_half * sines,
            shaped[:, :, ROT:],
        ],
        axis=2,
    )
    return turned.reshape(row_count, -1).astype(jnp.bfloat16)


SCORE_DIMS = (((1,), (1,)), ((), ()))


def head_cols(ref, g):
    return ref[..., g * HEAD_DIM:(g + 1) * HEAD_DIM]


def local_kernel(q_ref, kl_ref, vl_ref, acc_ref, st_ref):
    score_scale = 1.0 / math.sqrt(HEAD_DIM)
    for g in range(st_ref.shape[0]):
        q = head_cols(q_ref, g)
        span = q.shape[0]
        s = lax.dot_general(q, head_cols(kl_ref, g), SCORE_DIMS, preferred_element_type=jnp.float32) * score_scale
        row = lax.broadcasted_iota(jnp.int32, (span, span), 0)
        col = lax.broadcasted_iota(jnp.int32, (span, span), 1)
        s = jnp.where(row >= col, s, NEG_FILL)
        m = jnp.max(s, axis=1, keepdims=True)
        p = jnp.exp(s - m)
        acc_ref[:, g * HEAD_DIM:(g + 1) * HEAD_DIM] = jnp.dot(
            p.astype(jnp.bfloat16), head_cols(vl_ref, g), preferred_element_type=jnp.float32
        )
        st_ref[g, :, 0:1] = m
        st_ref[g, :, 1:2] = jnp.sum(p, axis=1, keepdims=True)


def head_pages(kp_ref, vp_ref, g):
    block_count, page_size, _ = kp_ref.shape
    keys = head_cols(kp_ref, g).reshape(block_count * page_size, HEAD_DIM)
    values = head_cols(vp_ref, g).reshape(block_count * page_size, HEAD_DIM)
    return keys, values


def page_partial(q, keys_p, values_p, ok):
    score_scale = 1.0 / math.sqrt(HEAD_DIM)
    s = lax.dot_general(q, keys_p, SCORE_DIMS, preferred_element_type=jnp.float32) * score_scale
    s = jnp.where(ok > 0, s, NEG_FILL)
    m = jnp.max(s, axis=1, keepdims=True)
    p = jnp.exp(s - m)
    l = jnp.sum(p, axis=1, keepdims=True)
    acc = jnp.dot(p.astype(jnp.bfloat16), values_p, preferred_element_type=jnp.float32)
    return m, l, acc


def far_kernel(q_ref, kp_ref, vp_ref, ok_ref, o_ref, st_ref):
    ok = ok_ref[...]
    for g in range(st_ref.shape[0]):
        keys, values = head_pages(kp_ref, vp_ref, g)
        m, l, acc = page_partial(head_cols(q_ref, g), keys, values, ok)
        o_ref[:, g * HEAD_DIM:(g + 1) * HEAD_DIM] = (acc / l).astype(o_ref.dtype)
        st_ref[g, :, 0:1] = m
        st_ref[g, :, 1:2] = l


def near_kernel(q_ref, kp_ref, vp_ref, ok_ref, la_ref, lst_ref, bo_ref, bst_ref, o_ref):
    ok = ok_ref[...]
    for g in range(lst_ref.shape[0]):
        keys, values = head_pages(kp_ref, vp_ref, g)
        m, l, acc = page_partial(head_cols(q_ref, g), keys, values, ok)
        local = lst_ref[g]
        local_max = local[:, 0:1]
        local_sum = local[:, 1:2]
        back = bst_ref[g]
        back_max = back[:, 0:1]
        back_sum = back[:, 1:2]
        peak = jnp.maximum(jnp.maximum(m, local_max), back_max)
        page_w = jnp.exp(m - peak)
        local_w = jnp.exp(local_max - peak)
        back_w = jnp.exp(back_max - peak) * back_sum
        merged = (
            acc * page_w
            + head_cols(la_ref, g) * local_w
            + head_cols(bo_ref, g).astype(jnp.float32) * back_w
        )
        total = l * page_w + local_sum * local_w + back_w
        o_ref[:, g * HEAD_DIM:(g + 1) * HEAD_DIM] = (merged / total).astype(o_ref.dtype)


def heads_per_step(head_count):
    return 2 if head_count % 2 == 0 else 1


def head_specs(span, block_count, page_size, group):
    cols = group * HEAD_DIM
    col_spec = pl.BlockSpec((span, cols), lambda h: (0, h))
    stat_spec = pl.BlockSpec((group, span, 2), lambda h: (h, 0, 0))
    page_specs = [
        pl.BlockSpec((block_count, None, page_size, cols), lambda h: (0, 0, 0, h)),
        pl.BlockSpec((block_count, None, page_size, cols), lambda h: (0, 1, 0, h)),
        pl.BlockSpec((1, block_count * page_size), lambda h: (0, 0)),
    ]
    return col_spec, stat_spec, page_specs


def local_attend(query_rot, key_rot, values):
    span, width = query_rot.shape
    head_count = width // HEAD_DIM
    group = heads_per_step(head_count)
    col_spec, stat_spec, _ = head_specs(span, 1, 1, group)
    return pl.pallas_call(
        local_kernel,
        grid=(head_count // group,),
        in_specs=[col_spec, col_spec, col_spec],
        out_specs=[col_spec, stat_spec],
        out_shape=[
            jax.ShapeDtypeStruct((span, width), jnp.float32),
            jax.ShapeDtypeStruct((head_count, span, 2), jnp.float32),
        ],
    )(query_rot, key_rot, values)


def far_attend(key_ok, query_rot, incoming):
    span, width = query_rot.shape
    head_count = width // HEAD_DIM
    group = heads_per_step(head_count)
    col_spec, stat_spec, page_specs = head_specs(span, incoming.shape[0], incoming.shape[2], group)
    return pl.pallas_call(
        far_kernel,
        grid=(head_count // group,),
        in_specs=[col_spec] + page_specs,
        out_specs=[col_spec, stat_spec],
        out_shape=[
            jax.ShapeDtypeStruct((span, width), jnp.bfloat16),
            jax.ShapeDtypeStruct((head_count, span, 2), jnp.float32),
        ],
    )(query_rot, incoming, incoming, key_ok)


def near_attend(key_ok, query_rot, incoming, local_acc, local_stats, back_out, back_stats):
    span, width = query_rot.shape
    head_count = width // HEAD_DIM
    group = heads_per_step(head_count)
    col_spec, stat_spec, page_specs = head_specs(span, incoming.shape[0], incoming.shape[2], group)
    return pl.pallas_call(
        near_kernel,
        grid=(head_count // group,),
        in_specs=[col_spec] + page_specs + [col_spec, stat_spec, col_spec, stat_spec],
        out_specs=col_spec,
        out_shape=jax.ShapeDtypeStruct((span, width), jnp.bfloat16),
    )(query_rot, incoming, incoming, key_ok, local_acc, local_stats, back_out, back_stats)


def projection_kernel(*refs):
    count = (len(refs) - 2) // 2
    total = refs[2 * count][...].astype(jnp.float32)
    for j in range(count):
        total = total + jnp.dot(refs[j][...], refs[count + j][...], preferred_element_type=jnp.float32)
    refs[-1][...] = total.astype(refs[-1].dtype)


def project(parts, weights, bias):
    span, rows = parts[0].shape
    out_cols = weights[0].shape[1]
    block = 512 if out_cols % 512 == 0 else out_cols
    a_spec = pl.BlockSpec((span, rows), lambda c: (0, 0))
    w_spec = pl.BlockSpec((rows, block), lambda c: (0, c))
    b_spec = pl.BlockSpec((1, block), lambda c: (0, c))
    return pl.pallas_call(
        projection_kernel,
        grid=(out_cols // block,),
        in_specs=[a_spec] * len(parts) + [w_spec] * len(weights) + [b_spec],
        out_specs=pl.BlockSpec((span, block), lambda c: (0, c)),
        out_shape=jax.ShapeDtypeStruct((span, out_cols), jnp.bfloat16),
    )(*parts, *weights, bias.reshape(1, out_cols))


def usable_keys(page_table, request, length, source_base, source_count, page_count, page_size):
    row = lax.dynamic_index_in_dim(page_table, request, 0, keepdims=False)
    row_owner = jnp.where(row >= 0, row // page_count, -1)
    sources = source_base + jnp.arange(source_count, dtype=jnp.int32)
    slot_ids = jnp.arange(row.shape[0], dtype=jnp.int32)
    matches = row_owner[None, :] == sources[:, None]
    present = jnp.any(matches, axis=1)
    slot_of = jnp.sum(jnp.where(matches, slot_ids[None, :], 0), axis=1)
    nvalid = jnp.where(present, jnp.clip(length - slot_of * page_size, 0, page_size), 0)
    within = jnp.arange(page_size, dtype=jnp.int32)
    return (within[None, :] < nvalid[:, None]).astype(jnp.int32).reshape(1, source_count * page_size)


def on_device(new_queries, new_keys, new_values, kv_pages, page_table, cache_len, w_out, out_bias):
    half = lax.axis_index("half")
    sub = lax.axis_index("sub")
    sub_count = lax.axis_size("sub")
    tp_index = lax.axis_index("tp")
    tp_count = lax.axis_size("tp")
    own_index = half * sub_count + sub
    partner = (1 - half) * sub_count + sub
    span_len = new_queries.shape[0]
    width = new_queries.shape[1]
    head_count = width // HEAD_DIM
    page_count = kv_pages.shape[0]
    page_size = kv_pages.shape[2]
    out_cols = w_out.shape[1] // tp_count
    swap = [(0, 1), (1, 0)]

    w_recv = []
    for shift in range(1, tp_count):
        target = (tp_index + shift) % tp_count
        piece = lax.dynamic_slice_in_dim(w_out, target * out_cols, out_cols, axis=1)
        perm = [(i, (i + shift) % tp_count) for i in range(tp_count)]
        w_recv.append(lax.ppermute(piece, "tp", perm))
    w_mine = lax.dynamic_slice_in_dim(w_out, tp_index * out_cols, out_cols, axis=1)

    owners = jnp.where(page_table >= 0, page_table // page_count, -1)
    held_here = owners == own_index
    local_page = jnp.sum(jnp.where(held_here, page_table - own_index * page_count, 0), axis=1)
    dest = jnp.arange(sub_count, dtype=jnp.int32)
    own_length = lax.dynamic_index_in_dim(cache_len, own_index, 0, keepdims=False)
    partner_length = lax.dynamic_index_in_dim(cache_len, partner, 0, keepdims=False)
    positions = own_length + jnp.arange(span_len, dtype=jnp.int32)
    query_rot = rotate_rows(new_queries, positions)
    partner_query = lax.ppermute(query_rot, "half", swap)

    far_pages = jnp.take(kv_pages, jnp.take(local_page, (1 - half) * sub_count + dest), axis=0, mode="clip")
    far_incoming = lax.all_to_all(far_pages, "sub", split_axis=0, concat_axis=0, tiled=True)
    near_pages = jnp.take(kv_pages, jnp.take(local_page, half * sub_count + dest), axis=0, mode="clip")
    partner_query, near_pages = lax.optimization_barrier((partner_query, near_pages))
    near_incoming = lax.all_to_all(near_pages, "sub", split_axis=0, concat_axis=0, tiled=True)
    key_rot = rotate_rows(new_keys, positions)

    source_base = half * sub_count
    ok_own = usable_keys(page_table, own_index, own_length, source_base, sub_count, page_count, page_size)
    ok_partner = usable_keys(page_table, partner, partner_length, source_base, sub_count, page_count, page_size)

    local_acc, local_stats = local_attend(query_rot, key_rot, new_values)
    far_out, far_stats = far_attend(ok_partner, partner_query, far_incoming)
    back_out = lax.ppermute(far_out, "half", swap)
    back_stats = lax.ppermute(far_stats, "half", swap)
    attended = near_attend(
        ok_own, query_rot, near_incoming, local_acc, local_stats, back_out, back_stats
    )

    parts = [attended]
    for shift in range(1, tp_count):
        perm = [(i, (i + shift) % tp_count) for i in range(tp_count)]
        parts.append(lax.ppermute(attended, "tp", perm))
    return project(parts, [w_mine] + w_recv, out_bias)


def solution(mesh):
    req_count = mesh.shape["req"]
    tp_count = mesh.shape["tp"]
    assert tuple(mesh.axis_names) == ("req", "tp")
    devices = mesh.devices.reshape(2, req_count // 2, tp_count)
    split_mesh = jax.sharding.Mesh(devices, ("half", "sub", "tp"))
    rows = ("half", "sub")
    return jax.shard_map(
        on_device,
        mesh=split_mesh,
        in_specs=(
            P(rows, "tp"),
            P(rows, "tp"),
            P(rows, "tp"),
            P(rows, None, None, "tp"),
            P(),
            P(),
            P("tp", None),
            P("tp"),
        ),
        out_specs=P(rows, "tp"),
        check_vma=False,
    )
```

```python
import math
from functools import partial

import jax
import jax.numpy as jnp
from jax import lax
from jax.experimental import pallas as pl
from jax.experimental.pallas import tpu as pltpu
from jax.sharding import PartitionSpec as P

HEAD_DIM = 128
ROT = 32


NEG_FILL = -1e30


def rotate_rows(block, positions):
    row_count = block.shape[0]
    shaped = block.astype(jnp.float32).reshape(row_count, -1, HEAD_DIM)
    half_rot = ROT // 2
    frequency = 10000.0 ** (-2.0 * jnp.arange(half_rot, dtype=jnp.float32) / ROT)
    angles = positions.astype(jnp.float32)[:, None] * frequency[None, :]
    cosine = jnp.cos(angles)[:, None, :]
    sines = jnp.sin(angles)[:, None, :]
    first_half = shaped[:, :, :half_rot]
    second_half = shaped[:, :, half_rot:ROT]
    turned = jnp.concatenate(
        [
            first_half * cosine - second_half * sines,
            second_half * cosine + first_half * sines,
            shaped[:, :, ROT:],
        ],
        axis=2,
    )
    return turned.reshape(row_count, -1).astype(jnp.bfloat16)


SCORE_DIMS = (((1,), (1,)), ((), ()))


def head_cols(ref, g):
    return ref[..., g * HEAD_DIM:(g + 1) * HEAD_DIM]


def local_kernel(q_ref, kl_ref, vl_ref, acc_ref, st_ref):
    score_scale = 1.0 / math.sqrt(HEAD_DIM)
    for g in range(st_ref.shape[0]):
        q = head_cols(q_ref, g)
        span = q.shape[0]
        s = lax.dot_general(q, head_cols(kl_ref, g), SCORE_DIMS, preferred_element_type=jnp.float32) * score_scale
        row = lax.broadcasted_iota(jnp.int32, (span, span), 0)
        col = lax.broadcasted_iota(jnp.int32, (span, span), 1)
        s = jnp.where(row >= col, s, NEG_FILL)
        m = jnp.max(s, axis=1, keepdims=True)
        p = jnp.exp(s - m)
        acc_ref[:, g * HEAD_DIM:(g + 1) * HEAD_DIM] = jnp.dot(
            p.astype(jnp.bfloat16), head_cols(vl_ref, g), preferred_element_type=jnp.float32
        )
        st_ref[g, :, 0:1] = m
        st_ref[g, :, 1:2] = jnp.sum(p, axis=1, keepdims=True)


def head_pages(kp_ref, vp_ref, g):
    block_count, page_size, _ = kp_ref.shape
    keys = head_cols(kp_ref, g).reshape(block_count * page_size, HEAD_DIM)
    values = head_cols(vp_ref, g).reshape(block_count * page_size, HEAD_DIM)
    return keys, values


def page_partial(q, keys_p, values_p, ok):
    score_scale = 1.0 / math.sqrt(HEAD_DIM)
    s = lax.dot_general(q, keys_p, SCORE_DIMS, preferred_element_type=jnp.float32) * score_scale
    s = jnp.where(ok > 0, s, NEG_FILL)
    m = jnp.max(s, axis=1, keepdims=True)
    p = jnp.exp(s - m)
    l = jnp.sum(p, axis=1, keepdims=True)
    acc = jnp.dot(p.astype(jnp.bfloat16), values_p, preferred_element_type=jnp.float32)
    return m, l, acc


def far_kernel(q_ref, kp_ref, vp_ref, ok_ref, o_ref, st_ref):
    ok = ok_ref[...]
    for g in range(st_ref.shape[0]):
        keys, values = head_pages(kp_ref, vp_ref, g)
        m, l, acc = page_partial(head_cols(q_ref, g), keys, values, ok)
        o_ref[:, g * HEAD_DIM:(g + 1) * HEAD_DIM] = (acc / l).astype(o_ref.dtype)
        st_ref[g, :, 0:1] = m
        st_ref[g, :, 1:2] = l


def near_kernel(q_ref, kp_ref, vp_ref, ok_ref, la_ref, lst_ref, bo_ref, bst_ref, o_ref):
    ok = ok_ref[...]
    for g in range(lst_ref.shape[0]):
        keys, values = head_pages(kp_ref, vp_ref, g)
        m, l, acc = page_partial(head_cols(q_ref, g), keys, values, ok)
        local = lst_ref[g]
        local_max = local[:, 0:1]
        local_sum = local[:, 1:2]
        back = bst_ref[g]
        back_max = back[:, 0:1]
        back_sum = back[:, 1:2]
        peak = jnp.maximum(jnp.maximum(m, local_max), back_max)
        page_w = jnp.exp(m - peak)
        local_w = jnp.exp(local_max - peak)
        back_w = jnp.exp(back_max - peak) * back_sum
        merged = (
            acc * page_w
            + head_cols(la_ref, g) * local_w
            + head_cols(bo_ref, g).astype(jnp.float32) * back_w
        )
        total = l * page_w + local_sum * local_w + back_w
        o_ref[:, g * HEAD_DIM:(g + 1) * HEAD_DIM] = (merged / total).astype(o_ref.dtype)


def heads_per_step(head_count):
    return 2 if head_count % 2 == 0 else 1


def head_specs(span, block_count, page_size, group):
    cols = group * HEAD_DIM
    col_spec = pl.BlockSpec((span, cols), lambda h: (0, h))
    stat_spec = pl.BlockSpec((group, span, 2), lambda h: (h, 0, 0))
    page_specs = [
        pl.BlockSpec((block_count, None, page_size, cols), lambda h: (0, 0, 0, h)),
        pl.BlockSpec((block_count, None, page_size, cols), lambda h: (0, 1, 0, h)),
        pl.BlockSpec((1, block_count * page_size), lambda h: (0, 0)),
    ]
    return col_spec, stat_spec, page_specs


def local_attend(query_rot, key_rot, values):
    span, width = query_rot.shape
    head_count = width // HEAD_DIM
    group = heads_per_step(head_count)
    col_spec, stat_spec, _ = head_specs(span, 1, 1, group)
    return pl.pallas_call(
        local_kernel,
        grid=(head_count // group,),
        in_specs=[col_spec, col_spec, col_spec],
        out_specs=[col_spec, stat_spec],
        out_shape=[
            jax.ShapeDtypeStruct((span, width), jnp.float32),
            jax.ShapeDtypeStruct((head_count, span, 2), jnp.float32),
        ],
    )(query_rot, key_rot, values)


def far_attend(key_ok, query_rot, incoming):
    span, width = query_rot.shape
    head_count = width // HEAD_DIM
    group = heads_per_step(head_count)
    col_spec, stat_spec, page_specs = head_specs(span, incoming.shape[0], incoming.shape[2], group)
    return pl.pallas_call(
        far_kernel,
        grid=(head_count // group,),
        in_specs=[col_spec] + page_specs,
        out_specs=[col_spec, stat_spec],
        out_shape=[
            jax.ShapeDtypeStruct((span, width), jnp.bfloat16),
            jax.ShapeDtypeStruct((head_count, span, 2), jnp.float32),
        ],
    )(query_rot, incoming, incoming, key_ok)


def near_attend(key_ok, query_rot, incoming, local_acc, local_stats, back_out, back_stats, first_head):
    span, width = query_rot.shape
    head_count = incoming.shape[3] // HEAD_DIM
    group = heads_per_step(head_count)
    base = first_head // group
    cols = group * HEAD_DIM
    _, _, page_specs = head_specs(span, incoming.shape[0], incoming.shape[2], group)
    wide_spec = pl.BlockSpec((span, cols), lambda h: (0, h + base))
    wide_stats = pl.BlockSpec((group, span, 2), lambda h: (h + base, 0, 0))
    return pl.pallas_call(
        near_kernel,
        grid=(head_count // group,),
        in_specs=[wide_spec] + page_specs + [wide_spec, wide_stats, wide_spec, wide_stats],
        out_specs=pl.BlockSpec((span, cols), lambda h: (0, h)),
        out_shape=jax.ShapeDtypeStruct((span, head_count * HEAD_DIM), jnp.bfloat16),
    )(query_rot, incoming, incoming, key_ok, local_acc, local_stats, back_out, back_stats)


def projection_kernel(*refs):
    count = (len(refs) - 2) // 2
    total = refs[2 * count][...].astype(jnp.float32)
    for j in range(count):
        total = total + jnp.dot(refs[j][...], refs[count + j][...], preferred_element_type=jnp.float32)
    refs[-1][...] = total.astype(refs[-1].dtype)


def project(parts, weights, bias):
    span, rows = parts[0].shape
    out_cols = weights[0].shape[1]
    block = 512 if out_cols % 512 == 0 else out_cols
    a_spec = pl.BlockSpec((span, rows), lambda c: (0, 0))
    w_spec = pl.BlockSpec((rows, block), lambda c: (0, c))
    b_spec = pl.BlockSpec((1, block), lambda c: (0, c))
    return pl.pallas_call(
        projection_kernel,
        grid=(out_cols // block,),
        in_specs=[a_spec] * len(parts) + [w_spec] * len(weights) + [b_spec],
        out_specs=pl.BlockSpec((span, block), lambda c: (0, c)),
        out_shape=jax.ShapeDtypeStruct((span, out_cols), jnp.bfloat16),
    )(*parts, *weights, bias.reshape(1, out_cols))


def usable_keys(page_table, request, length, source_base, source_count, page_count, page_size):
    row = lax.dynamic_index_in_dim(page_table, request, 0, keepdims=False)
    row_owner = jnp.where(row >= 0, row // page_count, -1)
    sources = source_base + jnp.arange(source_count, dtype=jnp.int32)
    slot_ids = jnp.arange(row.shape[0], dtype=jnp.int32)
    matches = row_owner[None, :] == sources[:, None]
    present = jnp.any(matches, axis=1)
    slot_of = jnp.sum(jnp.where(matches, slot_ids[None, :], 0), axis=1)
    nvalid = jnp.where(present, jnp.clip(length - slot_of * page_size, 0, page_size), 0)
    within = jnp.arange(page_size, dtype=jnp.int32)
    return (within[None, :] < nvalid[:, None]).astype(jnp.int32).reshape(1, source_count * page_size)


def on_device(new_queries, new_keys, new_values, kv_pages, page_table, cache_len, w_out, out_bias):
    half = lax.axis_index("half")
    sub = lax.axis_index("sub")
    sub_count = lax.axis_size("sub")
    tp_index = lax.axis_index("tp")
    tp_count = lax.axis_size("tp")
    own_index = half * sub_count + sub
    partner = (1 - half) * sub_count + sub
    span_len = new_queries.shape[0]
    width = new_queries.shape[1]
    head_count = width // HEAD_DIM
    page_count = kv_pages.shape[0]
    page_size = kv_pages.shape[2]
    out_cols = w_out.shape[1] // tp_count
    swap = [(0, 1), (1, 0)]

    w_recv = []
    for shift in range(1, tp_count):
        target = (tp_index + shift) % tp_count
        piece = lax.dynamic_slice_in_dim(w_out, target * out_cols, out_cols, axis=1)
        perm = [(i, (i + shift) % tp_count) for i in range(tp_count)]
        w_recv.append(lax.ppermute(piece, "tp", perm))
    w_mine = lax.dynamic_slice_in_dim(w_out, tp_index * out_cols, out_cols, axis=1)

    owners = jnp.where(page_table >= 0, page_table // page_count, -1)
    held_here = owners == own_index
    local_page = jnp.sum(jnp.where(held_here, page_table - own_index * page_count, 0), axis=1)
    dest = jnp.arange(sub_count, dtype=jnp.int32)
    own_length = lax.dynamic_index_in_dim(cache_len, own_index, 0, keepdims=False)
    partner_length = lax.dynamic_index_in_dim(cache_len, partner, 0, keepdims=False)
    positions = own_length + jnp.arange(span_len, dtype=jnp.int32)
    query_rot = rotate_rows(new_queries, positions)
    partner_query = lax.ppermute(query_rot, "half", swap)

    far_pages = jnp.take(kv_pages, jnp.take(local_page, (1 - half) * sub_count + dest), axis=0, mode="clip")
    far_incoming = lax.all_to_all(far_pages, "sub", split_axis=0, concat_axis=0, tiled=True)
    near_pages = jnp.take(kv_pages, jnp.take(local_page, half * sub_count + dest), axis=0, mode="clip")
    split_heads = head_count // 2 if head_count % 2 == 0 else head_count
    split_cols = split_heads * HEAD_DIM
    near_first = near_pages[..., :split_cols]
    near_rest = near_pages[..., split_cols:]
    partner_query, near_first = lax.optimization_barrier((partner_query, near_first))
    near_incoming = [lax.all_to_all(near_first, "sub", split_axis=0, concat_axis=0, tiled=True)]
    if split_cols < width:
        near_incoming.append(lax.all_to_all(near_rest, "sub", split_axis=0, concat_axis=0, tiled=True))
    key_rot = rotate_rows(new_keys, positions)

    source_base = half * sub_count
    ok_own = usable_keys(page_table, own_index, own_length, source_base, sub_count, page_count, page_size)
    ok_partner = usable_keys(page_table, partner, partner_length, source_base, sub_count, page_count, page_size)

    local_acc, local_stats = local_attend(query_rot, key_rot, new_values)
    far_out, far_stats = far_attend(ok_partner, partner_query, far_incoming)
    back_out = lax.ppermute(far_out, "half", swap)
    back_stats = lax.ppermute(far_stats, "half", swap)
    attended = [
        near_attend(ok_own, query_rot, part, local_acc, local_stats, back_out, back_stats, index * split_heads)
        for index, part in enumerate(near_incoming)
    ]
    parts = list(attended)
    for shift in range(1, tp_count):
        perm = [(i, (i + shift) % tp_count) for i in range(tp_count)]
        parts.extend(lax.ppermute(piece, "tp", perm) for piece in attended)
    weights = []
    for rows in [w_mine] + w_recv:
        weights.extend(rows[index * split_cols:(index + 1) * split_cols] for index in range(len(attended)))
    return project(parts, weights, out_bias)


def solution(mesh):
    req_count = mesh.shape["req"]
    tp_count = mesh.shape["tp"]
    assert tuple(mesh.axis_names) == ("req", "tp")
    devices = mesh.devices.reshape(2, req_count // 2, tp_count)
    split_mesh = jax.sharding.Mesh(devices, ("half", "sub", "tp"))
    rows = ("half", "sub")
    return jax.shard_map(
        on_device,
        mesh=split_mesh,
        in_specs=(
            P(rows, "tp"),
            P(rows, "tp"),
            P(rows, "tp"),
            P(rows, None, None, "tp"),
            P(),
            P(),
            P("tp", None),
            P("tp"),
        ),
        out_specs=P(rows, "tp"),
        check_vma=False,
    )
```

```python
import math
from functools import partial

import jax
import jax.numpy as jnp
from jax import lax
from jax.experimental import pallas as pl
from jax.experimental.pallas import tpu as pltpu
from jax.sharding import PartitionSpec as P

HEAD_DIM = 128
ROT = 32


NEG_FILL = -1e30


def rotate_rows(block, positions):
    row_count = block.shape[0]
    shaped = block.astype(jnp.float32).reshape(row_count, -1, HEAD_DIM)
    half_rot = ROT // 2
    frequency = 10000.0 ** (-2.0 * jnp.arange(half_rot, dtype=jnp.float32) / ROT)
    angles = positions.astype(jnp.float32)[:, None] * frequency[None, :]
    cosine = jnp.cos(angles)[:, None, :]
    sines = jnp.sin(angles)[:, None, :]
    first_half = shaped[:, :, :half_rot]
    second_half = shaped[:, :, half_rot:ROT]
    turned = jnp.concatenate(
        [
            first_half * cosine - second_half * sines,
            second_half * cosine + first_half * sines,
            shaped[:, :, ROT:],
        ],
        axis=2,
    )
    return turned.reshape(row_count, -1).astype(jnp.bfloat16)


SCORE_DIMS = (((1,), (1,)), ((), ()))


def head_cols(ref, g):
    return ref[..., g * HEAD_DIM:(g + 1) * HEAD_DIM]


def local_kernel(q_ref, kl_ref, vl_ref, acc_ref, st_ref):
    score_scale = 1.0 / math.sqrt(HEAD_DIM)
    for g in range(st_ref.shape[0]):
        q = head_cols(q_ref, g)
        span = q.shape[0]
        s = lax.dot_general(q, head_cols(kl_ref, g), SCORE_DIMS, preferred_element_type=jnp.float32) * score_scale
        row = lax.broadcasted_iota(jnp.int32, (span, span), 0)
        col = lax.broadcasted_iota(jnp.int32, (span, span), 1)
        s = jnp.where(row >= col, s, NEG_FILL)
        m = jnp.max(s, axis=1, keepdims=True)
        p = jnp.exp(s - m)
        acc_ref[:, g * HEAD_DIM:(g + 1) * HEAD_DIM] = jnp.dot(
            p.astype(jnp.bfloat16), head_cols(vl_ref, g), preferred_element_type=jnp.float32
        )
        st_ref[g, :, 0:1] = m
        st_ref[g, :, 1:2] = jnp.sum(p, axis=1, keepdims=True)


def head_pages(kp_ref, vp_ref, g):
    block_count, page_size, _ = kp_ref.shape
    keys = head_cols(kp_ref, g).reshape(block_count * page_size, HEAD_DIM)
    values = head_cols(vp_ref, g).reshape(block_count * page_size, HEAD_DIM)
    return keys, values


def page_partial(q, keys_p, values_p, ok):
    score_scale = 1.0 / math.sqrt(HEAD_DIM)
    s = lax.dot_general(q, keys_p, SCORE_DIMS, preferred_element_type=jnp.float32) * score_scale
    s = jnp.where(ok > 0, s, NEG_FILL)
    m = jnp.max(s, axis=1, keepdims=True)
    p = jnp.exp(s - m)
    l = jnp.sum(p, axis=1, keepdims=True)
    acc = jnp.dot(p.astype(jnp.bfloat16), values_p, preferred_element_type=jnp.float32)
    return m, l, acc


def far_kernel(q_ref, kp_ref, vp_ref, ok_ref, o_ref, st_ref):
    ok = ok_ref[...]
    for g in range(st_ref.shape[0]):
        keys, values = head_pages(kp_ref, vp_ref, g)
        m, l, acc = page_partial(head_cols(q_ref, g), keys, values, ok)
        o_ref[:, g * HEAD_DIM:(g + 1) * HEAD_DIM] = (acc / l).astype(o_ref.dtype)
        st_ref[g, :, 0:1] = m
        st_ref[g, :, 1:2] = l


def near_kernel(q_ref, kp_ref, vp_ref, ok_ref, la_ref, lst_ref, bo_ref, bst_ref, o_ref):
    ok = ok_ref[...]
    for g in range(lst_ref.shape[0]):
        keys, values = head_pages(kp_ref, vp_ref, g)
        m, l, acc = page_partial(head_cols(q_ref, g), keys, values, ok)
        local = lst_ref[g]
        local_max = local[:, 0:1]
        local_sum = local[:, 1:2]
        back = bst_ref[g]
        back_max = back[:, 0:1]
        back_sum = back[:, 1:2]
        peak = jnp.maximum(jnp.maximum(m, local_max), back_max)
        page_w = jnp.exp(m - peak)
        local_w = jnp.exp(local_max - peak)
        back_w = jnp.exp(back_max - peak) * back_sum
        merged = (
            acc * page_w
            + head_cols(la_ref, g) * local_w
            + head_cols(bo_ref, g).astype(jnp.float32) * back_w
        )
        total = l * page_w + local_sum * local_w + back_w
        o_ref[:, g * HEAD_DIM:(g + 1) * HEAD_DIM] = (merged / total).astype(o_ref.dtype)


def heads_per_step(head_count):
    return 2 if head_count % 2 == 0 else 1


def head_specs(span, block_count, page_size, group):
    cols = group * HEAD_DIM
    col_spec = pl.BlockSpec((span, cols), lambda h: (0, h))
    stat_spec = pl.BlockSpec((group, span, 2), lambda h: (h, 0, 0))
    page_specs = [
        pl.BlockSpec((block_count, None, page_size, cols), lambda h: (0, 0, 0, h)),
        pl.BlockSpec((block_count, None, page_size, cols), lambda h: (0, 1, 0, h)),
        pl.BlockSpec((1, block_count * page_size), lambda h: (0, 0)),
    ]
    return col_spec, stat_spec, page_specs


def local_attend(query_rot, key_rot, values):
    span, width = query_rot.shape
    head_count = width // HEAD_DIM
    group = heads_per_step(head_count)
    col_spec, stat_spec, _ = head_specs(span, 1, 1, group)
    return pl.pallas_call(
        local_kernel,
        grid=(head_count // group,),
        in_specs=[col_spec, col_spec, col_spec],
        out_specs=[col_spec, stat_spec],
        out_shape=[
            jax.ShapeDtypeStruct((span, width), jnp.float32),
            jax.ShapeDtypeStruct((head_count, span, 2), jnp.float32),
        ],
    )(query_rot, key_rot, values)


def far_attend(key_ok, query_rot, incoming):
    span, width = query_rot.shape
    head_count = width // HEAD_DIM
    group = heads_per_step(head_count)
    col_spec, stat_spec, page_specs = head_specs(span, incoming.shape[0], incoming.shape[2], group)
    return pl.pallas_call(
        far_kernel,
        grid=(head_count // group,),
        in_specs=[col_spec] + page_specs,
        out_specs=[col_spec, stat_spec],
        out_shape=[
            jax.ShapeDtypeStruct((span, width), jnp.bfloat16),
            jax.ShapeDtypeStruct((head_count, span, 2), jnp.float32),
        ],
    )(query_rot, incoming, incoming, key_ok)


def near_attend(key_ok, query_rot, incoming, local_acc, local_stats, back_out, back_stats):
    span, width = query_rot.shape
    head_count = width // HEAD_DIM
    group = heads_per_step(head_count)
    col_spec, stat_spec, page_specs = head_specs(span, incoming.shape[0], incoming.shape[2], group)
    return pl.pallas_call(
        near_kernel,
        grid=(head_count // group,),
        in_specs=[col_spec] + page_specs + [col_spec, stat_spec, col_spec, stat_spec],
        out_specs=col_spec,
        out_shape=jax.ShapeDtypeStruct((span, width), jnp.bfloat16),
    )(query_rot, incoming, incoming, key_ok, local_acc, local_stats, back_out, back_stats)


def projection_kernel(*refs):
    count = (len(refs) - 2) // 2
    total = refs[2 * count][...].astype(jnp.float32)
    for j in range(count):
        total = total + jnp.dot(refs[j][...], refs[count + j][...], preferred_element_type=jnp.float32)
    refs[-1][...] = total.astype(refs[-1].dtype)


def projection_block(out_cols):
    return 512 if out_cols % 512 == 0 else out_cols


def blocked(w, block):
    rows, cols = w.shape
    return jnp.transpose(w.reshape(rows, cols // block, block), (1, 0, 2))


def project(parts, weights, bias):
    span, rows = parts[0].shape
    block = weights[0].shape[2]
    out_cols = weights[0].shape[0] * block
    a_spec = pl.BlockSpec((span, rows), lambda c: (0, 0))
    w_spec = pl.BlockSpec((None, rows, block), lambda c: (c, 0, 0))
    b_spec = pl.BlockSpec((1, block), lambda c: (0, c))
    return pl.pallas_call(
        projection_kernel,
        grid=(out_cols // block,),
        in_specs=[a_spec] * len(parts) + [w_spec] * len(weights) + [b_spec],
        out_specs=pl.BlockSpec((span, block), lambda c: (0, c)),
        out_shape=jax.ShapeDtypeStruct((span, out_cols), jnp.bfloat16),
    )(*parts, *weights, bias.reshape(1, out_cols))


def usable_keys(page_table, request, length, source_base, source_count, page_count, page_size):
    row = lax.dynamic_index_in_dim(page_table, request, 0, keepdims=False)
    row_owner = jnp.where(row >= 0, row // page_count, -1)
    sources = source_base + jnp.arange(source_count, dtype=jnp.int32)
    slot_ids = jnp.arange(row.shape[0], dtype=jnp.int32)
    matches = row_owner[None, :] == sources[:, None]
    present = jnp.any(matches, axis=1)
    slot_of = jnp.sum(jnp.where(matches, slot_ids[None, :], 0), axis=1)
    nvalid = jnp.where(present, jnp.clip(length - slot_of * page_size, 0, page_size), 0)
    within = jnp.arange(page_size, dtype=jnp.int32)
    return (within[None, :] < nvalid[:, None]).astype(jnp.int32).reshape(1, source_count * page_size)


def on_device(new_queries, new_keys, new_values, kv_pages, page_table, cache_len, w_out, out_bias):
    half = lax.axis_index("half")
    sub = lax.axis_index("sub")
    sub_count = lax.axis_size("sub")
    tp_index = lax.axis_index("tp")
    tp_count = lax.axis_size("tp")
    own_index = half * sub_count + sub
    partner = (1 - half) * sub_count + sub
    span_len = new_queries.shape[0]
    width = new_queries.shape[1]
    head_count = width // HEAD_DIM
    page_count = kv_pages.shape[0]
    page_size = kv_pages.shape[2]
    out_cols = w_out.shape[1] // tp_count
    swap = [(0, 1), (1, 0)]

    w_recv = []
    for shift in range(1, tp_count):
        target = (tp_index + shift) % tp_count
        piece = lax.dynamic_slice_in_dim(w_out, target * out_cols, out_cols, axis=1)
        perm = [(i, (i + shift) % tp_count) for i in range(tp_count)]
        w_recv.append(lax.ppermute(blocked(piece, projection_block(out_cols)), "tp", perm))
    w_mine = lax.dynamic_slice_in_dim(w_out, tp_index * out_cols, out_cols, axis=1)
    w_mine = blocked(w_mine, projection_block(out_cols))

    owners = jnp.where(page_table >= 0, page_table // page_count, -1)
    held_here = owners == own_index
    local_page = jnp.sum(jnp.where(held_here, page_table - own_index * page_count, 0), axis=1)
    dest = jnp.arange(sub_count, dtype=jnp.int32)
    own_length = lax.dynamic_index_in_dim(cache_len, own_index, 0, keepdims=False)
    partner_length = lax.dynamic_index_in_dim(cache_len, partner, 0, keepdims=False)
    positions = own_length + jnp.arange(span_len, dtype=jnp.int32)
    query_rot = rotate_rows(new_queries, positions)
    partner_query = lax.ppermute(query_rot, "half", swap)

    far_pages = jnp.take(kv_pages, jnp.take(local_page, (1 - half) * sub_count + dest), axis=0, mode="clip")
    far_incoming = lax.all_to_all(far_pages, "sub", split_axis=0, concat_axis=0, tiled=True)
    near_pages = jnp.take(kv_pages, jnp.take(local_page, half * sub_count + dest), axis=0, mode="clip")
    partner_query, near_pages = lax.optimization_barrier((partner_query, near_pages))
    near_incoming = lax.all_to_all(near_pages, "sub", split_axis=0, concat_axis=0, tiled=True)
    key_rot = rotate_rows(new_keys, positions)

    source_base = half * sub_count
    ok_own = usable_keys(page_table, own_index, own_length, source_base, sub_count, page_count, page_size)
    ok_partner = usable_keys(page_table, partner, partner_length, source_base, sub_count, page_count, page_size)

    local_acc, local_stats = local_attend(query_rot, key_rot, new_values)
    far_out, far_stats = far_attend(ok_partner, partner_query, far_incoming)
    back_out = lax.ppermute(far_out, "half", swap)
    back_stats = lax.ppermute(far_stats, "half", swap)
    attended = near_attend(
        ok_own, query_rot, near_incoming, local_acc, local_stats, back_out, back_stats
    )

    parts = [attended]
    for shift in range(1, tp_count):
        perm = [(i, (i + shift) % tp_count) for i in range(tp_count)]
        parts.append(lax.ppermute(attended, "tp", perm))
    return project(parts, [w_mine] + w_recv, out_bias)


def solution(mesh):
    req_count = mesh.shape["req"]
    tp_count = mesh.shape["tp"]
    assert tuple(mesh.axis_names) == ("req", "tp")
    devices = mesh.devices.reshape(2, req_count // 2, tp_count)
    split_mesh = jax.sharding.Mesh(devices, ("half", "sub", "tp"))
    rows = ("half", "sub")
    return jax.shard_map(
        on_device,
        mesh=split_mesh,
        in_specs=(
            P(rows, "tp"),
            P(rows, "tp"),
            P(rows, "tp"),
            P(rows, None, None, "tp"),
            P(),
            P(),
            P("tp", None),
            P("tp"),
        ),
        out_specs=P(rows, "tp"),
        check_vma=False,
    )
```

```python
import math
from functools import partial

import jax
import jax.numpy as jnp
from jax import lax
from jax.experimental import pallas as pl
from jax.experimental.pallas import tpu as pltpu
from jax.sharding import PartitionSpec as P

HEAD_DIM = 128
ROT = 32


NEG_FILL = -1e30


def rotate_rows(block, positions):
    row_count = block.shape[0]
    shaped = block.astype(jnp.float32).reshape(row_count, -1, HEAD_DIM)
    half_rot = ROT // 2
    frequency = 10000.0 ** (-2.0 * jnp.arange(half_rot, dtype=jnp.float32) / ROT)
    angles = positions.astype(jnp.float32)[:, None] * frequency[None, :]
    cosine = jnp.cos(angles)[:, None, :]
    sines = jnp.sin(angles)[:, None, :]
    first_half = shaped[:, :, :half_rot]
    second_half = shaped[:, :, half_rot:ROT]
    turned = jnp.concatenate(
        [
            first_half * cosine - second_half * sines,
            second_half * cosine + first_half * sines,
            shaped[:, :, ROT:],
        ],
        axis=2,
    )
    return turned.reshape(row_count, -1).astype(jnp.bfloat16)


SCORE_DIMS = (((1,), (1,)), ((), ()))


def head_cols(ref, g):
    return ref[..., g * HEAD_DIM:(g + 1) * HEAD_DIM]


def local_kernel(q_ref, kl_ref, vl_ref, acc_ref, st_ref):
    score_scale = 1.0 / math.sqrt(HEAD_DIM)
    for g in range(st_ref.shape[0]):
        q = head_cols(q_ref, g)
        span = q.shape[0]
        s = lax.dot_general(q, head_cols(kl_ref, g), SCORE_DIMS, preferred_element_type=jnp.float32) * score_scale
        row = lax.broadcasted_iota(jnp.int32, (span, span), 0)
        col = lax.broadcasted_iota(jnp.int32, (span, span), 1)
        s = jnp.where(row >= col, s, NEG_FILL)
        m = jnp.max(s, axis=1, keepdims=True)
        p = jnp.exp(s - m)
        acc_ref[:, g * HEAD_DIM:(g + 1) * HEAD_DIM] = jnp.dot(
            p.astype(jnp.bfloat16), head_cols(vl_ref, g), preferred_element_type=jnp.float32
        )
        st_ref[g, :, 0:1] = m
        st_ref[g, :, 1:2] = jnp.sum(p, axis=1, keepdims=True)


def head_pages(kp_ref, vp_ref, g):
    block_count, page_size, _ = kp_ref.shape
    keys = head_cols(kp_ref, g).reshape(block_count * page_size, HEAD_DIM)
    values = head_cols(vp_ref, g).reshape(block_count * page_size, HEAD_DIM)
    return keys, values


def page_partial(q, keys_p, values_p, ok):
    score_scale = 1.0 / math.sqrt(HEAD_DIM)
    s = lax.dot_general(q, keys_p, SCORE_DIMS, preferred_element_type=jnp.float32) * score_scale
    s = jnp.where(ok > 0, s, NEG_FILL)
    m = jnp.max(s, axis=1, keepdims=True)
    p = jnp.exp(s - m)
    l = jnp.sum(p, axis=1, keepdims=True)
    acc = jnp.dot(p.astype(jnp.bfloat16), values_p, preferred_element_type=jnp.float32)
    return m, l, acc


def far_kernel(q_ref, kp_ref, vp_ref, ok_ref, o_ref, st_ref):
    ok = ok_ref[...]
    for g in range(st_ref.shape[0]):
        keys, values = head_pages(kp_ref, vp_ref, g)
        m, l, acc = page_partial(head_cols(q_ref, g), keys, values, ok)
        o_ref[:, g * HEAD_DIM:(g + 1) * HEAD_DIM] = (acc / l).astype(o_ref.dtype)
        st_ref[g, :, 0:1] = m
        st_ref[g, :, 1:2] = l


def near_kernel(q_ref, kp_ref, vp_ref, ok_ref, la_ref, lst_ref, bo_ref, bst_ref, o_ref):
    ok = ok_ref[...]
    for g in range(lst_ref.shape[0]):
        keys, values = head_pages(kp_ref, vp_ref, g)
        m, l, acc = page_partial(head_cols(q_ref, g), keys, values, ok)
        local = lst_ref[g]
        local_max = local[:, 0:1]
        local_sum = local[:, 1:2]
        back = bst_ref[g]
        back_max = back[:, 0:1]
        back_sum = back[:, 1:2]
        peak = jnp.maximum(jnp.maximum(m, local_max), back_max)
        page_w = jnp.exp(m - peak)
        local_w = jnp.exp(local_max - peak)
        back_w = jnp.exp(back_max - peak) * back_sum
        merged = (
            acc * page_w
            + head_cols(la_ref, g) * local_w
            + head_cols(bo_ref, g).astype(jnp.float32) * back_w
        )
        total = l * page_w + local_sum * local_w + back_w
        o_ref[:, g * HEAD_DIM:(g + 1) * HEAD_DIM] = (merged / total).astype(o_ref.dtype)


def heads_per_step(head_count):
    return 2 if head_count % 2 == 0 else 1


def head_specs(span, block_count, page_size, group):
    cols = group * HEAD_DIM
    col_spec = pl.BlockSpec((span, cols), lambda h: (0, h))
    stat_spec = pl.BlockSpec((group, span, 2), lambda h: (h, 0, 0))
    page_specs = [
        pl.BlockSpec((block_count, None, page_size, cols), lambda h: (0, 0, 0, h)),
        pl.BlockSpec((block_count, None, page_size, cols), lambda h: (0, 1, 0, h)),
        pl.BlockSpec((1, block_count * page_size), lambda h: (0, 0)),
    ]
    return col_spec, stat_spec, page_specs


def local_attend(query_rot, key_rot, values):
    span, width = query_rot.shape
    head_count = width // HEAD_DIM
    group = heads_per_step(head_count)
    col_spec, stat_spec, _ = head_specs(span, 1, 1, group)
    return pl.pallas_call(
        local_kernel,
        grid=(head_count // group,),
        in_specs=[col_spec, col_spec, col_spec],
        out_specs=[col_spec, stat_spec],
        out_shape=[
            jax.ShapeDtypeStruct((span, width), jnp.float32),
            jax.ShapeDtypeStruct((head_count, span, 2), jnp.float32),
        ],
    )(query_rot, key_rot, values)


def far_attend(key_ok, query_rot, incoming):
    span, width = query_rot.shape
    head_count = width // HEAD_DIM
    group = heads_per_step(head_count)
    col_spec, stat_spec, page_specs = head_specs(span, incoming.shape[0], incoming.shape[2], group)
    return pl.pallas_call(
        far_kernel,
        grid=(head_count // group,),
        in_specs=[col_spec] + page_specs,
        out_specs=[col_spec, stat_spec],
        out_shape=[
            jax.ShapeDtypeStruct((span, width), jnp.bfloat16),
            jax.ShapeDtypeStruct((head_count, span, 2), jnp.float32),
        ],
    )(query_rot, incoming, incoming, key_ok)


def near_attend(key_ok, query_rot, incoming, local_acc, local_stats, back_out, back_stats):
    span, width = query_rot.shape
    head_count = width // HEAD_DIM
    group = heads_per_step(head_count)
    col_spec, stat_spec, page_specs = head_specs(span, incoming.shape[0], incoming.shape[2], group)
    return pl.pallas_call(
        near_kernel,
        grid=(head_count // group,),
        in_specs=[col_spec] + page_specs + [col_spec, stat_spec, col_spec, stat_spec],
        out_specs=col_spec,
        out_shape=jax.ShapeDtypeStruct((span, width), jnp.bfloat16),
    )(query_rot, incoming, incoming, key_ok, local_acc, local_stats, back_out, back_stats)


def projection_kernel(*refs):
    count = (len(refs) - 2) // 2
    total = refs[2 * count][...].astype(jnp.float32)
    for j in range(count):
        total = total + jnp.dot(refs[j][...], refs[count + j][...], preferred_element_type=jnp.float32)
    refs[-1][...] = total.astype(refs[-1].dtype)


def project(parts, weights, bias):
    span, rows = parts[0].shape
    out_cols = weights[0].shape[1]
    block = 512 if out_cols % 512 == 0 else out_cols
    a_spec = pl.BlockSpec((span, rows), lambda c: (0, 0))
    w_spec = pl.BlockSpec((rows, block), lambda c: (0, c))
    b_spec = pl.BlockSpec((1, block), lambda c: (0, c))
    return pl.pallas_call(
        projection_kernel,
        grid=(out_cols // block,),
        in_specs=[a_spec] * len(parts) + [w_spec] * len(weights) + [b_spec],
        out_specs=pl.BlockSpec((span, block), lambda c: (0, c)),
        out_shape=jax.ShapeDtypeStruct((span, out_cols), jnp.bfloat16),
    )(*parts, *weights, bias.reshape(1, out_cols))


def gather_kernel(ids_ref, src_ref, dst_ref, sems):
    copies = [
        pltpu.make_async_copy(src_ref.at[ids_ref[i]], dst_ref.at[i], sems.at[i])
        for i in range(dst_ref.shape[0])
    ]
    for copy in copies:
        copy.start()
    for copy in copies:
        copy.wait()


def gather_pages(kv_pages, ids):
    count = ids.shape[0]
    ids = jnp.clip(ids, 0, kv_pages.shape[0] - 1).astype(jnp.int32)
    return pl.pallas_call(
        gather_kernel,
        grid_spec=pltpu.PrefetchScalarGridSpec(
            num_scalar_prefetch=1,
            grid=(1,),
            in_specs=[pl.BlockSpec(memory_space=pl.ANY)],
            out_specs=pl.BlockSpec(memory_space=pl.ANY),
            scratch_shapes=[pltpu.SemaphoreType.DMA((count,))],
        ),
        out_shape=jax.ShapeDtypeStruct((count,) + kv_pages.shape[1:], kv_pages.dtype),
    )(ids, kv_pages)


def usable_keys(page_table, request, length, source_base, source_count, page_count, page_size):
    row = lax.dynamic_index_in_dim(page_table, request, 0, keepdims=False)
    row_owner = jnp.where(row >= 0, row // page_count, -1)
    sources = source_base + jnp.arange(source_count, dtype=jnp.int32)
    slot_ids = jnp.arange(row.shape[0], dtype=jnp.int32)
    matches = row_owner[None, :] == sources[:, None]
    present = jnp.any(matches, axis=1)
    slot_of = jnp.sum(jnp.where(matches, slot_ids[None, :], 0), axis=1)
    nvalid = jnp.where(present, jnp.clip(length - slot_of * page_size, 0, page_size), 0)
    within = jnp.arange(page_size, dtype=jnp.int32)
    return (within[None, :] < nvalid[:, None]).astype(jnp.int32).reshape(1, source_count * page_size)


def on_device(new_queries, new_keys, new_values, kv_pages, page_table, cache_len, w_out, out_bias):
    half = lax.axis_index("half")
    sub = lax.axis_index("sub")
    sub_count = lax.axis_size("sub")
    tp_index = lax.axis_index("tp")
    tp_count = lax.axis_size("tp")
    own_index = half * sub_count + sub
    partner = (1 - half) * sub_count + sub
    span_len = new_queries.shape[0]
    width = new_queries.shape[1]
    head_count = width // HEAD_DIM
    page_count = kv_pages.shape[0]
    page_size = kv_pages.shape[2]
    out_cols = w_out.shape[1] // tp_count
    swap = [(0, 1), (1, 0)]

    w_recv = []
    for shift in range(1, tp_count):
        target = (tp_index + shift) % tp_count
        piece = lax.dynamic_slice_in_dim(w_out, target * out_cols, out_cols, axis=1)
        perm = [(i, (i + shift) % tp_count) for i in range(tp_count)]
        w_recv.append(lax.ppermute(piece, "tp", perm))
    w_mine = lax.dynamic_slice_in_dim(w_out, tp_index * out_cols, out_cols, axis=1)

    owners = jnp.where(page_table >= 0, page_table // page_count, -1)
    held_here = owners == own_index
    local_page = jnp.sum(jnp.where(held_here, page_table - own_index * page_count, 0), axis=1)
    dest = jnp.arange(sub_count, dtype=jnp.int32)
    own_length = lax.dynamic_index_in_dim(cache_len, own_index, 0, keepdims=False)
    partner_length = lax.dynamic_index_in_dim(cache_len, partner, 0, keepdims=False)
    positions = own_length + jnp.arange(span_len, dtype=jnp.int32)
    query_rot = rotate_rows(new_queries, positions)
    partner_query = lax.ppermute(query_rot, "half", swap)

    far_pages = gather_pages(kv_pages, jnp.take(local_page, (1 - half) * sub_count + dest))
    far_incoming = lax.all_to_all(far_pages, "sub", split_axis=0, concat_axis=0, tiled=True)
    near_pages = gather_pages(kv_pages, jnp.take(local_page, half * sub_count + dest))
    partner_query, near_pages = lax.optimization_barrier((partner_query, near_pages))
    near_incoming = lax.all_to_all(near_pages, "sub", split_axis=0, concat_axis=0, tiled=True)
    key_rot = rotate_rows(new_keys, positions)

    source_base = half * sub_count
    ok_own = usable_keys(page_table, own_index, own_length, source_base, sub_count, page_count, page_size)
    ok_partner = usable_keys(page_table, partner, partner_length, source_base, sub_count, page_count, page_size)

    local_acc, local_stats = local_attend(query_rot, key_rot, new_values)
    far_out, far_stats = far_attend(ok_partner, partner_query, far_incoming)
    back_out = lax.ppermute(far_out, "half", swap)
    back_stats = lax.ppermute(far_stats, "half", swap)
    attended = near_attend(
        ok_own, query_rot, near_incoming, local_acc, local_stats, back_out, back_stats
    )

    parts = [attended]
    for shift in range(1, tp_count):
        perm = [(i, (i + shift) % tp_count) for i in range(tp_count)]
        parts.append(lax.ppermute(attended, "tp", perm))
    return project(parts, [w_mine] + w_recv, out_bias)


def solution(mesh):
    req_count = mesh.shape["req"]
    tp_count = mesh.shape["tp"]
    assert tuple(mesh.axis_names) == ("req", "tp")
    devices = mesh.devices.reshape(2, req_count // 2, tp_count)
    split_mesh = jax.sharding.Mesh(devices, ("half", "sub", "tp"))
    rows = ("half", "sub")
    return jax.shard_map(
        on_device,
        mesh=split_mesh,
        in_specs=(
            P(rows, "tp"),
            P(rows, "tp"),
            P(rows, "tp"),
            P(rows, None, None, "tp"),
            P(),
            P(),
            P("tp", None),
            P("tp"),
        ),
        out_specs=P(rows, "tp"),
        check_vma=False,
    )
```

```python
import math
from functools import partial

import jax
import jax.numpy as jnp
from jax import lax
from jax.experimental import pallas as pl
from jax.experimental.pallas import tpu as pltpu
from jax.sharding import PartitionSpec as P

HEAD_DIM = 128
ROT = 32


NEG_FILL = -1e30


def rotate_rows(block, positions):
    row_count = block.shape[0]
    shaped = block.astype(jnp.float32).reshape(row_count, -1, HEAD_DIM)
    half_rot = ROT // 2
    frequency = 10000.0 ** (-2.0 * jnp.arange(half_rot, dtype=jnp.float32) / ROT)
    angles = positions.astype(jnp.float32)[:, None] * frequency[None, :]
    cosine = jnp.cos(angles)[:, None, :]
    sines = jnp.sin(angles)[:, None, :]
    first_half = shaped[:, :, :half_rot]
    second_half = shaped[:, :, half_rot:ROT]
    turned = jnp.concatenate(
        [
            first_half * cosine - second_half * sines,
            second_half * cosine + first_half * sines,
            shaped[:, :, ROT:],
        ],
        axis=2,
    )
    return turned.reshape(row_count, -1).astype(jnp.bfloat16)


SCORE_DIMS = (((1,), (1,)), ((), ()))


def head_cols(ref, g):
    return ref[..., g * HEAD_DIM:(g + 1) * HEAD_DIM]


def local_kernel(q_ref, kl_ref, vl_ref, acc_ref, st_ref):
    score_scale = 1.0 / math.sqrt(HEAD_DIM)
    for g in range(st_ref.shape[0]):
        q = head_cols(q_ref, g)
        span = q.shape[0]
        s = lax.dot_general(q, head_cols(kl_ref, g), SCORE_DIMS, preferred_element_type=jnp.float32) * score_scale
        row = lax.broadcasted_iota(jnp.int32, (span, span), 0)
        col = lax.broadcasted_iota(jnp.int32, (span, span), 1)
        s = jnp.where(row >= col, s, NEG_FILL)
        m = jnp.max(s, axis=1, keepdims=True)
        p = jnp.exp(s - m)
        acc_ref[:, g * HEAD_DIM:(g + 1) * HEAD_DIM] = jnp.dot(
            p.astype(jnp.bfloat16), head_cols(vl_ref, g), preferred_element_type=jnp.float32
        )
        st_ref[g, :, 0:1] = m
        st_ref[g, :, 1:2] = jnp.sum(p, axis=1, keepdims=True)


def head_pages(kp_ref, vp_ref, g):
    block_count, page_size, _ = kp_ref.shape
    keys = head_cols(kp_ref, g).reshape(block_count * page_size, HEAD_DIM)
    values = head_cols(vp_ref, g).reshape(block_count * page_size, HEAD_DIM)
    return keys, values


def page_partial(q, keys_p, values_p, ok):
    score_scale = 1.0 / math.sqrt(HEAD_DIM)
    s = lax.dot_general(q, keys_p, SCORE_DIMS, preferred_element_type=jnp.float32) * score_scale
    s = jnp.where(ok > 0, s, NEG_FILL)
    m = jnp.max(s, axis=1, keepdims=True)
    p = jnp.exp(s - m)
    l = jnp.sum(p, axis=1, keepdims=True)
    acc = jnp.dot(p.astype(jnp.bfloat16), values_p, preferred_element_type=jnp.float32)
    return m, l, acc


def far_kernel(q_ref, kp_ref, vp_ref, ok_ref, o_ref, st_ref):
    ok = ok_ref[...]
    for g in range(st_ref.shape[0]):
        keys, values = head_pages(kp_ref, vp_ref, g)
        m, l, acc = page_partial(head_cols(q_ref, g), keys, values, ok)
        o_ref[:, g * HEAD_DIM:(g + 1) * HEAD_DIM] = (acc / l).astype(o_ref.dtype)
        st_ref[g, :, 0:1] = m
        st_ref[g, :, 1:2] = l


def near_kernel(q_ref, kp_ref, vp_ref, ok_ref, la_ref, lst_ref, bo_ref, bst_ref, o_ref):
    ok = ok_ref[...]
    for g in range(lst_ref.shape[0]):
        keys, values = head_pages(kp_ref, vp_ref, g)
        m, l, acc = page_partial(head_cols(q_ref, g), keys, values, ok)
        local = lst_ref[g]
        local_max = local[:, 0:1]
        local_sum = local[:, 1:2]
        back = bst_ref[g]
        back_max = back[:, 0:1]
        back_sum = back[:, 1:2]
        peak = jnp.maximum(jnp.maximum(m, local_max), back_max)
        page_w = jnp.exp(m - peak)
        local_w = jnp.exp(local_max - peak)
        back_w = jnp.exp(back_max - peak) * back_sum
        merged = (
            acc * page_w
            + head_cols(la_ref, g) * local_w
            + head_cols(bo_ref, g).astype(jnp.float32) * back_w
        )
        total = l * page_w + local_sum * local_w + back_w
        o_ref[:, g * HEAD_DIM:(g + 1) * HEAD_DIM] = (merged / total).astype(o_ref.dtype)


def heads_per_step(head_count):
    return 2 if head_count % 2 == 0 else 1


def head_specs(span, block_count, page_size, group):
    cols = group * HEAD_DIM
    col_spec = pl.BlockSpec((span, cols), lambda h: (0, h))
    stat_spec = pl.BlockSpec((group, span, 2), lambda h: (h, 0, 0))
    page_specs = [
        pl.BlockSpec((block_count, None, page_size, cols), lambda h: (0, 0, 0, h)),
        pl.BlockSpec((block_count, None, page_size, cols), lambda h: (0, 1, 0, h)),
        pl.BlockSpec((1, block_count * page_size), lambda h: (0, 0)),
    ]
    return col_spec, stat_spec, page_specs


def local_attend(query_rot, key_rot, values):
    span, width = query_rot.shape
    head_count = width // HEAD_DIM
    group = heads_per_step(head_count)
    col_spec, stat_spec, _ = head_specs(span, 1, 1, group)
    return pl.pallas_call(
        local_kernel,
        grid=(head_count // group,),
        in_specs=[col_spec, col_spec, col_spec],
        out_specs=[col_spec, stat_spec],
        out_shape=[
            jax.ShapeDtypeStruct((span, width), jnp.float32),
            jax.ShapeDtypeStruct((head_count, span, 2), jnp.float32),
        ],
    )(query_rot, key_rot, values)


def far_attend(key_ok, query_rot, incoming):
    span, width = query_rot.shape
    head_count = width // HEAD_DIM
    group = heads_per_step(head_count)
    col_spec, stat_spec, page_specs = head_specs(span, incoming.shape[0], incoming.shape[2], group)
    return pl.pallas_call(
        far_kernel,
        grid=(head_count // group,),
        in_specs=[col_spec] + page_specs,
        out_specs=[col_spec, stat_spec],
        out_shape=[
            jax.ShapeDtypeStruct((span, width), jnp.bfloat16),
            jax.ShapeDtypeStruct((head_count, span, 2), jnp.float32),
        ],
    )(query_rot, incoming, incoming, key_ok)


def near_attend(key_ok, query_rot, incoming, local_acc, local_stats, back_out, back_stats):
    span, width = query_rot.shape
    head_count = width // HEAD_DIM
    group = heads_per_step(head_count)
    col_spec, stat_spec, page_specs = head_specs(span, incoming.shape[0], incoming.shape[2], group)
    return pl.pallas_call(
        near_kernel,
        grid=(head_count // group,),
        in_specs=[col_spec] + page_specs + [col_spec, stat_spec, col_spec, stat_spec],
        out_specs=col_spec,
        out_shape=jax.ShapeDtypeStruct((span, width), jnp.bfloat16),
    )(query_rot, incoming, incoming, key_ok, local_acc, local_stats, back_out, back_stats)


def projection_kernel(*refs):
    count = (len(refs) - 2) // 2
    total = refs[2 * count][...].astype(jnp.float32)
    for j in range(count):
        total = total + jnp.dot(refs[j][...], refs[count + j][...], preferred_element_type=jnp.float32)
    refs[-1][...] = total.astype(refs[-1].dtype)


def project(parts, weights, bias):
    span, rows = parts[0].shape
    out_cols = weights[0].shape[1]
    block = 1024 if out_cols % 1024 == 0 else out_cols
    a_spec = pl.BlockSpec((span, rows), lambda c: (0, 0))
    w_spec = pl.BlockSpec((rows, block), lambda c: (0, c))
    b_spec = pl.BlockSpec((1, block), lambda c: (0, c))
    return pl.pallas_call(
        projection_kernel,
        grid=(out_cols // block,),
        in_specs=[a_spec] * len(parts) + [w_spec] * len(weights) + [b_spec],
        out_specs=pl.BlockSpec((span, block), lambda c: (0, c)),
        out_shape=jax.ShapeDtypeStruct((span, out_cols), jnp.bfloat16),
    )(*parts, *weights, bias.reshape(1, out_cols))


def usable_keys(page_table, request, length, source_base, source_count, page_count, page_size):
    row = lax.dynamic_index_in_dim(page_table, request, 0, keepdims=False)
    row_owner = jnp.where(row >= 0, row // page_count, -1)
    sources = source_base + jnp.arange(source_count, dtype=jnp.int32)
    slot_ids = jnp.arange(row.shape[0], dtype=jnp.int32)
    matches = row_owner[None, :] == sources[:, None]
    present = jnp.any(matches, axis=1)
    slot_of = jnp.sum(jnp.where(matches, slot_ids[None, :], 0), axis=1)
    nvalid = jnp.where(present, jnp.clip(length - slot_of * page_size, 0, page_size), 0)
    within = jnp.arange(page_size, dtype=jnp.int32)
    return (within[None, :] < nvalid[:, None]).astype(jnp.int32).reshape(1, source_count * page_size)


def on_device(new_queries, new_keys, new_values, kv_pages, page_table, cache_len, w_out, out_bias):
    half = lax.axis_index("half")
    sub = lax.axis_index("sub")
    sub_count = lax.axis_size("sub")
    tp_index = lax.axis_index("tp")
    tp_count = lax.axis_size("tp")
    own_index = half * sub_count + sub
    partner = (1 - half) * sub_count + sub
    span_len = new_queries.shape[0]
    width = new_queries.shape[1]
    head_count = width // HEAD_DIM
    page_count = kv_pages.shape[0]
    page_size = kv_pages.shape[2]
    out_cols = w_out.shape[1] // tp_count
    swap = [(0, 1), (1, 0)]

    w_recv = []
    for shift in range(1, tp_count):
        target = (tp_index + shift) % tp_count
        piece = lax.dynamic_slice_in_dim(w_out, target * out_cols, out_cols, axis=1)
        perm = [(i, (i + shift) % tp_count) for i in range(tp_count)]
        w_recv.append(lax.ppermute(piece, "tp", perm))
    w_mine = lax.dynamic_slice_in_dim(w_out, tp_index * out_cols, out_cols, axis=1)

    owners = jnp.where(page_table >= 0, page_table // page_count, -1)
    held_here = owners == own_index
    local_page = jnp.sum(jnp.where(held_here, page_table - own_index * page_count, 0), axis=1)
    dest = jnp.arange(sub_count, dtype=jnp.int32)
    own_length = lax.dynamic_index_in_dim(cache_len, own_index, 0, keepdims=False)
    partner_length = lax.dynamic_index_in_dim(cache_len, partner, 0, keepdims=False)
    positions = own_length + jnp.arange(span_len, dtype=jnp.int32)
    query_rot = rotate_rows(new_queries, positions)
    partner_query = lax.ppermute(query_rot, "half", swap)

    far_pages = jnp.take(kv_pages, jnp.take(local_page, (1 - half) * sub_count + dest), axis=0, mode="clip")
    far_incoming = lax.all_to_all(far_pages, "sub", split_axis=0, concat_axis=0, tiled=True)
    near_pages = jnp.take(kv_pages, jnp.take(local_page, half * sub_count + dest), axis=0, mode="clip")
    partner_query, near_pages = lax.optimization_barrier((partner_query, near_pages))
    near_incoming = lax.all_to_all(near_pages, "sub", split_axis=0, concat_axis=0, tiled=True)
    key_rot = rotate_rows(new_keys, positions)

    source_base = half * sub_count
    ok_own = usable_keys(page_table, own_index, own_length, source_base, sub_count, page_count, page_size)
    ok_partner = usable_keys(page_table, partner, partner_length, source_base, sub_count, page_count, page_size)

    local_acc, local_stats = local_attend(query_rot, key_rot, new_values)
    far_out, far_stats = far_attend(ok_partner, partner_query, far_incoming)
    back_out = lax.ppermute(far_out, "half", swap)
    back_stats = lax.ppermute(far_stats, "half", swap)
    attended = near_attend(
        ok_own, query_rot, near_incoming, local_acc, local_stats, back_out, back_stats
    )

    parts = [attended]
    for shift in range(1, tp_count):
        perm = [(i, (i + shift) % tp_count) for i in range(tp_count)]
        parts.append(lax.ppermute(attended, "tp", perm))
    return project(parts, [w_mine] + w_recv, out_bias)


def solution(mesh):
    req_count = mesh.shape["req"]
    tp_count = mesh.shape["tp"]
    assert tuple(mesh.axis_names) == ("req", "tp")
    devices = mesh.devices.reshape(2, req_count // 2, tp_count)
    split_mesh = jax.sharding.Mesh(devices, ("half", "sub", "tp"))
    rows = ("half", "sub")
    return jax.shard_map(
        on_device,
        mesh=split_mesh,
        in_specs=(
            P(rows, "tp"),
            P(rows, "tp"),
            P(rows, "tp"),
            P(rows, None, None, "tp"),
            P(),
            P(),
            P("tp", None),
            P("tp"),
        ),
        out_specs=P(rows, "tp"),
        check_vma=False,
    )
```

```python
import math
from functools import partial

import jax
import jax.numpy as jnp
from jax import lax
from jax.experimental import pallas as pl
from jax.experimental.pallas import tpu as pltpu
from jax.sharding import PartitionSpec as P

HEAD_DIM = 128
ROT = 32


NEG_FILL = -1e30


def rotate_rows(block, positions):
    row_count = block.shape[0]
    shaped = block.astype(jnp.float32).reshape(row_count, -1, HEAD_DIM)
    half_rot = ROT // 2
    frequency = 10000.0 ** (-2.0 * jnp.arange(half_rot, dtype=jnp.float32) / ROT)
    angles = positions.astype(jnp.float32)[:, None] * frequency[None, :]
    cosine = jnp.cos(angles)[:, None, :]
    sines = jnp.sin(angles)[:, None, :]
    first_half = shaped[:, :, :half_rot]
    second_half = shaped[:, :, half_rot:ROT]
    turned = jnp.concatenate(
        [
            first_half * cosine - second_half * sines,
            second_half * cosine + first_half * sines,
            shaped[:, :, ROT:],
        ],
        axis=2,
    )
    return turned.reshape(row_count, -1).astype(jnp.bfloat16)


SCORE_DIMS = (((1,), (1,)), ((), ()))


def head_cols(ref, g):
    return ref[..., g * HEAD_DIM:(g + 1) * HEAD_DIM]


def local_kernel(q_ref, kl_ref, vl_ref, acc_ref, st_ref):
    score_scale = 1.0 / math.sqrt(HEAD_DIM)
    for g in range(st_ref.shape[0]):
        q = head_cols(q_ref, g)
        span = q.shape[0]
        s = lax.dot_general(q, head_cols(kl_ref, g), SCORE_DIMS, preferred_element_type=jnp.float32) * score_scale
        row = lax.broadcasted_iota(jnp.int32, (span, span), 0)
        col = lax.broadcasted_iota(jnp.int32, (span, span), 1)
        s = jnp.where(row >= col, s, NEG_FILL)
        m = jnp.max(s, axis=1, keepdims=True)
        p = jnp.exp(s - m)
        acc_ref[:, g * HEAD_DIM:(g + 1) * HEAD_DIM] = jnp.dot(
            p.astype(jnp.bfloat16), head_cols(vl_ref, g), preferred_element_type=jnp.float32
        )
        st_ref[g, :, 0:1] = m
        st_ref[g, :, 1:2] = jnp.sum(p, axis=1, keepdims=True)


def head_pages(kp_ref, vp_ref, g):
    block_count, page_size, _ = kp_ref.shape
    keys = head_cols(kp_ref, g).reshape(block_count * page_size, HEAD_DIM)
    values = head_cols(vp_ref, g).reshape(block_count * page_size, HEAD_DIM)
    return keys, values


def page_partial(q, keys_p, values_p, ok):
    score_scale = 1.0 / math.sqrt(HEAD_DIM)
    s = lax.dot_general(q, keys_p, SCORE_DIMS, preferred_element_type=jnp.float32) * score_scale
    s = jnp.where(ok > 0, s, NEG_FILL)
    m = jnp.max(s, axis=1, keepdims=True)
    p = jnp.exp(s - m)
    l = jnp.sum(p, axis=1, keepdims=True)
    acc = jnp.dot(p.astype(jnp.bfloat16), values_p, preferred_element_type=jnp.float32)
    return m, l, acc


def far_kernel(q_ref, kp_ref, vp_ref, ok_ref, o_ref, st_ref):
    ok = ok_ref[...]
    for g in range(st_ref.shape[0]):
        keys, values = head_pages(kp_ref, vp_ref, g)
        m, l, acc = page_partial(head_cols(q_ref, g), keys, values, ok)
        o_ref[:, g * HEAD_DIM:(g + 1) * HEAD_DIM] = (acc / l).astype(o_ref.dtype)
        st_ref[g, :, 0:1] = m
        st_ref[g, :, 1:2] = l


def near_kernel(q_ref, kp_ref, vp_ref, ok_ref, la_ref, lst_ref, bo_ref, bst_ref, o_ref):
    ok = ok_ref[...]
    for g in range(lst_ref.shape[0]):
        keys, values = head_pages(kp_ref, vp_ref, g)
        m, l, acc = page_partial(head_cols(q_ref, g), keys, values, ok)
        local = lst_ref[g]
        local_max = local[:, 0:1]
        local_sum = local[:, 1:2]
        back = bst_ref[g]
        back_max = back[:, 0:1]
        back_sum = back[:, 1:2]
        peak = jnp.maximum(jnp.maximum(m, local_max), back_max)
        page_w = jnp.exp(m - peak)
        local_w = jnp.exp(local_max - peak)
        back_w = jnp.exp(back_max - peak) * back_sum
        merged = (
            acc * page_w
            + head_cols(la_ref, g) * local_w
            + head_cols(bo_ref, g).astype(jnp.float32) * back_w
        )
        total = l * page_w + local_sum * local_w + back_w
        o_ref[:, g * HEAD_DIM:(g + 1) * HEAD_DIM] = (merged / total).astype(o_ref.dtype)


def heads_per_step(head_count):
    for group in (4, 2):
        if head_count % group == 0:
            return group
    return 1


def head_specs(span, block_count, page_size, group):
    cols = group * HEAD_DIM
    col_spec = pl.BlockSpec((span, cols), lambda h: (0, h))
    stat_spec = pl.BlockSpec((group, span, 2), lambda h: (h, 0, 0))
    page_specs = [
        pl.BlockSpec((block_count, None, page_size, cols), lambda h: (0, 0, 0, h)),
        pl.BlockSpec((block_count, None, page_size, cols), lambda h: (0, 1, 0, h)),
        pl.BlockSpec((1, block_count * page_size), lambda h: (0, 0)),
    ]
    return col_spec, stat_spec, page_specs


def local_attend(query_rot, key_rot, values):
    span, width = query_rot.shape
    head_count = width // HEAD_DIM
    group = heads_per_step(head_count)
    col_spec, stat_spec, _ = head_specs(span, 1, 1, group)
    return pl.pallas_call(
        local_kernel,
        grid=(head_count // group,),
        in_specs=[col_spec, col_spec, col_spec],
        out_specs=[col_spec, stat_spec],
        out_shape=[
            jax.ShapeDtypeStruct((span, width), jnp.float32),
            jax.ShapeDtypeStruct((head_count, span, 2), jnp.float32),
        ],
    )(query_rot, key_rot, values)


def far_attend(key_ok, query_rot, incoming):
    span, width = query_rot.shape
    head_count = width // HEAD_DIM
    group = heads_per_step(head_count)
    col_spec, stat_spec, page_specs = head_specs(span, incoming.shape[0], incoming.shape[2], group)
    return pl.pallas_call(
        far_kernel,
        grid=(head_count // group,),
        in_specs=[col_spec] + page_specs,
        out_specs=[col_spec, stat_spec],
        out_shape=[
            jax.ShapeDtypeStruct((span, width), jnp.bfloat16),
            jax.ShapeDtypeStruct((head_count, span, 2), jnp.float32),
        ],
    )(query_rot, incoming, incoming, key_ok)


def near_attend(key_ok, query_rot, incoming, local_acc, local_stats, back_out, back_stats):
    span, width = query_rot.shape
    head_count = width // HEAD_DIM
    group = heads_per_step(head_count)
    col_spec, stat_spec, page_specs = head_specs(span, incoming.shape[0], incoming.shape[2], group)
    return pl.pallas_call(
        near_kernel,
        grid=(head_count // group,),
        in_specs=[col_spec] + page_specs + [col_spec, stat_spec, col_spec, stat_spec],
        out_specs=col_spec,
        out_shape=jax.ShapeDtypeStruct((span, width), jnp.bfloat16),
    )(query_rot, incoming, incoming, key_ok, local_acc, local_stats, back_out, back_stats)


def projection_kernel(*refs):
    count = (len(refs) - 2) // 2
    total = refs[2 * count][...].astype(jnp.float32)
    for j in range(count):
        total = total + jnp.dot(refs[j][...], refs[count + j][...], preferred_element_type=jnp.float32)
    refs[-1][...] = total.astype(refs[-1].dtype)


def project(parts, weights, bias):
    span, rows = parts[0].shape
    out_cols = weights[0].shape[1]
    block = 1024 if out_cols % 1024 == 0 else out_cols
    a_spec = pl.BlockSpec((span, rows), lambda c: (0, 0))
    w_spec = pl.BlockSpec((rows, block), lambda c: (0, c))
    b_spec = pl.BlockSpec((1, block), lambda c: (0, c))
    return pl.pallas_call(
        projection_kernel,
        grid=(out_cols // block,),
        in_specs=[a_spec] * len(parts) + [w_spec] * len(weights) + [b_spec],
        out_specs=pl.BlockSpec((span, block), lambda c: (0, c)),
        out_shape=jax.ShapeDtypeStruct((span, out_cols), jnp.bfloat16),
    )(*parts, *weights, bias.reshape(1, out_cols))


def usable_keys(page_table, request, length, source_base, source_count, page_count, page_size):
    row = lax.dynamic_index_in_dim(page_table, request, 0, keepdims=False)
    row_owner = jnp.where(row >= 0, row // page_count, -1)
    sources = source_base + jnp.arange(source_count, dtype=jnp.int32)
    slot_ids = jnp.arange(row.shape[0], dtype=jnp.int32)
    matches = row_owner[None, :] == sources[:, None]
    present = jnp.any(matches, axis=1)
    slot_of = jnp.sum(jnp.where(matches, slot_ids[None, :], 0), axis=1)
    nvalid = jnp.where(present, jnp.clip(length - slot_of * page_size, 0, page_size), 0)
    within = jnp.arange(page_size, dtype=jnp.int32)
    return (within[None, :] < nvalid[:, None]).astype(jnp.int32).reshape(1, source_count * page_size)


def on_device(new_queries, new_keys, new_values, kv_pages, page_table, cache_len, w_out, out_bias):
    half = lax.axis_index("half")
    sub = lax.axis_index("sub")
    sub_count = lax.axis_size("sub")
    tp_index = lax.axis_index("tp")
    tp_count = lax.axis_size("tp")
    own_index = half * sub_count + sub
    partner = (1 - half) * sub_count + sub
    span_len = new_queries.shape[0]
    width = new_queries.shape[1]
    head_count = width // HEAD_DIM
    page_count = kv_pages.shape[0]
    page_size = kv_pages.shape[2]
    out_cols = w_out.shape[1] // tp_count
    swap = [(0, 1), (1, 0)]

    w_recv = []
    for shift in range(1, tp_count):
        target = (tp_index + shift) % tp_count
        piece = lax.dynamic_slice_in_dim(w_out, target * out_cols, out_cols, axis=1)
        perm = [(i, (i + shift) % tp_count) for i in range(tp_count)]
        w_recv.append(lax.ppermute(piece, "tp", perm))
    w_mine = lax.dynamic_slice_in_dim(w_out, tp_index * out_cols, out_cols, axis=1)

    owners = jnp.where(page_table >= 0, page_table // page_count, -1)
    held_here = owners == own_index
    local_page = jnp.sum(jnp.where(held_here, page_table - own_index * page_count, 0), axis=1)
    dest = jnp.arange(sub_count, dtype=jnp.int32)
    own_length = lax.dynamic_index_in_dim(cache_len, own_index, 0, keepdims=False)
    partner_length = lax.dynamic_index_in_dim(cache_len, partner, 0, keepdims=False)
    positions = own_length + jnp.arange(span_len, dtype=jnp.int32)
    query_rot = rotate_rows(new_queries, positions)
    partner_query = lax.ppermute(query_rot, "half", swap)

    far_pages = jnp.take(kv_pages, jnp.take(local_page, (1 - half) * sub_count + dest), axis=0, mode="clip")
    far_incoming = lax.all_to_all(far_pages, "sub", split_axis=0, concat_axis=0, tiled=True)
    near_pages = jnp.take(kv_pages, jnp.take(local_page, half * sub_count + dest), axis=0, mode="clip")
    partner_query, near_pages = lax.optimization_barrier((partner_query, near_pages))
    near_incoming = lax.all_to_all(near_pages, "sub", split_axis=0, concat_axis=0, tiled=True)
    key_rot = rotate_rows(new_keys, positions)

    source_base = half * sub_count
    ok_own = usable_keys(page_table, own_index, own_length, source_base, sub_count, page_count, page_size)
    ok_partner = usable_keys(page_table, partner, partner_length, source_base, sub_count, page_count, page_size)

    local_acc, local_stats = local_attend(query_rot, key_rot, new_values)
    far_out, far_stats = far_attend(ok_partner, partner_query, far_incoming)
    back_out = lax.ppermute(far_out, "half", swap)
    back_stats = lax.ppermute(far_stats, "half", swap)
    attended = near_attend(
        ok_own, query_rot, near_incoming, local_acc, local_stats, back_out, back_stats
    )

    parts = [attended]
    for shift in range(1, tp_count):
        perm = [(i, (i + shift) % tp_count) for i in range(tp_count)]
        parts.append(lax.ppermute(attended, "tp", perm))
    return project(parts, [w_mine] + w_recv, out_bias)


def solution(mesh):
    req_count = mesh.shape["req"]
    tp_count = mesh.shape["tp"]
    assert tuple(mesh.axis_names) == ("req", "tp")
    devices = mesh.devices.reshape(2, req_count // 2, tp_count)
    split_mesh = jax.sharding.Mesh(devices, ("half", "sub", "tp"))
    rows = ("half", "sub")
    return jax.shard_map(
        on_device,
        mesh=split_mesh,
        in_specs=(
            P(rows, "tp"),
            P(rows, "tp"),
            P(rows, "tp"),
            P(rows, None, None, "tp"),
            P(),
            P(),
            P("tp", None),
            P("tp"),
        ),
        out_specs=P(rows, "tp"),
        check_vma=False,
    )
```

```python
import math
from functools import partial

import jax
import jax.numpy as jnp
from jax import lax
from jax.experimental import pallas as pl
from jax.experimental.pallas import tpu as pltpu
from jax.sharding import PartitionSpec as P

HEAD_DIM = 128
ROT = 32


NEG_FILL = -1e30


def rotate_rows(block, positions):
    row_count = block.shape[0]
    shaped = block.astype(jnp.float32).reshape(row_count, -1, HEAD_DIM)
    half_rot = ROT // 2
    frequency = 10000.0 ** (-2.0 * jnp.arange(half_rot, dtype=jnp.float32) / ROT)
    angles = positions.astype(jnp.float32)[:, None] * frequency[None, :]
    cosine = jnp.cos(angles)[:, None, :]
    sines = jnp.sin(angles)[:, None, :]
    first_half = shaped[:, :, :half_rot]
    second_half = shaped[:, :, half_rot:ROT]
    turned = jnp.concatenate(
        [
            first_half * cosine - second_half * sines,
            second_half * cosine + first_half * sines,
            shaped[:, :, ROT:],
        ],
        axis=2,
    )
    return turned.reshape(row_count, -1).astype(jnp.bfloat16)


SCORE_DIMS = (((1,), (1,)), ((), ()))


def head_cols(ref, g):
    return ref[..., g * HEAD_DIM:(g + 1) * HEAD_DIM]


def local_kernel(q_ref, kl_ref, vl_ref, acc_ref, st_ref):
    score_scale = 1.0 / math.sqrt(HEAD_DIM)
    for g in range(st_ref.shape[0]):
        q = head_cols(q_ref, g)
        span = q.shape[0]
        s = lax.dot_general(q, head_cols(kl_ref, g), SCORE_DIMS, preferred_element_type=jnp.float32) * score_scale
        row = lax.broadcasted_iota(jnp.int32, (span, span), 0)
        col = lax.broadcasted_iota(jnp.int32, (span, span), 1)
        s = jnp.where(row >= col, s, NEG_FILL)
        m = jnp.max(s, axis=1, keepdims=True)
        p = jnp.exp(s - m)
        acc_ref[:, g * HEAD_DIM:(g + 1) * HEAD_DIM] = jnp.dot(
            p.astype(jnp.bfloat16), head_cols(vl_ref, g), preferred_element_type=jnp.float32
        )
        st_ref[g, :, 0:1] = m
        st_ref[g, :, 1:2] = jnp.sum(p, axis=1, keepdims=True)


def head_pages(kp_ref, vp_ref, g):
    block_count, page_size, _ = kp_ref.shape
    keys = head_cols(kp_ref, g).reshape(block_count * page_size, HEAD_DIM)
    values = head_cols(vp_ref, g).reshape(block_count * page_size, HEAD_DIM)
    return keys, values


def page_partial(q, keys_p, values_p, ok):
    score_scale = 1.0 / math.sqrt(HEAD_DIM)
    s = lax.dot_general(q, keys_p, SCORE_DIMS, preferred_element_type=jnp.float32) * score_scale
    s = jnp.where(ok > 0, s, NEG_FILL)
    m = jnp.max(s, axis=1, keepdims=True)
    p = jnp.exp(s - m)
    l = jnp.sum(p, axis=1, keepdims=True)
    acc = jnp.dot(p.astype(jnp.bfloat16), values_p, preferred_element_type=jnp.float32)
    return m, l, acc


def far_kernel(q_ref, kp_ref, vp_ref, ok_ref, o_ref, st_ref):
    ok = ok_ref[...]
    for g in range(st_ref.shape[0]):
        keys, values = head_pages(kp_ref, vp_ref, g)
        m, l, acc = page_partial(head_cols(q_ref, g), keys, values, ok)
        o_ref[:, g * HEAD_DIM:(g + 1) * HEAD_DIM] = (acc / l).astype(o_ref.dtype)
        st_ref[g, :, 0:1] = m
        st_ref[g, :, 1:2] = l


def near_kernel(q_ref, kp_ref, vp_ref, ok_ref, la_ref, lst_ref, bo_ref, bst_ref, o_ref):
    ok = ok_ref[...]
    for g in range(lst_ref.shape[0]):
        keys, values = head_pages(kp_ref, vp_ref, g)
        m, l, acc = page_partial(head_cols(q_ref, g), keys, values, ok)
        local = lst_ref[g]
        local_max = local[:, 0:1]
        local_sum = local[:, 1:2]
        back = bst_ref[g]
        back_max = back[:, 0:1]
        back_sum = back[:, 1:2]
        peak = jnp.maximum(jnp.maximum(m, local_max), back_max)
        page_w = jnp.exp(m - peak)
        local_w = jnp.exp(local_max - peak)
        back_w = jnp.exp(back_max - peak) * back_sum
        merged = (
            acc * page_w
            + head_cols(la_ref, g) * local_w
            + head_cols(bo_ref, g).astype(jnp.float32) * back_w
        )
        total = l * page_w + local_sum * local_w + back_w
        o_ref[:, g * HEAD_DIM:(g + 1) * HEAD_DIM] = (merged / total).astype(o_ref.dtype)


def heads_per_step(head_count):
    for group in (4, 2):
        if head_count % group == 0:
            return group
    return 1


def head_specs(span, block_count, page_size, group):
    cols = group * HEAD_DIM
    col_spec = pl.BlockSpec((span, cols), lambda h: (0, h))
    stat_spec = pl.BlockSpec((group, span, 2), lambda h: (h, 0, 0))
    page_specs = [
        pl.BlockSpec((block_count, None, page_size, cols), lambda h: (0, 0, 0, h)),
        pl.BlockSpec((block_count, None, page_size, cols), lambda h: (0, 1, 0, h)),
        pl.BlockSpec((1, block_count * page_size), lambda h: (0, 0)),
    ]
    return col_spec, stat_spec, page_specs


def local_attend(query_rot, key_rot, values):
    span, width = query_rot.shape
    head_count = width // HEAD_DIM
    group = heads_per_step(head_count)
    col_spec, stat_spec, _ = head_specs(span, 1, 1, group)
    return pl.pallas_call(
        local_kernel,
        grid=(head_count // group,),
        in_specs=[col_spec, col_spec, col_spec],
        out_specs=[col_spec, stat_spec],
        out_shape=[
            jax.ShapeDtypeStruct((span, width), jnp.float32),
            jax.ShapeDtypeStruct((head_count, span, 2), jnp.float32),
        ],
    )(query_rot, key_rot, values)


def far_attend(key_ok, query_rot, incoming):
    span, width = query_rot.shape
    head_count = width // HEAD_DIM
    group = heads_per_step(head_count)
    col_spec, stat_spec, page_specs = head_specs(span, incoming.shape[0], incoming.shape[2], group)
    return pl.pallas_call(
        far_kernel,
        grid=(head_count // group,),
        in_specs=[col_spec] + page_specs,
        out_specs=[col_spec, stat_spec],
        out_shape=[
            jax.ShapeDtypeStruct((span, width), jnp.bfloat16),
            jax.ShapeDtypeStruct((head_count, span, 2), jnp.float32),
        ],
    )(query_rot, incoming, incoming, key_ok)


def near_attend(key_ok, query_rot, incoming, local_acc, local_stats, back_out, back_stats):
    span, width = query_rot.shape
    head_count = width // HEAD_DIM
    group = heads_per_step(head_count)
    col_spec, stat_spec, page_specs = head_specs(span, incoming.shape[0], incoming.shape[2], group)
    return pl.pallas_call(
        near_kernel,
        grid=(head_count // group,),
        in_specs=[col_spec] + page_specs + [col_spec, stat_spec, col_spec, stat_spec],
        out_specs=col_spec,
        out_shape=jax.ShapeDtypeStruct((span, width), jnp.bfloat16),
    )(query_rot, incoming, incoming, key_ok, local_acc, local_stats, back_out, back_stats)


def projection_kernel(*refs):
    count = (len(refs) - 2) // 2
    total = refs[2 * count][...].astype(jnp.float32)
    for j in range(count):
        total = total + jnp.dot(refs[j][...], refs[count + j][...], preferred_element_type=jnp.float32)
    refs[-1][...] = total.astype(refs[-1].dtype)


def project(parts, weights, bias):
    span, rows = parts[0].shape
    out_cols = weights[0].shape[1]
    block = 1024 if out_cols % 1024 == 0 else out_cols
    a_spec = pl.BlockSpec((span, rows), lambda c: (0, 0))
    w_spec = pl.BlockSpec((rows, block), lambda c: (0, c))
    b_spec = pl.BlockSpec((1, block), lambda c: (0, c))
    return pl.pallas_call(
        projection_kernel,
        grid=(out_cols // block,),
        in_specs=[a_spec] * len(parts) + [w_spec] * len(weights) + [b_spec],
        out_specs=pl.BlockSpec((span, block), lambda c: (0, c)),
        out_shape=jax.ShapeDtypeStruct((span, out_cols), jnp.bfloat16),
    )(*parts, *weights, bias.reshape(1, out_cols))


def pick_pages(kv_pages, ids):
    ids = jnp.clip(ids, 0, kv_pages.shape[0] - 1)
    return jnp.stack(
        [lax.dynamic_index_in_dim(kv_pages, ids[i], 0, keepdims=False) for i in range(ids.shape[0])]
    )


def usable_keys(page_table, request, length, source_base, source_count, page_count, page_size):
    row = lax.dynamic_index_in_dim(page_table, request, 0, keepdims=False)
    row_owner = jnp.where(row >= 0, row // page_count, -1)
    sources = source_base + jnp.arange(source_count, dtype=jnp.int32)
    slot_ids = jnp.arange(row.shape[0], dtype=jnp.int32)
    matches = row_owner[None, :] == sources[:, None]
    present = jnp.any(matches, axis=1)
    slot_of = jnp.sum(jnp.where(matches, slot_ids[None, :], 0), axis=1)
    nvalid = jnp.where(present, jnp.clip(length - slot_of * page_size, 0, page_size), 0)
    within = jnp.arange(page_size, dtype=jnp.int32)
    return (within[None, :] < nvalid[:, None]).astype(jnp.int32).reshape(1, source_count * page_size)


def on_device(new_queries, new_keys, new_values, kv_pages, page_table, cache_len, w_out, out_bias):
    half = lax.axis_index("half")
    sub = lax.axis_index("sub")
    sub_count = lax.axis_size("sub")
    tp_index = lax.axis_index("tp")
    tp_count = lax.axis_size("tp")
    own_index = half * sub_count + sub
    partner = (1 - half) * sub_count + sub
    span_len = new_queries.shape[0]
    width = new_queries.shape[1]
    head_count = width // HEAD_DIM
    page_count = kv_pages.shape[0]
    page_size = kv_pages.shape[2]
    out_cols = w_out.shape[1] // tp_count
    swap = [(0, 1), (1, 0)]

    w_recv = []
    for shift in range(1, tp_count):
        target = (tp_index + shift) % tp_count
        piece = lax.dynamic_slice_in_dim(w_out, target * out_cols, out_cols, axis=1)
        perm = [(i, (i + shift) % tp_count) for i in range(tp_count)]
        w_recv.append(lax.ppermute(piece, "tp", perm))
    w_mine = lax.dynamic_slice_in_dim(w_out, tp_index * out_cols, out_cols, axis=1)

    owners = jnp.where(page_table >= 0, page_table // page_count, -1)
    held_here = owners == own_index
    local_page = jnp.sum(jnp.where(held_here, page_table - own_index * page_count, 0), axis=1)
    dest = jnp.arange(sub_count, dtype=jnp.int32)
    own_length = lax.dynamic_index_in_dim(cache_len, own_index, 0, keepdims=False)
    partner_length = lax.dynamic_index_in_dim(cache_len, partner, 0, keepdims=False)
    positions = own_length + jnp.arange(span_len, dtype=jnp.int32)
    query_rot = rotate_rows(new_queries, positions)
    partner_query = lax.ppermute(query_rot, "half", swap)

    far_pages = pick_pages(kv_pages, jnp.take(local_page, (1 - half) * sub_count + dest))
    far_incoming = lax.all_to_all(far_pages, "sub", split_axis=0, concat_axis=0, tiled=True)
    near_pages = pick_pages(kv_pages, jnp.take(local_page, half * sub_count + dest))
    partner_query, near_pages = lax.optimization_barrier((partner_query, near_pages))
    near_incoming = lax.all_to_all(near_pages, "sub", split_axis=0, concat_axis=0, tiled=True)
    key_rot = rotate_rows(new_keys, positions)

    source_base = half * sub_count
    ok_own = usable_keys(page_table, own_index, own_length, source_base, sub_count, page_count, page_size)
    ok_partner = usable_keys(page_table, partner, partner_length, source_base, sub_count, page_count, page_size)

    local_acc, local_stats = local_attend(query_rot, key_rot, new_values)
    far_out, far_stats = far_attend(ok_partner, partner_query, far_incoming)
    back_out = lax.ppermute(far_out, "half", swap)
    back_stats = lax.ppermute(far_stats, "half", swap)
    attended = near_attend(
        ok_own, query_rot, near_incoming, local_acc, local_stats, back_out, back_stats
    )

    parts = [attended]
    for shift in range(1, tp_count):
        perm = [(i, (i + shift) % tp_count) for i in range(tp_count)]
        parts.append(lax.ppermute(attended, "tp", perm))
    return project(parts, [w_mine] + w_recv, out_bias)


def solution(mesh):
    req_count = mesh.shape["req"]
    tp_count = mesh.shape["tp"]
    assert tuple(mesh.axis_names) == ("req", "tp")
    devices = mesh.devices.reshape(2, req_count // 2, tp_count)
    split_mesh = jax.sharding.Mesh(devices, ("half", "sub", "tp"))
    rows = ("half", "sub")
    return jax.shard_map(
        on_device,
        mesh=split_mesh,
        in_specs=(
            P(rows, "tp"),
            P(rows, "tp"),
            P(rows, "tp"),
            P(rows, None, None, "tp"),
            P(),
            P(),
            P("tp", None),
            P("tp"),
        ),
        out_specs=P(rows, "tp"),
        check_vma=False,
    )
```

```python
import math
from functools import partial

import jax
import jax.numpy as jnp
from jax import lax
from jax.experimental import pallas as pl
from jax.experimental.pallas import tpu as pltpu
from jax.sharding import PartitionSpec as P

HEAD_DIM = 128
ROT = 32


NEG_FILL = -1e30


def rotate_rows(block, positions):
    row_count = block.shape[0]
    shaped = block.astype(jnp.float32).reshape(row_count, -1, HEAD_DIM)
    half_rot = ROT // 2
    frequency = 10000.0 ** (-2.0 * jnp.arange(half_rot, dtype=jnp.float32) / ROT)
    angles = positions.astype(jnp.float32)[:, None] * frequency[None, :]
    cosine = jnp.cos(angles)[:, None, :]
    sines = jnp.sin(angles)[:, None, :]
    first_half = shaped[:, :, :half_rot]
    second_half = shaped[:, :, half_rot:ROT]
    turned = jnp.concatenate(
        [
            first_half * cosine - second_half * sines,
            second_half * cosine + first_half * sines,
            shaped[:, :, ROT:],
        ],
        axis=2,
    )
    return turned.reshape(row_count, -1).astype(jnp.bfloat16)


SCORE_DIMS = (((1,), (1,)), ((), ()))


def head_cols(ref, g):
    return ref[..., g * HEAD_DIM:(g + 1) * HEAD_DIM]


def local_kernel(q_ref, kl_ref, vl_ref, acc_ref, st_ref):
    score_scale = 1.0 / math.sqrt(HEAD_DIM)
    for g in range(st_ref.shape[0]):
        q = head_cols(q_ref, g)
        span = q.shape[0]
        s = lax.dot_general(q, head_cols(kl_ref, g), SCORE_DIMS, preferred_element_type=jnp.float32) * score_scale
        row = lax.broadcasted_iota(jnp.int32, (span, span), 0)
        col = lax.broadcasted_iota(jnp.int32, (span, span), 1)
        s = jnp.where(row >= col, s, NEG_FILL)
        m = jnp.max(s, axis=1, keepdims=True)
        p = jnp.exp(s - m)
        acc_ref[:, g * HEAD_DIM:(g + 1) * HEAD_DIM] = jnp.dot(
            p.astype(jnp.bfloat16), head_cols(vl_ref, g), preferred_element_type=jnp.float32
        )
        st_ref[g, :, 0:1] = m
        st_ref[g, :, 1:2] = jnp.sum(p, axis=1, keepdims=True)


def head_pages(kp_ref, vp_ref, g):
    block_count, page_size, _ = kp_ref.shape
    keys = head_cols(kp_ref, g).reshape(block_count * page_size, HEAD_DIM)
    values = head_cols(vp_ref, g).reshape(block_count * page_size, HEAD_DIM)
    return keys, values


def page_partial(q, keys_p, values_p, ok):
    score_scale = 1.0 / math.sqrt(HEAD_DIM)
    s = lax.dot_general(q, keys_p, SCORE_DIMS, preferred_element_type=jnp.float32) * score_scale
    s = jnp.where(ok > 0, s, NEG_FILL)
    m = jnp.max(s, axis=1, keepdims=True)
    p = jnp.exp(s - m)
    l = jnp.sum(p, axis=1, keepdims=True)
    acc = jnp.dot(p.astype(jnp.bfloat16), values_p, preferred_element_type=jnp.float32)
    return m, l, acc


def far_kernel(q_ref, kp_ref, vp_ref, ok_ref, o_ref, st_ref):
    ok = ok_ref[...]
    for g in range(st_ref.shape[0]):
        keys, values = head_pages(kp_ref, vp_ref, g)
        m, l, acc = page_partial(head_cols(q_ref, g), keys, values, ok)
        o_ref[:, g * HEAD_DIM:(g + 1) * HEAD_DIM] = (acc / l).astype(o_ref.dtype)
        st_ref[g, :, 0:1] = m
        st_ref[g, :, 1:2] = l


def near_kernel(q_ref, kp_ref, vp_ref, ok_ref, la_ref, lst_ref, bo_ref, bst_ref, o_ref):
    ok = ok_ref[...]
    for g in range(lst_ref.shape[0]):
        keys, values = head_pages(kp_ref, vp_ref, g)
        m, l, acc = page_partial(head_cols(q_ref, g), keys, values, ok)
        local = lst_ref[g]
        local_max = local[:, 0:1]
        local_sum = local[:, 1:2]
        back = bst_ref[g]
        back_max = back[:, 0:1]
        back_sum = back[:, 1:2]
        peak = jnp.maximum(jnp.maximum(m, local_max), back_max)
        page_w = jnp.exp(m - peak)
        local_w = jnp.exp(local_max - peak)
        back_w = jnp.exp(back_max - peak) * back_sum
        merged = (
            acc * page_w
            + head_cols(la_ref, g) * local_w
            + head_cols(bo_ref, g).astype(jnp.float32) * back_w
        )
        total = l * page_w + local_sum * local_w + back_w
        o_ref[:, g * HEAD_DIM:(g + 1) * HEAD_DIM] = (merged / total).astype(o_ref.dtype)


def heads_per_step(head_count):
    for group in (4, 2):
        if head_count % group == 0:
            return group
    return 1


def head_specs(span, block_count, page_size, group):
    cols = group * HEAD_DIM
    col_spec = pl.BlockSpec((span, cols), lambda h: (0, h))
    stat_spec = pl.BlockSpec((group, span, 2), lambda h: (h, 0, 0))
    page_specs = [
        pl.BlockSpec((block_count, None, page_size, cols), lambda h: (0, 0, 0, h)),
        pl.BlockSpec((block_count, None, page_size, cols), lambda h: (0, 1, 0, h)),
        pl.BlockSpec((1, block_count * page_size), lambda h: (0, 0)),
    ]
    return col_spec, stat_spec, page_specs


def local_attend(query_rot, key_rot, values):
    span, width = query_rot.shape
    head_count = width // HEAD_DIM
    group = heads_per_step(head_count)
    col_spec, stat_spec, _ = head_specs(span, 1, 1, group)
    return pl.pallas_call(
        local_kernel,
        grid=(head_count // group,),
        in_specs=[col_spec, col_spec, col_spec],
        out_specs=[col_spec, stat_spec],
        out_shape=[
            jax.ShapeDtypeStruct((span, width), jnp.float32),
            jax.ShapeDtypeStruct((head_count, span, 2), jnp.float32),
        ],
    )(query_rot, key_rot, values)


def far_attend(key_ok, query_rot, incoming):
    span, width = query_rot.shape
    head_count = width // HEAD_DIM
    group = heads_per_step(head_count)
    col_spec, stat_spec, page_specs = head_specs(span, incoming.shape[0], incoming.shape[2], group)
    return pl.pallas_call(
        far_kernel,
        grid=(head_count // group,),
        in_specs=[col_spec] + page_specs,
        out_specs=[col_spec, stat_spec],
        out_shape=[
            jax.ShapeDtypeStruct((span, width), jnp.bfloat16),
            jax.ShapeDtypeStruct((head_count, span, 2), jnp.float32),
        ],
    )(query_rot, incoming, incoming, key_ok)


def near_attend(key_ok, query_rot, incoming, local_acc, local_stats, back_out, back_stats):
    span, width = query_rot.shape
    head_count = width // HEAD_DIM
    group = heads_per_step(head_count)
    col_spec, stat_spec, page_specs = head_specs(span, incoming.shape[0], incoming.shape[2], group)
    return pl.pallas_call(
        near_kernel,
        grid=(head_count // group,),
        in_specs=[col_spec] + page_specs + [col_spec, stat_spec, col_spec, stat_spec],
        out_specs=col_spec,
        out_shape=jax.ShapeDtypeStruct((span, width), jnp.bfloat16),
    )(query_rot, incoming, incoming, key_ok, local_acc, local_stats, back_out, back_stats)


def projection_kernel(*refs, count):
    total = refs[2 * count][...].astype(jnp.float32)
    for j in range(count):
        total = total + jnp.dot(refs[j][...], refs[count + j][...], preferred_element_type=jnp.float32)
    refs[-1][...] = total.astype(refs[-1].dtype)


def project(parts, weights, base, out_dtype):
    span, rows = parts[0].shape
    out_cols = weights[0].shape[1]
    block = 1024 if out_cols % 1024 == 0 else out_cols
    a_spec = pl.BlockSpec((span, rows), lambda c: (0, 0))
    w_spec = pl.BlockSpec((rows, block), lambda c: (0, c))
    base_spec = pl.BlockSpec((base.shape[0], block), lambda c: (0, c))
    return pl.pallas_call(
        partial(projection_kernel, count=len(parts)),
        grid=(out_cols // block,),
        in_specs=[a_spec] * len(parts) + [w_spec] * len(weights) + [base_spec],
        out_specs=pl.BlockSpec((span, block), lambda c: (0, c)),
        out_shape=jax.ShapeDtypeStruct((span, out_cols), out_dtype),
    )(*parts, *weights, base)


def usable_keys(page_table, request, length, source_base, source_count, page_count, page_size):
    row = lax.dynamic_index_in_dim(page_table, request, 0, keepdims=False)
    row_owner = jnp.where(row >= 0, row // page_count, -1)
    sources = source_base + jnp.arange(source_count, dtype=jnp.int32)
    slot_ids = jnp.arange(row.shape[0], dtype=jnp.int32)
    matches = row_owner[None, :] == sources[:, None]
    present = jnp.any(matches, axis=1)
    slot_of = jnp.sum(jnp.where(matches, slot_ids[None, :], 0), axis=1)
    nvalid = jnp.where(present, jnp.clip(length - slot_of * page_size, 0, page_size), 0)
    within = jnp.arange(page_size, dtype=jnp.int32)
    return (within[None, :] < nvalid[:, None]).astype(jnp.int32).reshape(1, source_count * page_size)


def on_device(new_queries, new_keys, new_values, kv_pages, page_table, cache_len, w_out, out_bias):
    half = lax.axis_index("half")
    sub = lax.axis_index("sub")
    sub_count = lax.axis_size("sub")
    tp_index = lax.axis_index("tp")
    tp_count = lax.axis_size("tp")
    own_index = half * sub_count + sub
    partner = (1 - half) * sub_count + sub
    span_len = new_queries.shape[0]
    width = new_queries.shape[1]
    head_count = width // HEAD_DIM
    page_count = kv_pages.shape[0]
    page_size = kv_pages.shape[2]
    out_cols = w_out.shape[1] // tp_count
    swap = [(0, 1), (1, 0)]

    w_recv = []
    for shift in range(1, tp_count):
        target = (tp_index + shift) % tp_count
        piece = lax.dynamic_slice_in_dim(w_out, target * out_cols, out_cols, axis=1)
        perm = [(i, (i + shift) % tp_count) for i in range(tp_count)]
        w_recv.append(lax.ppermute(piece, "tp", perm))
    w_mine = lax.dynamic_slice_in_dim(w_out, tp_index * out_cols, out_cols, axis=1)

    owners = jnp.where(page_table >= 0, page_table // page_count, -1)
    held_here = owners == own_index
    local_page = jnp.sum(jnp.where(held_here, page_table - own_index * page_count, 0), axis=1)
    dest = jnp.arange(sub_count, dtype=jnp.int32)
    own_length = lax.dynamic_index_in_dim(cache_len, own_index, 0, keepdims=False)
    partner_length = lax.dynamic_index_in_dim(cache_len, partner, 0, keepdims=False)
    positions = own_length + jnp.arange(span_len, dtype=jnp.int32)
    query_rot = rotate_rows(new_queries, positions)
    partner_query = lax.ppermute(query_rot, "half", swap)

    far_pages = jnp.take(kv_pages, jnp.take(local_page, (1 - half) * sub_count + dest), axis=0, mode="clip")
    far_incoming = lax.all_to_all(far_pages, "sub", split_axis=0, concat_axis=0, tiled=True)
    near_pages = jnp.take(kv_pages, jnp.take(local_page, half * sub_count + dest), axis=0, mode="clip")
    partner_query, near_pages = lax.optimization_barrier((partner_query, near_pages))
    near_incoming = lax.all_to_all(near_pages, "sub", split_axis=0, concat_axis=0, tiled=True)
    key_rot = rotate_rows(new_keys, positions)

    source_base = half * sub_count
    ok_own = usable_keys(page_table, own_index, own_length, source_base, sub_count, page_count, page_size)
    ok_partner = usable_keys(page_table, partner, partner_length, source_base, sub_count, page_count, page_size)

    local_acc, local_stats = local_attend(query_rot, key_rot, new_values)
    far_out, far_stats = far_attend(ok_partner, partner_query, far_incoming)
    back_out = lax.ppermute(far_out, "half", swap)
    back_stats = lax.ppermute(far_stats, "half", swap)
    attended = near_attend(
        ok_own, query_rot, near_incoming, local_acc, local_stats, back_out, back_stats
    )

    parts = [attended]
    for shift in range(1, tp_count):
        perm = [(i, (i + shift) % tp_count) for i in range(tp_count)]
        parts.append(lax.ppermute(attended, "tp", perm))
    local_sum = project([attended], [w_mine], out_bias.reshape(1, -1), jnp.float32)
    return project(parts[1:], w_recv, local_sum, jnp.bfloat16)


def solution(mesh):
    req_count = mesh.shape["req"]
    tp_count = mesh.shape["tp"]
    assert tuple(mesh.axis_names) == ("req", "tp")
    devices = mesh.devices.reshape(2, req_count // 2, tp_count)
    split_mesh = jax.sharding.Mesh(devices, ("half", "sub", "tp"))
    rows = ("half", "sub")
    return jax.shard_map(
        on_device,
        mesh=split_mesh,
        in_specs=(
            P(rows, "tp"),
            P(rows, "tp"),
            P(rows, "tp"),
            P(rows, None, None, "tp"),
            P(),
            P(),
            P("tp", None),
            P("tp"),
        ),
        out_specs=P(rows, "tp"),
        check_vma=False,
    )
```

```python
import math
from functools import partial

import jax
import jax.numpy as jnp
from jax import lax
from jax.experimental import pallas as pl
from jax.experimental.pallas import tpu as pltpu
from jax.sharding import PartitionSpec as P

HEAD_DIM = 128
ROT = 32


NEG_FILL = -1e30


def rotate_rows(block, positions):
    row_count = block.shape[0]
    shaped = block.astype(jnp.float32).reshape(row_count, -1, HEAD_DIM)
    half_rot = ROT // 2
    frequency = 10000.0 ** (-2.0 * jnp.arange(half_rot, dtype=jnp.float32) / ROT)
    angles = positions.astype(jnp.float32)[:, None] * frequency[None, :]
    cosine = jnp.cos(angles)[:, None, :]
    sines = jnp.sin(angles)[:, None, :]
    first_half = shaped[:, :, :half_rot]
    second_half = shaped[:, :, half_rot:ROT]
    turned = jnp.concatenate(
        [
            first_half * cosine - second_half * sines,
            second_half * cosine + first_half * sines,
            shaped[:, :, ROT:],
        ],
        axis=2,
    )
    return turned.reshape(row_count, -1).astype(jnp.bfloat16)


SCORE_DIMS = (((1,), (1,)), ((), ()))


def head_cols(ref, g):
    return ref[..., g * HEAD_DIM:(g + 1) * HEAD_DIM]


def local_kernel(q_ref, kl_ref, vl_ref, acc_ref, st_ref):
    score_scale = 1.0 / math.sqrt(HEAD_DIM)
    for g in range(st_ref.shape[0]):
        q = head_cols(q_ref, g)
        span = q.shape[0]
        s = lax.dot_general(q, head_cols(kl_ref, g), SCORE_DIMS, preferred_element_type=jnp.float32) * score_scale
        row = lax.broadcasted_iota(jnp.int32, (span, span), 0)
        col = lax.broadcasted_iota(jnp.int32, (span, span), 1)
        s = jnp.where(row >= col, s, NEG_FILL)
        m = jnp.max(s, axis=1, keepdims=True)
        p = jnp.exp(s - m)
        acc_ref[:, g * HEAD_DIM:(g + 1) * HEAD_DIM] = jnp.dot(
            p.astype(jnp.bfloat16), head_cols(vl_ref, g), preferred_element_type=jnp.float32
        )
        st_ref[g, :, 0:1] = m
        st_ref[g, :, 1:2] = jnp.sum(p, axis=1, keepdims=True)


def head_pages(kp_ref, vp_ref, g):
    block_count, page_size, _ = kp_ref.shape
    keys = head_cols(kp_ref, g).reshape(block_count * page_size, HEAD_DIM)
    values = head_cols(vp_ref, g).reshape(block_count * page_size, HEAD_DIM)
    return keys, values


def page_partial(q, keys_p, values_p, ok):
    score_scale = 1.0 / math.sqrt(HEAD_DIM)
    s = lax.dot_general(q, keys_p, SCORE_DIMS, preferred_element_type=jnp.float32) * score_scale + ok
    m = jnp.max(s, axis=1, keepdims=True)
    p = jnp.exp(s - m)
    l = jnp.sum(p, axis=1, keepdims=True)
    acc = jnp.dot(p.astype(jnp.bfloat16), values_p, preferred_element_type=jnp.float32)
    return m, l, acc


def far_kernel(q_ref, kp_ref, vp_ref, ok_ref, o_ref, st_ref):
    ok = ok_ref[...]
    for g in range(st_ref.shape[0]):
        keys, values = head_pages(kp_ref, vp_ref, g)
        m, l, acc = page_partial(head_cols(q_ref, g), keys, values, ok)
        o_ref[:, g * HEAD_DIM:(g + 1) * HEAD_DIM] = (acc / l).astype(o_ref.dtype)
        st_ref[g, :, 0:1] = m
        st_ref[g, :, 1:2] = l


def near_kernel(q_ref, kp_ref, vp_ref, ok_ref, la_ref, lst_ref, bo_ref, bst_ref, o_ref):
    ok = ok_ref[...]
    for g in range(lst_ref.shape[0]):
        keys, values = head_pages(kp_ref, vp_ref, g)
        m, l, acc = page_partial(head_cols(q_ref, g), keys, values, ok)
        local = lst_ref[g]
        local_max = local[:, 0:1]
        local_sum = local[:, 1:2]
        back = bst_ref[g]
        back_max = back[:, 0:1]
        back_sum = back[:, 1:2]
        peak = jnp.maximum(jnp.maximum(m, local_max), back_max)
        page_w = jnp.exp(m - peak)
        local_w = jnp.exp(local_max - peak)
        back_w = jnp.exp(back_max - peak) * back_sum
        merged = (
            acc * page_w
            + head_cols(la_ref, g) * local_w
            + head_cols(bo_ref, g).astype(jnp.float32) * back_w
        )
        total = l * page_w + local_sum * local_w + back_w
        o_ref[:, g * HEAD_DIM:(g + 1) * HEAD_DIM] = (merged / total).astype(o_ref.dtype)


def heads_per_step(head_count):
    for group in (4, 2):
        if head_count % group == 0:
            return group
    return 1


def head_specs(span, block_count, page_size, group):
    cols = group * HEAD_DIM
    col_spec = pl.BlockSpec((span, cols), lambda h: (0, h))
    stat_spec = pl.BlockSpec((group, span, 2), lambda h: (h, 0, 0))
    page_specs = [
        pl.BlockSpec((block_count, None, page_size, cols), lambda h: (0, 0, 0, h)),
        pl.BlockSpec((block_count, None, page_size, cols), lambda h: (0, 1, 0, h)),
        pl.BlockSpec((1, block_count * page_size), lambda h: (0, 0)),
    ]
    return col_spec, stat_spec, page_specs


def local_attend(query_rot, key_rot, values):
    span, width = query_rot.shape
    head_count = width // HEAD_DIM
    group = heads_per_step(head_count)
    col_spec, stat_spec, _ = head_specs(span, 1, 1, group)
    return pl.pallas_call(
        local_kernel,
        grid=(head_count // group,),
        in_specs=[col_spec, col_spec, col_spec],
        out_specs=[col_spec, stat_spec],
        out_shape=[
            jax.ShapeDtypeStruct((span, width), jnp.float32),
            jax.ShapeDtypeStruct((head_count, span, 2), jnp.float32),
        ],
    )(query_rot, key_rot, values)


def far_attend(key_ok, query_rot, incoming):
    span, width = query_rot.shape
    head_count = width // HEAD_DIM
    group = heads_per_step(head_count)
    col_spec, stat_spec, page_specs = head_specs(span, incoming.shape[0], incoming.shape[2], group)
    return pl.pallas_call(
        far_kernel,
        grid=(head_count // group,),
        in_specs=[col_spec] + page_specs,
        out_specs=[col_spec, stat_spec],
        out_shape=[
            jax.ShapeDtypeStruct((span, width), jnp.bfloat16),
            jax.ShapeDtypeStruct((head_count, span, 2), jnp.float32),
        ],
    )(query_rot, incoming, incoming, key_ok)


def near_attend(key_ok, query_rot, incoming, local_acc, local_stats, back_out, back_stats):
    span, width = query_rot.shape
    head_count = width // HEAD_DIM
    group = heads_per_step(head_count)
    col_spec, stat_spec, page_specs = head_specs(span, incoming.shape[0], incoming.shape[2], group)
    return pl.pallas_call(
        near_kernel,
        grid=(head_count // group,),
        in_specs=[col_spec] + page_specs + [col_spec, stat_spec, col_spec, stat_spec],
        out_specs=col_spec,
        out_shape=jax.ShapeDtypeStruct((span, width), jnp.bfloat16),
    )(query_rot, incoming, incoming, key_ok, local_acc, local_stats, back_out, back_stats)


def projection_kernel(*refs):
    count = (len(refs) - 2) // 2
    total = refs[2 * count][...].astype(jnp.float32)
    for j in range(count):
        total = total + jnp.dot(refs[j][...], refs[count + j][...], preferred_element_type=jnp.float32)
    refs[-1][...] = total.astype(refs[-1].dtype)


def project(parts, weights, bias):
    span, rows = parts[0].shape
    out_cols = weights[0].shape[1]
    block = 1024 if out_cols % 1024 == 0 else out_cols
    a_spec = pl.BlockSpec((span, rows), lambda c: (0, 0))
    w_spec = pl.BlockSpec((rows, block), lambda c: (0, c))
    b_spec = pl.BlockSpec((1, block), lambda c: (0, c))
    return pl.pallas_call(
        projection_kernel,
        grid=(out_cols // block,),
        in_specs=[a_spec] * len(parts) + [w_spec] * len(weights) + [b_spec],
        out_specs=pl.BlockSpec((span, block), lambda c: (0, c)),
        out_shape=jax.ShapeDtypeStruct((span, out_cols), jnp.bfloat16),
    )(*parts, *weights, bias.reshape(1, out_cols))


def usable_keys(page_table, request, length, source_base, source_count, page_count, page_size):
    row = lax.dynamic_index_in_dim(page_table, request, 0, keepdims=False)
    row_owner = jnp.where(row >= 0, row // page_count, -1)
    sources = source_base + jnp.arange(source_count, dtype=jnp.int32)
    slot_ids = jnp.arange(row.shape[0], dtype=jnp.int32)
    matches = row_owner[None, :] == sources[:, None]
    present = jnp.any(matches, axis=1)
    slot_of = jnp.sum(jnp.where(matches, slot_ids[None, :], 0), axis=1)
    nvalid = jnp.where(present, jnp.clip(length - slot_of * page_size, 0, page_size), 0)
    within = jnp.arange(page_size, dtype=jnp.int32)
    usable = within[None, :] < nvalid[:, None]
    return jnp.where(usable, 0.0, NEG_FILL).astype(jnp.float32).reshape(1, source_count * page_size)


def on_device(new_queries, new_keys, new_values, kv_pages, page_table, cache_len, w_out, out_bias):
    half = lax.axis_index("half")
    sub = lax.axis_index("sub")
    sub_count = lax.axis_size("sub")
    tp_index = lax.axis_index("tp")
    tp_count = lax.axis_size("tp")
    own_index = half * sub_count + sub
    partner = (1 - half) * sub_count + sub
    span_len = new_queries.shape[0]
    width = new_queries.shape[1]
    head_count = width // HEAD_DIM
    page_count = kv_pages.shape[0]
    page_size = kv_pages.shape[2]
    out_cols = w_out.shape[1] // tp_count
    swap = [(0, 1), (1, 0)]

    w_recv = []
    for shift in range(1, tp_count):
        target = (tp_index + shift) % tp_count
        piece = lax.dynamic_slice_in_dim(w_out, target * out_cols, out_cols, axis=1)
        perm = [(i, (i + shift) % tp_count) for i in range(tp_count)]
        w_recv.append(lax.ppermute(piece, "tp", perm))
    w_mine = lax.dynamic_slice_in_dim(w_out, tp_index * out_cols, out_cols, axis=1)

    owners = jnp.where(page_table >= 0, page_table // page_count, -1)
    held_here = owners == own_index
    local_page = jnp.sum(jnp.where(held_here, page_table - own_index * page_count, 0), axis=1)
    dest = jnp.arange(sub_count, dtype=jnp.int32)
    own_length = lax.dynamic_index_in_dim(cache_len, own_index, 0, keepdims=False)
    partner_length = lax.dynamic_index_in_dim(cache_len, partner, 0, keepdims=False)
    positions = own_length + jnp.arange(span_len, dtype=jnp.int32)
    query_rot = rotate_rows(new_queries, positions)
    partner_query = lax.ppermute(query_rot, "half", swap)

    far_pages = jnp.take(kv_pages, jnp.take(local_page, (1 - half) * sub_count + dest), axis=0, mode="clip")
    far_incoming = lax.all_to_all(far_pages, "sub", split_axis=0, concat_axis=0, tiled=True)
    near_pages = jnp.take(kv_pages, jnp.take(local_page, half * sub_count + dest), axis=0, mode="clip")
    partner_query, near_pages = lax.optimization_barrier((partner_query, near_pages))
    near_incoming = lax.all_to_all(near_pages, "sub", split_axis=0, concat_axis=0, tiled=True)
    key_rot = rotate_rows(new_keys, positions)

    source_base = half * sub_count
    ok_own = usable_keys(page_table, own_index, own_length, source_base, sub_count, page_count, page_size)
    ok_partner = usable_keys(page_table, partner, partner_length, source_base, sub_count, page_count, page_size)

    local_acc, local_stats = local_attend(query_rot, key_rot, new_values)
    far_out, far_stats = far_attend(ok_partner, partner_query, far_incoming)
    back_out = lax.ppermute(far_out, "half", swap)
    back_stats = lax.ppermute(far_stats, "half", swap)
    attended = near_attend(
        ok_own, query_rot, near_incoming, local_acc, local_stats, back_out, back_stats
    )

    parts = [attended]
    for shift in range(1, tp_count):
        perm = [(i, (i + shift) % tp_count) for i in range(tp_count)]
        parts.append(lax.ppermute(attended, "tp", perm))
    return project(parts, [w_mine] + w_recv, out_bias)


def solution(mesh):
    req_count = mesh.shape["req"]
    tp_count = mesh.shape["tp"]
    assert tuple(mesh.axis_names) == ("req", "tp")
    devices = mesh.devices.reshape(2, req_count // 2, tp_count)
    split_mesh = jax.sharding.Mesh(devices, ("half", "sub", "tp"))
    rows = ("half", "sub")
    return jax.shard_map(
        on_device,
        mesh=split_mesh,
        in_specs=(
            P(rows, "tp"),
            P(rows, "tp"),
            P(rows, "tp"),
            P(rows, None, None, "tp"),
            P(),
            P(),
            P("tp", None),
            P("tp"),
        ),
        out_specs=P(rows, "tp"),
        check_vma=False,
    )
```

```python
import math
from functools import partial

import jax
import jax.numpy as jnp
from jax import lax
from jax.experimental import pallas as pl
from jax.experimental.pallas import tpu as pltpu
from jax.sharding import PartitionSpec as P

HEAD_DIM = 128
ROT = 32


NEG_FILL = -1e30


def rotate_rows(block, positions):
    row_count = block.shape[0]
    shaped = block.astype(jnp.float32).reshape(row_count, -1, HEAD_DIM)
    half_rot = ROT // 2
    frequency = 10000.0 ** (-2.0 * jnp.arange(half_rot, dtype=jnp.float32) / ROT)
    angles = positions.astype(jnp.float32)[:, None] * frequency[None, :]
    cosine = jnp.cos(angles)[:, None, :]
    sines = jnp.sin(angles)[:, None, :]
    first_half = shaped[:, :, :half_rot]
    second_half = shaped[:, :, half_rot:ROT]
    turned = jnp.concatenate(
        [
            first_half * cosine - second_half * sines,
            second_half * cosine + first_half * sines,
            shaped[:, :, ROT:],
        ],
        axis=2,
    )
    return turned.reshape(row_count, -1).astype(jnp.bfloat16)


SCORE_DIMS = (((1,), (1,)), ((), ()))


def head_cols(ref, g):
    return ref[..., g * HEAD_DIM:(g + 1) * HEAD_DIM]


def local_kernel(q_ref, kl_ref, vl_ref, acc_ref, st_ref):
    score_scale = 1.0 / math.sqrt(HEAD_DIM)
    for g in range(st_ref.shape[0]):
        q = head_cols(q_ref, g)
        span = q.shape[0]
        s = lax.dot_general(q, head_cols(kl_ref, g), SCORE_DIMS, preferred_element_type=jnp.float32) * score_scale
        row = lax.broadcasted_iota(jnp.int32, (span, span), 0)
        col = lax.broadcasted_iota(jnp.int32, (span, span), 1)
        s = jnp.where(row >= col, s, NEG_FILL)
        m = jnp.max(s, axis=1, keepdims=True)
        p = jnp.exp(s - m)
        acc_ref[:, g * HEAD_DIM:(g + 1) * HEAD_DIM] = jnp.dot(
            p.astype(jnp.bfloat16), head_cols(vl_ref, g), preferred_element_type=jnp.float32
        )
        st_ref[g, :, 0:1] = m
        st_ref[g, :, 1:2] = jnp.sum(p, axis=1, keepdims=True)


def head_pages(kp_ref, vp_ref, g):
    block_count, page_size, _ = kp_ref.shape
    keys = head_cols(kp_ref, g).reshape(block_count * page_size, HEAD_DIM)
    values = head_cols(vp_ref, g).reshape(block_count * page_size, HEAD_DIM)
    return keys, values


def page_partial(q, keys_p, values_p, ok):
    score_scale = 1.0 / math.sqrt(HEAD_DIM)
    s = lax.dot_general(q, keys_p, SCORE_DIMS, preferred_element_type=jnp.float32) * score_scale + ok
    m = jnp.max(s, axis=1, keepdims=True)
    p = jnp.exp(s - m)
    l = jnp.sum(p, axis=1, keepdims=True)
    acc = jnp.dot(p.astype(jnp.bfloat16), values_p, preferred_element_type=jnp.float32)
    return m, l, acc


def far_kernel(q_ref, kp_ref, vp_ref, ok_ref, o_ref, st_ref):
    ok = ok_ref[...]
    span = q_ref.shape[0]
    lane = lax.broadcasted_iota(jnp.int32, (span, HEAD_DIM), 1)
    packed = jnp.zeros((span, HEAD_DIM), jnp.float32)
    for g in range(st_ref.shape[0] // 2):
        keys, values = head_pages(kp_ref, vp_ref, g)
        m, l, acc = page_partial(head_cols(q_ref, g), keys, values, ok)
        o_ref[:, g * HEAD_DIM:(g + 1) * HEAD_DIM] = (acc / l).astype(o_ref.dtype)
        packed = jnp.where(lane == 2 * g, m, jnp.where(lane == 2 * g + 1, l, packed))
    st_ref[...] = packed.T[: st_ref.shape[0]]


def near_kernel(q_ref, kp_ref, vp_ref, ok_ref, la_ref, lst_ref, bo_ref, bst_ref, o_ref):
    ok = ok_ref[...]
    rows, span = bst_ref.shape
    back = jnp.concatenate([bst_ref[...], jnp.zeros((HEAD_DIM - rows, span), jnp.float32)], axis=0).T
    for g in range(lst_ref.shape[0]):
        keys, values = head_pages(kp_ref, vp_ref, g)
        m, l, acc = page_partial(head_cols(q_ref, g), keys, values, ok)
        local = lst_ref[g]
        local_max = local[:, 0:1]
        local_sum = local[:, 1:2]
        back_max = back[:, 2 * g:2 * g + 1]
        back_sum = back[:, 2 * g + 1:2 * g + 2]
        peak = jnp.maximum(jnp.maximum(m, local_max), back_max)
        page_w = jnp.exp(m - peak)
        local_w = jnp.exp(local_max - peak)
        back_w = jnp.exp(back_max - peak) * back_sum
        merged = (
            acc * page_w
            + head_cols(la_ref, g) * local_w
            + head_cols(bo_ref, g).astype(jnp.float32) * back_w
        )
        total = l * page_w + local_sum * local_w + back_w
        o_ref[:, g * HEAD_DIM:(g + 1) * HEAD_DIM] = (merged / total).astype(o_ref.dtype)


def heads_per_step(head_count):
    for group in (4, 2):
        if head_count % group == 0:
            return group
    return 1


def head_specs(span, block_count, page_size, group):
    cols = group * HEAD_DIM
    col_spec = pl.BlockSpec((span, cols), lambda h: (0, h))
    stat_spec = pl.BlockSpec((group, span, 2), lambda h: (h, 0, 0))
    page_specs = [
        pl.BlockSpec((block_count, None, page_size, cols), lambda h: (0, 0, 0, h)),
        pl.BlockSpec((block_count, None, page_size, cols), lambda h: (0, 1, 0, h)),
        pl.BlockSpec((1, block_count * page_size), lambda h: (0, 0)),
    ]
    return col_spec, stat_spec, page_specs


def local_attend(query_rot, key_rot, values):
    span, width = query_rot.shape
    head_count = width // HEAD_DIM
    group = heads_per_step(head_count)
    col_spec, stat_spec, _ = head_specs(span, 1, 1, group)
    return pl.pallas_call(
        local_kernel,
        grid=(head_count // group,),
        in_specs=[col_spec, col_spec, col_spec],
        out_specs=[col_spec, stat_spec],
        out_shape=[
            jax.ShapeDtypeStruct((span, width), jnp.float32),
            jax.ShapeDtypeStruct((head_count, span, 2), jnp.float32),
        ],
    )(query_rot, key_rot, values)


def far_attend(key_ok, query_rot, incoming):
    span, width = query_rot.shape
    head_count = width // HEAD_DIM
    group = heads_per_step(head_count)
    col_spec, stat_spec, page_specs = head_specs(span, incoming.shape[0], incoming.shape[2], group)
    return pl.pallas_call(
        far_kernel,
        grid=(head_count // group,),
        in_specs=[col_spec] + page_specs,
        out_specs=[col_spec, pl.BlockSpec((2 * group, span), lambda h: (h, 0))],
        out_shape=[
            jax.ShapeDtypeStruct((span, width), jnp.bfloat16),
            jax.ShapeDtypeStruct((2 * head_count, span), jnp.float32),
        ],
    )(query_rot, incoming, incoming, key_ok)


def near_attend(key_ok, query_rot, incoming, local_acc, local_stats, back_out, back_stats):
    span, width = query_rot.shape
    head_count = width // HEAD_DIM
    group = heads_per_step(head_count)
    col_spec, stat_spec, page_specs = head_specs(span, incoming.shape[0], incoming.shape[2], group)
    return pl.pallas_call(
        near_kernel,
        grid=(head_count // group,),
        in_specs=[col_spec] + page_specs + [
            col_spec, stat_spec, col_spec, pl.BlockSpec((2 * group, span), lambda h: (h, 0))
        ],
        out_specs=col_spec,
        out_shape=jax.ShapeDtypeStruct((span, width), jnp.bfloat16),
    )(query_rot, incoming, incoming, key_ok, local_acc, local_stats, back_out, back_stats)


def projection_kernel(*refs):
    count = (len(refs) - 2) // 2
    total = refs[2 * count][...].astype(jnp.float32)
    for j in range(count):
        total = total + jnp.dot(refs[j][...], refs[count + j][...], preferred_element_type=jnp.float32)
    refs[-1][...] = total.astype(refs[-1].dtype)


def project(parts, weights, bias):
    span, rows = parts[0].shape
    out_cols = weights[0].shape[1]
    block = 1024 if out_cols % 1024 == 0 else out_cols
    a_spec = pl.BlockSpec((span, rows), lambda c: (0, 0))
    w_spec = pl.BlockSpec((rows, block), lambda c: (0, c))
    b_spec = pl.BlockSpec((1, block), lambda c: (0, c))
    return pl.pallas_call(
        projection_kernel,
        grid=(out_cols // block,),
        in_specs=[a_spec] * len(parts) + [w_spec] * len(weights) + [b_spec],
        out_specs=pl.BlockSpec((span, block), lambda c: (0, c)),
        out_shape=jax.ShapeDtypeStruct((span, out_cols), jnp.bfloat16),
    )(*parts, *weights, bias.reshape(1, out_cols))


def usable_keys(page_table, request, length, source_base, source_count, page_count, page_size):
    row = lax.dynamic_index_in_dim(page_table, request, 0, keepdims=False)
    row_owner = jnp.where(row >= 0, row // page_count, -1)
    sources = source_base + jnp.arange(source_count, dtype=jnp.int32)
    slot_ids = jnp.arange(row.shape[0], dtype=jnp.int32)
    matches = row_owner[None, :] == sources[:, None]
    present = jnp.any(matches, axis=1)
    slot_of = jnp.sum(jnp.where(matches, slot_ids[None, :], 0), axis=1)
    nvalid = jnp.where(present, jnp.clip(length - slot_of * page_size, 0, page_size), 0)
    within = jnp.arange(page_size, dtype=jnp.int32)
    usable = within[None, :] < nvalid[:, None]
    return jnp.where(usable, 0.0, NEG_FILL).astype(jnp.float32).reshape(1, source_count * page_size)


def on_device(new_queries, new_keys, new_values, kv_pages, page_table, cache_len, w_out, out_bias):
    half = lax.axis_index("half")
    sub = lax.axis_index("sub")
    sub_count = lax.axis_size("sub")
    tp_index = lax.axis_index("tp")
    tp_count = lax.axis_size("tp")
    own_index = half * sub_count + sub
    partner = (1 - half) * sub_count + sub
    span_len = new_queries.shape[0]
    width = new_queries.shape[1]
    head_count = width // HEAD_DIM
    page_count = kv_pages.shape[0]
    page_size = kv_pages.shape[2]
    out_cols = w_out.shape[1] // tp_count
    swap = [(0, 1), (1, 0)]

    w_recv = []
    for shift in range(1, tp_count):
        target = (tp_index + shift) % tp_count
        piece = lax.dynamic_slice_in_dim(w_out, target * out_cols, out_cols, axis=1)
        perm = [(i, (i + shift) % tp_count) for i in range(tp_count)]
        w_recv.append(lax.ppermute(piece, "tp", perm))
    w_mine = lax.dynamic_slice_in_dim(w_out, tp_index * out_cols, out_cols, axis=1)

    owners = jnp.where(page_table >= 0, page_table // page_count, -1)
    held_here = owners == own_index
    local_page = jnp.sum(jnp.where(held_here, page_table - own_index * page_count, 0), axis=1)
    dest = jnp.arange(sub_count, dtype=jnp.int32)
    own_length = lax.dynamic_index_in_dim(cache_len, own_index, 0, keepdims=False)
    partner_length = lax.dynamic_index_in_dim(cache_len, partner, 0, keepdims=False)
    positions = own_length + jnp.arange(span_len, dtype=jnp.int32)
    query_rot = rotate_rows(new_queries, positions)
    partner_query = lax.ppermute(query_rot, "half", swap)

    far_pages = jnp.take(kv_pages, jnp.take(local_page, (1 - half) * sub_count + dest), axis=0, mode="clip")
    far_incoming = lax.all_to_all(far_pages, "sub", split_axis=0, concat_axis=0, tiled=True)
    near_pages = jnp.take(kv_pages, jnp.take(local_page, half * sub_count + dest), axis=0, mode="clip")
    partner_query, near_pages = lax.optimization_barrier((partner_query, near_pages))
    near_incoming = lax.all_to_all(near_pages, "sub", split_axis=0, concat_axis=0, tiled=True)
    key_rot = rotate_rows(new_keys, positions)

    source_base = half * sub_count
    ok_own = usable_keys(page_table, own_index, own_length, source_base, sub_count, page_count, page_size)
    ok_partner = usable_keys(page_table, partner, partner_length, source_base, sub_count, page_count, page_size)

    local_acc, local_stats = local_attend(query_rot, key_rot, new_values)
    far_out, far_stats = far_attend(ok_partner, partner_query, far_incoming)
    back_out = lax.ppermute(far_out, "half", swap)
    back_stats = lax.ppermute(far_stats, "half", swap)
    attended = near_attend(
        ok_own, query_rot, near_incoming, local_acc, local_stats, back_out, back_stats
    )

    parts = [attended]
    for shift in range(1, tp_count):
        perm = [(i, (i + shift) % tp_count) for i in range(tp_count)]
        parts.append(lax.ppermute(attended, "tp", perm))
    return project(parts, [w_mine] + w_recv, out_bias)


def solution(mesh):
    req_count = mesh.shape["req"]
    tp_count = mesh.shape["tp"]
    assert tuple(mesh.axis_names) == ("req", "tp")
    devices = mesh.devices.reshape(2, req_count // 2, tp_count)
    split_mesh = jax.sharding.Mesh(devices, ("half", "sub", "tp"))
    rows = ("half", "sub")
    return jax.shard_map(
        on_device,
        mesh=split_mesh,
        in_specs=(
            P(rows, "tp"),
            P(rows, "tp"),
            P(rows, "tp"),
            P(rows, None, None, "tp"),
            P(),
            P(),
            P("tp", None),
            P("tp"),
        ),
        out_specs=P(rows, "tp"),
        check_vma=False,
    )
```

```python
import math
from functools import partial

import jax
import jax.numpy as jnp
from jax import lax
from jax.experimental import pallas as pl
from jax.experimental.pallas import tpu as pltpu
from jax.sharding import PartitionSpec as P

HEAD_DIM = 128
ROT = 32


NEG_FILL = -1e30


def rotate_rows(block, positions):
    row_count = block.shape[0]
    shaped = block.astype(jnp.float32).reshape(row_count, -1, HEAD_DIM)
    half_rot = ROT // 2
    frequency = 10000.0 ** (-2.0 * jnp.arange(half_rot, dtype=jnp.float32) / ROT)
    angles = positions.astype(jnp.float32)[:, None] * frequency[None, :]
    cosine = jnp.cos(angles)[:, None, :]
    sines = jnp.sin(angles)[:, None, :]
    first_half = shaped[:, :, :half_rot]
    second_half = shaped[:, :, half_rot:ROT]
    turned = jnp.concatenate(
        [
            first_half * cosine - second_half * sines,
            second_half * cosine + first_half * sines,
            shaped[:, :, ROT:],
        ],
        axis=2,
    )
    return turned.reshape(row_count, -1).astype(jnp.bfloat16)


SCORE_DIMS = (((1,), (1,)), ((), ()))


def head_cols(ref, g):
    return ref[..., g * HEAD_DIM:(g + 1) * HEAD_DIM]


def local_kernel(q_ref, kl_ref, vl_ref, acc_ref, st_ref):
    score_scale = 1.0 / math.sqrt(HEAD_DIM)
    span = q_ref.shape[0]
    lane = lax.broadcasted_iota(jnp.int32, (span, HEAD_DIM), 1)
    packed = jnp.zeros((span, HEAD_DIM), jnp.float32)
    for g in range(st_ref.shape[0] // 2):
        q = head_cols(q_ref, g)
        s = lax.dot_general(q, head_cols(kl_ref, g), SCORE_DIMS, preferred_element_type=jnp.float32) * score_scale
        row = lax.broadcasted_iota(jnp.int32, (span, span), 0)
        col = lax.broadcasted_iota(jnp.int32, (span, span), 1)
        s = jnp.where(row >= col, s, NEG_FILL)
        m = jnp.max(s, axis=1, keepdims=True)
        p = jnp.exp(s - m)
        acc_ref[:, g * HEAD_DIM:(g + 1) * HEAD_DIM] = jnp.dot(
            p.astype(jnp.bfloat16), head_cols(vl_ref, g), preferred_element_type=jnp.float32
        )
        packed = jnp.where(lane == 2 * g, m, jnp.where(lane == 2 * g + 1, jnp.sum(p, axis=1, keepdims=True), packed))
    st_ref[...] = packed.T[: st_ref.shape[0]]


def head_pages(kp_ref, vp_ref, g):
    block_count, page_size, _ = kp_ref.shape
    keys = head_cols(kp_ref, g).reshape(block_count * page_size, HEAD_DIM)
    values = head_cols(vp_ref, g).reshape(block_count * page_size, HEAD_DIM)
    return keys, values


def page_partial(q, keys_p, values_p, ok):
    score_scale = 1.0 / math.sqrt(HEAD_DIM)
    s = lax.dot_general(q, keys_p, SCORE_DIMS, preferred_element_type=jnp.float32) * score_scale + ok
    m = jnp.max(s, axis=1, keepdims=True)
    p = jnp.exp(s - m)
    l = jnp.sum(p, axis=1, keepdims=True)
    acc = jnp.dot(p.astype(jnp.bfloat16), values_p, preferred_element_type=jnp.float32)
    return m, l, acc


def far_kernel(q_ref, kp_ref, vp_ref, ok_ref, o_ref, st_ref):
    ok = ok_ref[...]
    span = q_ref.shape[0]
    lane = lax.broadcasted_iota(jnp.int32, (span, HEAD_DIM), 1)
    packed = jnp.zeros((span, HEAD_DIM), jnp.float32)
    for g in range(st_ref.shape[0] // 2):
        keys, values = head_pages(kp_ref, vp_ref, g)
        m, l, acc = page_partial(head_cols(q_ref, g), keys, values, ok)
        o_ref[:, g * HEAD_DIM:(g + 1) * HEAD_DIM] = (acc / l).astype(o_ref.dtype)
        packed = jnp.where(lane == 2 * g, m, jnp.where(lane == 2 * g + 1, l, packed))
    st_ref[...] = packed.T[: st_ref.shape[0]]


def near_kernel(q_ref, kp_ref, vp_ref, ok_ref, la_ref, lst_ref, bo_ref, bst_ref, o_ref):
    ok = ok_ref[...]
    rows, span = bst_ref.shape
    back = jnp.concatenate([bst_ref[...], jnp.zeros((HEAD_DIM - rows, span), jnp.float32)], axis=0).T
    local = jnp.concatenate([lst_ref[...], jnp.zeros((HEAD_DIM - rows, span), jnp.float32)], axis=0).T
    for g in range(rows // 2):
        keys, values = head_pages(kp_ref, vp_ref, g)
        m, l, acc = page_partial(head_cols(q_ref, g), keys, values, ok)
        local_max = local[:, 2 * g:2 * g + 1]
        local_sum = local[:, 2 * g + 1:2 * g + 2]
        back_max = back[:, 2 * g:2 * g + 1]
        back_sum = back[:, 2 * g + 1:2 * g + 2]
        peak = jnp.maximum(jnp.maximum(m, local_max), back_max)
        page_w = jnp.exp(m - peak)
        local_w = jnp.exp(local_max - peak)
        back_w = jnp.exp(back_max - peak) * back_sum
        merged = (
            acc * page_w
            + head_cols(la_ref, g) * local_w
            + head_cols(bo_ref, g).astype(jnp.float32) * back_w
        )
        total = l * page_w + local_sum * local_w + back_w
        o_ref[:, g * HEAD_DIM:(g + 1) * HEAD_DIM] = (merged / total).astype(o_ref.dtype)


def heads_per_step(head_count):
    for group in (4, 2):
        if head_count % group == 0:
            return group
    return 1


def head_specs(span, block_count, page_size, group):
    cols = group * HEAD_DIM
    col_spec = pl.BlockSpec((span, cols), lambda h: (0, h))
    stat_spec = pl.BlockSpec((group, span, 2), lambda h: (h, 0, 0))
    page_specs = [
        pl.BlockSpec((block_count, None, page_size, cols), lambda h: (0, 0, 0, h)),
        pl.BlockSpec((block_count, None, page_size, cols), lambda h: (0, 1, 0, h)),
        pl.BlockSpec((1, block_count * page_size), lambda h: (0, 0)),
    ]
    return col_spec, stat_spec, page_specs


def local_attend(query_rot, key_rot, values):
    span, width = query_rot.shape
    head_count = width // HEAD_DIM
    group = heads_per_step(head_count)
    col_spec, stat_spec, _ = head_specs(span, 1, 1, group)
    return pl.pallas_call(
        local_kernel,
        grid=(head_count // group,),
        in_specs=[col_spec, col_spec, col_spec],
        out_specs=[col_spec, pl.BlockSpec((2 * group, span), lambda h: (h, 0))],
        out_shape=[
            jax.ShapeDtypeStruct((span, width), jnp.float32),
            jax.ShapeDtypeStruct((2 * head_count, span), jnp.float32),
        ],
    )(query_rot, key_rot, values)


def far_attend(key_ok, query_rot, incoming):
    span, width = query_rot.shape
    head_count = width // HEAD_DIM
    group = heads_per_step(head_count)
    col_spec, stat_spec, page_specs = head_specs(span, incoming.shape[0], incoming.shape[2], group)
    return pl.pallas_call(
        far_kernel,
        grid=(head_count // group,),
        in_specs=[col_spec] + page_specs,
        out_specs=[col_spec, pl.BlockSpec((2 * group, span), lambda h: (h, 0))],
        out_shape=[
            jax.ShapeDtypeStruct((span, width), jnp.bfloat16),
            jax.ShapeDtypeStruct((2 * head_count, span), jnp.float32),
        ],
    )(query_rot, incoming, incoming, key_ok)


def near_attend(key_ok, query_rot, incoming, local_acc, local_stats, back_out, back_stats):
    span, width = query_rot.shape
    head_count = width // HEAD_DIM
    group = heads_per_step(head_count)
    col_spec, stat_spec, page_specs = head_specs(span, incoming.shape[0], incoming.shape[2], group)
    row_stats = pl.BlockSpec((2 * group, span), lambda h: (h, 0))
    return pl.pallas_call(
        near_kernel,
        grid=(head_count // group,),
        in_specs=[col_spec] + page_specs + [
            col_spec, row_stats, col_spec, row_stats
        ],
        out_specs=col_spec,
        out_shape=jax.ShapeDtypeStruct((span, width), jnp.bfloat16),
    )(query_rot, incoming, incoming, key_ok, local_acc, local_stats, back_out, back_stats)


def projection_kernel(*refs):
    count = (len(refs) - 2) // 2
    total = refs[2 * count][...].astype(jnp.float32)
    for j in range(count):
        total = total + jnp.dot(refs[j][...], refs[count + j][...], preferred_element_type=jnp.float32)
    refs[-1][...] = total.astype(refs[-1].dtype)


def project(parts, weights, bias):
    span, rows = parts[0].shape
    out_cols = weights[0].shape[1]
    block = 1024 if out_cols % 1024 == 0 else out_cols
    a_spec = pl.BlockSpec((span, rows), lambda c: (0, 0))
    w_spec = pl.BlockSpec((rows, block), lambda c: (0, c))
    b_spec = pl.BlockSpec((1, block), lambda c: (0, c))
    return pl.pallas_call(
        projection_kernel,
        grid=(out_cols // block,),
        in_specs=[a_spec] * len(parts) + [w_spec] * len(weights) + [b_spec],
        out_specs=pl.BlockSpec((span, block), lambda c: (0, c)),
        out_shape=jax.ShapeDtypeStruct((span, out_cols), jnp.bfloat16),
    )(*parts, *weights, bias.reshape(1, out_cols))


def usable_keys(page_table, request, length, source_base, source_count, page_count, page_size):
    row = lax.dynamic_index_in_dim(page_table, request, 0, keepdims=False)
    row_owner = jnp.where(row >= 0, row // page_count, -1)
    sources = source_base + jnp.arange(source_count, dtype=jnp.int32)
    slot_ids = jnp.arange(row.shape[0], dtype=jnp.int32)
    matches = row_owner[None, :] == sources[:, None]
    present = jnp.any(matches, axis=1)
    slot_of = jnp.sum(jnp.where(matches, slot_ids[None, :], 0), axis=1)
    nvalid = jnp.where(present, jnp.clip(length - slot_of * page_size, 0, page_size), 0)
    within = jnp.arange(page_size, dtype=jnp.int32)
    usable = within[None, :] < nvalid[:, None]
    return jnp.where(usable, 0.0, NEG_FILL).astype(jnp.float32).reshape(1, source_count * page_size)


def on_device(new_queries, new_keys, new_values, kv_pages, page_table, cache_len, w_out, out_bias):
    half = lax.axis_index("half")
    sub = lax.axis_index("sub")
    sub_count = lax.axis_size("sub")
    tp_index = lax.axis_index("tp")
    tp_count = lax.axis_size("tp")
    own_index = half * sub_count + sub
    partner = (1 - half) * sub_count + sub
    span_len = new_queries.shape[0]
    width = new_queries.shape[1]
    head_count = width // HEAD_DIM
    page_count = kv_pages.shape[0]
    page_size = kv_pages.shape[2]
    out_cols = w_out.shape[1] // tp_count
    swap = [(0, 1), (1, 0)]

    w_recv = []
    for shift in range(1, tp_count):
        target = (tp_index + shift) % tp_count
        piece = lax.dynamic_slice_in_dim(w_out, target * out_cols, out_cols, axis=1)
        perm = [(i, (i + shift) % tp_count) for i in range(tp_count)]
        w_recv.append(lax.ppermute(piece, "tp", perm))
    w_mine = lax.dynamic_slice_in_dim(w_out, tp_index * out_cols, out_cols, axis=1)

    owners = jnp.where(page_table >= 0, page_table // page_count, -1)
    held_here = owners == own_index
    local_page = jnp.sum(jnp.where(held_here, page_table - own_index * page_count, 0), axis=1)
    dest = jnp.arange(sub_count, dtype=jnp.int32)
    own_length = lax.dynamic_index_in_dim(cache_len, own_index, 0, keepdims=False)
    partner_length = lax.dynamic_index_in_dim(cache_len, partner, 0, keepdims=False)
    positions = own_length + jnp.arange(span_len, dtype=jnp.int32)
    query_rot = rotate_rows(new_queries, positions)
    partner_query = lax.ppermute(query_rot, "half", swap)

    far_pages = jnp.take(kv_pages, jnp.take(local_page, (1 - half) * sub_count + dest), axis=0, mode="clip")
    far_incoming = lax.all_to_all(far_pages, "sub", split_axis=0, concat_axis=0, tiled=True)
    near_pages = jnp.take(kv_pages, jnp.take(local_page, half * sub_count + dest), axis=0, mode="clip")
    partner_query, near_pages = lax.optimization_barrier((partner_query, near_pages))
    near_incoming = lax.all_to_all(near_pages, "sub", split_axis=0, concat_axis=0, tiled=True)
    key_rot = rotate_rows(new_keys, positions)

    source_base = half * sub_count
    ok_own = usable_keys(page_table, own_index, own_length, source_base, sub_count, page_count, page_size)
    ok_partner = usable_keys(page_table, partner, partner_length, source_base, sub_count, page_count, page_size)

    local_acc, local_stats = local_attend(query_rot, key_rot, new_values)
    far_out, far_stats = far_attend(ok_partner, partner_query, far_incoming)
    back_out = lax.ppermute(far_out, "half", swap)
    back_stats = lax.ppermute(far_stats, "half", swap)
    attended = near_attend(
        ok_own, query_rot, near_incoming, local_acc, local_stats, back_out, back_stats
    )

    parts = [attended]
    for shift in range(1, tp_count):
        perm = [(i, (i + shift) % tp_count) for i in range(tp_count)]
        parts.append(lax.ppermute(attended, "tp", perm))
    return project(parts, [w_mine] + w_recv, out_bias)


def solution(mesh):
    req_count = mesh.shape["req"]
    tp_count = mesh.shape["tp"]
    assert tuple(mesh.axis_names) == ("req", "tp")
    devices = mesh.devices.reshape(2, req_count // 2, tp_count)
    split_mesh = jax.sharding.Mesh(devices, ("half", "sub", "tp"))
    rows = ("half", "sub")
    return jax.shard_map(
        on_device,
        mesh=split_mesh,
        in_specs=(
            P(rows, "tp"),
            P(rows, "tp"),
            P(rows, "tp"),
            P(rows, None, None, "tp"),
            P(),
            P(),
            P("tp", None),
            P("tp"),
        ),
        out_specs=P(rows, "tp"),
        check_vma=False,
    )
```

```python
import math
from functools import partial

import jax
import jax.numpy as jnp
from jax import lax
from jax.experimental import pallas as pl
from jax.experimental.pallas import tpu as pltpu
from jax.sharding import PartitionSpec as P

HEAD_DIM = 128
ROT = 32


NEG_FILL = -1e30


def rotate_rows(block, positions):
    row_count = block.shape[0]
    shaped = block.astype(jnp.float32).reshape(row_count, -1, HEAD_DIM)
    half_rot = ROT // 2
    frequency = 10000.0 ** (-2.0 * jnp.arange(half_rot, dtype=jnp.float32) / ROT)
    angles = positions.astype(jnp.float32)[:, None] * frequency[None, :]
    cosine = jnp.cos(angles)[:, None, :]
    sines = jnp.sin(angles)[:, None, :]
    first_half = shaped[:, :, :half_rot]
    second_half = shaped[:, :, half_rot:ROT]
    turned = jnp.concatenate(
        [
            first_half * cosine - second_half * sines,
            second_half * cosine + first_half * sines,
            shaped[:, :, ROT:],
        ],
        axis=2,
    )
    return turned.reshape(row_count, -1).astype(jnp.bfloat16)


SCORE_DIMS = (((1,), (1,)), ((), ()))


def head_cols(ref, g):
    return ref[..., g * HEAD_DIM:(g + 1) * HEAD_DIM]


def local_kernel(q_ref, kl_ref, vl_ref, acc_ref, st_ref):
    score_scale = 1.0 / math.sqrt(HEAD_DIM)
    span = q_ref.shape[0]
    lane = lax.broadcasted_iota(jnp.int32, (span, HEAD_DIM), 1)
    packed = jnp.zeros((span, HEAD_DIM), jnp.float32)
    for g in range(st_ref.shape[0] // 2):
        q = head_cols(q_ref, g)
        s = lax.dot_general(q, head_cols(kl_ref, g), SCORE_DIMS, preferred_element_type=jnp.float32) * score_scale
        row = lax.broadcasted_iota(jnp.int32, (span, span), 0)
        col = lax.broadcasted_iota(jnp.int32, (span, span), 1)
        s = jnp.where(row >= col, s, NEG_FILL)
        m = jnp.max(s, axis=1, keepdims=True)
        p = jnp.exp(s - m)
        acc_ref[:, g * HEAD_DIM:(g + 1) * HEAD_DIM] = jnp.dot(
            p.astype(jnp.bfloat16), head_cols(vl_ref, g), preferred_element_type=jnp.float32
        )
        packed = jnp.where(lane == 2 * g, m, jnp.where(lane == 2 * g + 1, jnp.sum(p, axis=1, keepdims=True), packed))
    st_ref[...] = packed.T[: st_ref.shape[0]]


def head_pages(kp_ref, vp_ref, g):
    block_count, page_size, _ = kp_ref.shape
    keys = head_cols(kp_ref, g).reshape(block_count * page_size, HEAD_DIM)
    values = head_cols(vp_ref, g).reshape(block_count * page_size, HEAD_DIM)
    return keys, values


def page_partial(q, keys_p, values_p, ok):
    score_scale = 1.0 / math.sqrt(HEAD_DIM)
    s = lax.dot_general(q, keys_p, SCORE_DIMS, preferred_element_type=jnp.float32) * score_scale + ok
    m = jnp.max(s, axis=1, keepdims=True)
    p = jnp.exp(s - m)
    l = jnp.sum(p, axis=1, keepdims=True)
    acc = jnp.dot(p.astype(jnp.bfloat16), values_p, preferred_element_type=jnp.float32)
    return m, l, acc


def far_kernel(q_ref, kp_ref, vp_ref, ok_ref, o_ref, st_ref):
    ok = ok_ref[...]
    span = q_ref.shape[0]
    lane = lax.broadcasted_iota(jnp.int32, (span, HEAD_DIM), 1)
    packed = jnp.zeros((span, HEAD_DIM), jnp.float32)
    for g in range(st_ref.shape[0] // 2):
        keys, values = head_pages(kp_ref, vp_ref, g)
        m, l, acc = page_partial(head_cols(q_ref, g), keys, values, ok)
        o_ref[:, g * HEAD_DIM:(g + 1) * HEAD_DIM] = (acc / l).astype(o_ref.dtype)
        packed = jnp.where(lane == 2 * g, m, jnp.where(lane == 2 * g + 1, l, packed))
    st_ref[...] = packed.T[: st_ref.shape[0]]


def near_kernel(q_ref, kp_ref, vp_ref, ok_ref, la_ref, lst_ref, bo_ref, bst_ref, o_ref):
    ok = ok_ref[...]
    rows, span = bst_ref.shape
    back = jnp.concatenate([bst_ref[...], jnp.zeros((HEAD_DIM - rows, span), jnp.float32)], axis=0).T
    local = jnp.concatenate([lst_ref[...], jnp.zeros((HEAD_DIM - rows, span), jnp.float32)], axis=0).T
    for g in range(rows // 2):
        keys, values = head_pages(kp_ref, vp_ref, g)
        m, l, acc = page_partial(head_cols(q_ref, g), keys, values, ok)
        local_max = local[:, 2 * g:2 * g + 1]
        local_sum = local[:, 2 * g + 1:2 * g + 2]
        back_max = back[:, 2 * g:2 * g + 1]
        back_sum = back[:, 2 * g + 1:2 * g + 2]
        peak = jnp.maximum(jnp.maximum(m, local_max), back_max)
        page_w = jnp.exp(m - peak)
        local_w = jnp.exp(local_max - peak)
        back_w = jnp.exp(back_max - peak) * back_sum
        merged = (
            acc * page_w
            + head_cols(la_ref, g) * local_w
            + head_cols(bo_ref, g).astype(jnp.float32) * back_w
        )
        total = l * page_w + local_sum * local_w + back_w
        o_ref[:, g * HEAD_DIM:(g + 1) * HEAD_DIM] = (merged * (1.0 / total)).astype(o_ref.dtype)


def heads_per_step(head_count):
    for group in (4, 2):
        if head_count % group == 0:
            return group
    return 1


def head_specs(span, block_count, page_size, group):
    cols = group * HEAD_DIM
    col_spec = pl.BlockSpec((span, cols), lambda h: (0, h))
    stat_spec = pl.BlockSpec((group, span, 2), lambda h: (h, 0, 0))
    page_specs = [
        pl.BlockSpec((block_count, None, page_size, cols), lambda h: (0, 0, 0, h)),
        pl.BlockSpec((block_count, None, page_size, cols), lambda h: (0, 1, 0, h)),
        pl.BlockSpec((1, block_count * page_size), lambda h: (0, 0)),
    ]
    return col_spec, stat_spec, page_specs


def local_attend(query_rot, key_rot, values):
    span, width = query_rot.shape
    head_count = width // HEAD_DIM
    group = heads_per_step(head_count)
    col_spec, stat_spec, _ = head_specs(span, 1, 1, group)
    return pl.pallas_call(
        local_kernel,
        grid=(head_count // group,),
        in_specs=[col_spec, col_spec, col_spec],
        out_specs=[col_spec, pl.BlockSpec((2 * group, span), lambda h: (h, 0))],
        out_shape=[
            jax.ShapeDtypeStruct((span, width), jnp.float32),
            jax.ShapeDtypeStruct((2 * head_count, span), jnp.float32),
        ],
    )(query_rot, key_rot, values)


def far_attend(key_ok, query_rot, incoming):
    span, width = query_rot.shape
    head_count = width // HEAD_DIM
    group = heads_per_step(head_count)
    col_spec, stat_spec, page_specs = head_specs(span, incoming.shape[0], incoming.shape[2], group)
    return pl.pallas_call(
        far_kernel,
        grid=(head_count // group,),
        in_specs=[col_spec] + page_specs,
        out_specs=[col_spec, pl.BlockSpec((2 * group, span), lambda h: (h, 0))],
        out_shape=[
            jax.ShapeDtypeStruct((span, width), jnp.bfloat16),
            jax.ShapeDtypeStruct((2 * head_count, span), jnp.float32),
        ],
    )(query_rot, incoming, incoming, key_ok)


def near_attend(key_ok, query_rot, incoming, local_acc, local_stats, back_out, back_stats):
    span, width = query_rot.shape
    head_count = width // HEAD_DIM
    group = heads_per_step(head_count)
    col_spec, stat_spec, page_specs = head_specs(span, incoming.shape[0], incoming.shape[2], group)
    row_stats = pl.BlockSpec((2 * group, span), lambda h: (h, 0))
    return pl.pallas_call(
        near_kernel,
        grid=(head_count // group,),
        in_specs=[col_spec] + page_specs + [
            col_spec, row_stats, col_spec, row_stats
        ],
        out_specs=col_spec,
        out_shape=jax.ShapeDtypeStruct((span, width), jnp.bfloat16),
    )(query_rot, incoming, incoming, key_ok, local_acc, local_stats, back_out, back_stats)


def projection_kernel(*refs):
    count = (len(refs) - 2) // 2
    total = refs[2 * count][...].astype(jnp.float32)
    for j in range(count):
        total = total + jnp.dot(refs[j][...], refs[count + j][...], preferred_element_type=jnp.float32)
    refs[-1][...] = total.astype(refs[-1].dtype)


def project(parts, weights, bias):
    span, rows = parts[0].shape
    out_cols = weights[0].shape[1]
    block = 1024 if out_cols % 1024 == 0 else out_cols
    a_spec = pl.BlockSpec((span, rows), lambda c: (0, 0))
    w_spec = pl.BlockSpec((rows, block), lambda c: (0, c))
    b_spec = pl.BlockSpec((1, block), lambda c: (0, c))
    return pl.pallas_call(
        projection_kernel,
        grid=(out_cols // block,),
        in_specs=[a_spec] * len(parts) + [w_spec] * len(weights) + [b_spec],
        out_specs=pl.BlockSpec((span, block), lambda c: (0, c)),
        out_shape=jax.ShapeDtypeStruct((span, out_cols), jnp.bfloat16),
    )(*parts, *weights, bias.reshape(1, out_cols))


def usable_keys(page_table, request, length, source_base, source_count, page_count, page_size):
    row = lax.dynamic_index_in_dim(page_table, request, 0, keepdims=False)
    row_owner = jnp.where(row >= 0, row // page_count, -1)
    sources = source_base + jnp.arange(source_count, dtype=jnp.int32)
    slot_ids = jnp.arange(row.shape[0], dtype=jnp.int32)
    matches = row_owner[None, :] == sources[:, None]
    present = jnp.any(matches, axis=1)
    slot_of = jnp.sum(jnp.where(matches, slot_ids[None, :], 0), axis=1)
    nvalid = jnp.where(present, jnp.clip(length - slot_of * page_size, 0, page_size), 0)
    within = jnp.arange(page_size, dtype=jnp.int32)
    usable = within[None, :] < nvalid[:, None]
    return jnp.where(usable, 0.0, NEG_FILL).astype(jnp.float32).reshape(1, source_count * page_size)


def on_device(new_queries, new_keys, new_values, kv_pages, page_table, cache_len, w_out, out_bias):
    half = lax.axis_index("half")
    sub = lax.axis_index("sub")
    sub_count = lax.axis_size("sub")
    tp_index = lax.axis_index("tp")
    tp_count = lax.axis_size("tp")
    own_index = half * sub_count + sub
    partner = (1 - half) * sub_count + sub
    span_len = new_queries.shape[0]
    width = new_queries.shape[1]
    head_count = width // HEAD_DIM
    page_count = kv_pages.shape[0]
    page_size = kv_pages.shape[2]
    out_cols = w_out.shape[1] // tp_count
    swap = [(0, 1), (1, 0)]

    w_recv = []
    for shift in range(1, tp_count):
        target = (tp_index + shift) % tp_count
        piece = lax.dynamic_slice_in_dim(w_out, target * out_cols, out_cols, axis=1)
        perm = [(i, (i + shift) % tp_count) for i in range(tp_count)]
        w_recv.append(lax.ppermute(piece, "tp", perm))
    w_mine = lax.dynamic_slice_in_dim(w_out, tp_index * out_cols, out_cols, axis=1)

    owners = jnp.where(page_table >= 0, page_table // page_count, -1)
    held_here = owners == own_index
    local_page = jnp.sum(jnp.where(held_here, page_table - own_index * page_count, 0), axis=1)
    dest = jnp.arange(sub_count, dtype=jnp.int32)
    own_length = lax.dynamic_index_in_dim(cache_len, own_index, 0, keepdims=False)
    partner_length = lax.dynamic_index_in_dim(cache_len, partner, 0, keepdims=False)
    positions = own_length + jnp.arange(span_len, dtype=jnp.int32)
    query_rot = rotate_rows(new_queries, positions)
    partner_query = lax.ppermute(query_rot, "half", swap)

    far_pages = jnp.take(kv_pages, jnp.take(local_page, (1 - half) * sub_count + dest), axis=0, mode="clip")
    far_incoming = lax.all_to_all(far_pages, "sub", split_axis=0, concat_axis=0, tiled=True)
    near_pages = jnp.take(kv_pages, jnp.take(local_page, half * sub_count + dest), axis=0, mode="clip")
    partner_query, near_pages = lax.optimization_barrier((partner_query, near_pages))
    near_incoming = lax.all_to_all(near_pages, "sub", split_axis=0, concat_axis=0, tiled=True)
    key_rot = rotate_rows(new_keys, positions)

    source_base = half * sub_count
    ok_own = usable_keys(page_table, own_index, own_length, source_base, sub_count, page_count, page_size)
    ok_partner = usable_keys(page_table, partner, partner_length, source_base, sub_count, page_count, page_size)

    local_acc, local_stats = local_attend(query_rot, key_rot, new_values)
    far_out, far_stats = far_attend(ok_partner, partner_query, far_incoming)
    back_out = lax.ppermute(far_out, "half", swap)
    back_stats = lax.ppermute(far_stats, "half", swap)
    attended = near_attend(
        ok_own, query_rot, near_incoming, local_acc, local_stats, back_out, back_stats
    )

    parts = [attended]
    for shift in range(1, tp_count):
        perm = [(i, (i + shift) % tp_count) for i in range(tp_count)]
        parts.append(lax.ppermute(attended, "tp", perm))
    return project(parts, [w_mine] + w_recv, out_bias)


def solution(mesh):
    req_count = mesh.shape["req"]
    tp_count = mesh.shape["tp"]
    assert tuple(mesh.axis_names) == ("req", "tp")
    devices = mesh.devices.reshape(2, req_count // 2, tp_count)
    split_mesh = jax.sharding.Mesh(devices, ("half", "sub", "tp"))
    rows = ("half", "sub")
    return jax.shard_map(
        on_device,
        mesh=split_mesh,
        in_specs=(
            P(rows, "tp"),
            P(rows, "tp"),
            P(rows, "tp"),
            P(rows, None, None, "tp"),
            P(),
            P(),
            P("tp", None),
            P("tp"),
        ),
        out_specs=P(rows, "tp"),
        check_vma=False,
    )
```
